256 devices in a mesh: section: 2 (over y_hi), grp: 4 (over x), tok: 32 (over y_lo, z, core).
Axes of the slice: x: 4, y: 4 (y_hi: 2, y_lo: 2; y = y_hi * 2 + y_lo), z: 8, core: 2. Of those that a mesh axis runs over, the one named last changes fastest.
Arguments:
- image_in: bfloat16 [2, 4, 128, 3072], P('section', 'grp', 'tok'), may hold values from -1.5 to 1.5
- text_in: bfloat16 [2, 4, 512, 3072], P('section', 'grp', 'tok'), may hold values from -1.5 to 1.5
- text_length: int32 [4], P('grp'), may hold values from 256 to 512, as said below
- entry_order: int32 [4, 4], P('grp'), may hold values from 0 to 3, as said below
- step_index: int32 [4, 4], P('grp'), may hold values from 0 to 3
- image_modulation: bfloat16 [2, 4, 18432], P('section'), may hold values from -3 to 3
- text_modulation: bfloat16 [2, 4, 9216], P('section'), may hold values from -3 to 3
- image_to_heads: bfloat16 [2, 3072, 9216], P('section', None, 'tok'), may hold values from -0.109375 to 0.109375
- text_to_heads: bfloat16 [2, 3072, 9216], P('section', None, 'tok'), may hold values from -0.109375 to 0.109375
- head_gain: float32 [2, 4, 128], P('section'), may hold values from 0.5 to 2
- image_from_heads: bfloat16 [2, 3072, 3072], P('section', None, 'tok'), may hold values from -0.109375 to 0.109375
- text_from_heads: bfloat16 [2, 3072, 3072], P('section', None, 'tok'), may hold values from -0.109375 to 0.109375
- image_up: bfloat16 [2, 3072, 12288], P('section', None, 'tok'), may hold values from -0.109375 to 0.109375
- image_down: bfloat16 [2, 12288, 3072], P('section', 'tok'), may hold values from -0.0546875 to 0.0546875
- stale_cache: bfloat16 [2, 4, 512, 6144], P('section', 'grp', 'tok'), may hold values from -400 to 400
- final_modulation: bfloat16 [4, 6144], replicated, may hold values from -3 to 3
- final_weight: bfloat16 [3072, 64], P(None, 'section'), may hold values from -0.109375 to 0.109375
- latents: float32 [4, 128, 64], P('grp', 'tok', 'section'), may hold values from -6 to 6
Outputs:
- image_handoff: bfloat16 [2, 4, 128, 3072], P('section', 'grp', 'tok')
- text_handoff: bfloat16 [2, 4, 512, 3072], P('section', 'grp', 'tok')
- fresh_cache: bfloat16 [2, 4, 512, 6144], P('section', 'grp', 'tok')
- latents_next: float32 [4, 128, 64], P('grp', 'tok', 'section')
The draws below stay inside these ranges and needn't reach their ends.
Inputs may be any that keep to these rules, and one draw needn't show every extreme that they name: `text_length`: valid text tokens of each request; some request has exactly 512. `entry_order`: each row is a permutation of the 4 patch numbers.
All inputs are finite; a program needn't handle non-finite values.
Results may differ from the reference program's by a relative error of at most 0.023.
The reference program's roundings to bfloat16 on the way (of `attended`, `text_out`, `hidden` and `image_out`) count: a program that leaves them out, or rounds other values in their place, can miss the bound.
Values may be sent and summed in bfloat16 or wider, within the bound.
No kernel may reach another device: no remote copies, remote signals or barrier semaphores. Data moves between devices by JAX's collectives and lax.ppermute only.
A program may use at most 128 MiB of HBM per device.

```python
import jax
import jax.numpy as jnp
from jax import lax

D = 3072
HEADS = 24
HDIM = 128
FF = 12288
CH = 64
IMG = 512
TXT = 512
PATCHES = 4
TSTEPS = 4
LAYERS = 2
REQUESTS = 4
PATCH = 128


def draw_text_length(key, part):
    lengths = jax.random.randint(key, (REQUESTS,), TXT // 2, TXT + 1)
    chosen = jax.random.randint(jax.random.fold_in(key, 1), (), 0, REQUESTS)
    return jnp.where(jnp.arange(REQUESTS) == chosen, TXT, lengths).astype(jnp.int32)


def draw_entry_order(key, part):
    scores = jax.random.randint(jax.random.fold_in(key, 23), (REQUESTS, PATCHES), 0, 1 << 20)
    scores = scores * PATCHES + jnp.arange(PATCHES, dtype=jnp.int32)[None, :]
    return jnp.argsort(scores, axis=1, stable=True).astype(jnp.int32)


def draw_stale_cache(key, part):
    shape = (LAYERS, REQUESTS, IMG, 2 * D)
    values = jax.random.normal(key, shape, jnp.float32)
    values = jnp.clip(values, -400.0, 400.0)
    return values.astype(jnp.bfloat16)


def plant(entries, key, low, largest):
    longest = entries.shape.index(max(entries.shape))
    spots = []
    for shift in (0, 1):
        where = [jax.random.randint(jax.random.fold_in(key, axis), (), 0, length) for axis, length in enumerate(entries.shape)]
        where[longest] = (where[longest] + shift) % entries.shape[longest]
        spots.append(tuple(where))
    return entries.at[spots[0]].set(low).at[spots[1]].set(largest)


def block_scale(rng, extent, cuts, least, high):
    factor_of, own = 1.0, jax.random.fold_in(rng, 6)
    for position, shards_of in cuts:
        steps = jnp.exp(jax.random.uniform(jax.random.fold_in(own, position), (shards_of,), jnp.float32, least / len(cuts), high / len(cuts)))
        factor_of = factor_of * jnp.repeat(steps, extent[position] // shards_of).reshape([-1 if axis == position else 1 for axis in range(len(extent))])
    return factor_of


def scatter_about(rng, shape, scale, bound, shards=(), kind=jnp.bfloat16):
    factor_of = block_scale(rng, shape, shards, -0.22, 0.18) if shards else 1.0
    array = jax.random.normal(rng, shape, jnp.float32) * scale * factor_of
    return jnp.minimum(jnp.maximum(array, -bound), bound).astype(kind)


def setup_inputs(seed: int = 0) -> dict:
    key_of = jax.random.split(jax.random.key(seed), 19)
    image_in = scatter_about(key_of[0], (LAYERS, REQUESTS, PATCH, D), 0.25, 1.5, ((0, 2), (1, 4), (2, 32)))
    text_in = scatter_about(key_of[1], (LAYERS, REQUESTS, TXT, D), 0.25, 1.5, ((0, 2), (1, 4), (2, 32)))
    text_length = draw_text_length(jax.random.fold_in(key_of[18], 71), 0)
    entry_order = draw_entry_order(jax.random.fold_in(key_of[18], 71), 0)
    step_index = plant(jax.random.randint(key_of[4], (REQUESTS, PATCHES), 0, TSTEPS), jax.random.fold_in(key_of[4], 1), 0, TSTEPS - 1).astype(jnp.int32)
    image_modulation = scatter_about(key_of[5], (LAYERS, TSTEPS, 6 * D), 0.5, 3.0, ((0, 2),))
    text_modulation = scatter_about(key_of[6], (LAYERS, TSTEPS, 3 * D), 0.5, 3.0, ((0, 2),))
    image_to_heads = scatter_about(key_of[7], (LAYERS, D, 3 * D), D ** -0.5, 0.109375, ((0, 2), (2, 32)))
    text_to_heads = scatter_about(key_of[8], (LAYERS, D, 3 * D), D ** -0.5, 0.109375, ((0, 2), (2, 32)))
    head_gain = jnp.clip(0.5 + 1.5 * jax.random.uniform(key_of[9], (LAYERS, 4, HDIM), jnp.float32) ** block_scale(key_of[9], (LAYERS, 4, HDIM), ((0, 2),), -0.2, 0.2), 0.5, 2.0)
    image_from_heads = scatter_about(key_of[10], (LAYERS, D, D), D ** -0.5, 0.109375, ((0, 2), (2, 32)))
    text_from_heads = scatter_about(key_of[11], (LAYERS, D, D), D ** -0.5, 0.109375, ((0, 2), (2, 32)))
    image_up = scatter_about(key_of[12], (LAYERS, D, FF), D ** -0.5, 0.109375, ((0, 2), (2, 32)))
    image_down = scatter_about(key_of[13], (LAYERS, FF, D), FF ** -0.5, 0.0546875, ((0, 2), (1, 32)))
    stale_cache = draw_stale_cache(jax.random.fold_in(key_of[18], 71), 0)
    final_modulation = scatter_about(key_of[15], (TSTEPS, 2 * D), 0.5, 3.0)
    final_weight = scatter_about(key_of[16], (D, CH), D ** -0.5, 0.109375, ((1, 2),))
    latents = scatter_about(key_of[17], (REQUESTS, PATCH, CH), 1.0, 6.0, ((0, 4), (1, 32), (2, 2)), jnp.float32)
    return {"image_in": image_in, "text_in": text_in, "text_length": text_length, "entry_order": entry_order, "step_index": step_index, "image_modulation": image_modulation, "text_modulation": text_modulation, "image_to_heads": image_to_heads, "text_to_heads": text_to_heads, "head_gain": head_gain, "image_from_heads": image_from_heads, "text_from_heads": text_from_heads, "image_up": image_up, "image_down": image_down, "stale_cache": stale_cache, "final_modulation": final_modulation, "final_weight": final_weight, "latents": latents}


eps = 1e-06

def stored(field):
    return lax.optimization_barrier(field.astype(jnp.bfloat16))

def layer_norm(field):
    mean = lax.optimization_barrier(jnp.mean(field, axis=-1, keepdims=True))
    centred = field - mean
    spread = lax.optimization_barrier(jnp.mean(centred * centred, axis=-1, keepdims=True))
    return centred * lax.rsqrt(spread + eps)

def modulate(field, shift, scale):
    return layer_norm(field) * (1.0 + scale) + shift

def head_norm(field, gain):
    height = field.shape[0]
    shaped = field.reshape(height, HEADS, HDIM)
    power = lax.optimization_barrier(jnp.mean(shaped * shaped, axis=-1, keepdims=True))
    return (shaped * lax.rsqrt(power + eps) * gain).reshape(height, HEADS * HDIM)

def attention(queries, keys, values, valid):
    height = queries.shape[0]
    query_f = queries.astype(jnp.float32).reshape(height, HEADS, HDIM)
    key_f = keys.astype(jnp.float32).reshape(keys.shape[0], HEADS, HDIM)
    value_f = values.astype(jnp.float32).reshape(values.shape[0], HEADS, HDIM)
    scores = jnp.einsum('qhd,khd->qhk', query_f, key_f) * HDIM ** (-0.5)
    scores = jnp.where(valid[None, None, :], scores, -1e+30)
    highest = lax.optimization_barrier(jnp.max(scores, axis=-1, keepdims=True))
    expo = jnp.where(valid[None, None, :], jnp.exp(scores - highest), 0.0)
    total = lax.optimization_barrier(jnp.sum(expo, axis=-1))
    weights = stored(expo).astype(jnp.float32)
    mixed = jnp.einsum('qhk,khd->qhd', weights, value_f) / total[..., None]
    return mixed.reshape(height, HEADS * HDIM).astype(jnp.bfloat16)

def reference(image_in, text_in, text_length, entry_order, step_index, image_modulation, text_modulation, image_to_heads, text_to_heads, head_gain, image_from_heads, text_from_heads, image_up, image_down, stale_cache, final_modulation, final_weight, latents):
    image_layers = []
    text_layers = []
    cache_layers = []
    for layer in range(LAYERS):
        image_reqs = []
        text_reqs = []
        cache_reqs = []
        for request in range(REQUESTS):
            patch = entry_order[request, layer]
            step_now = step_index[request, patch]
            modul = lax.dynamic_index_in_dim(image_modulation[layer], step_now, 0, False).astype(jnp.float32).reshape(6, D)
            text_mod = lax.dynamic_index_in_dim(text_modulation[layer], step_now, 0, False).astype(jnp.float32).reshape(3, D)
            image_x = image_in[layer, request].astype(jnp.float32)
            text_x = text_in[layer, request].astype(jnp.float32)
            image_normed = modulate(image_x, modul[0], modul[1]).astype(jnp.bfloat16)
            text_normed = modulate(text_x, text_mod[0], text_mod[1]).astype(jnp.bfloat16)
            image_proj = stored(jnp.dot(image_normed, image_to_heads[layer], preferred_element_type=jnp.float32))
            text_proj = stored(jnp.dot(text_normed, text_to_heads[layer], preferred_element_type=jnp.float32))
            gains = head_gain[layer]
            image_query = head_norm(image_proj[:, :D].astype(jnp.float32), gains[0]).astype(jnp.bfloat16)
            image_key = head_norm(image_proj[:, D:2 * D].astype(jnp.float32), gains[1]).astype(jnp.bfloat16)
            text_query = head_norm(text_proj[:, :D].astype(jnp.float32), gains[2]).astype(jnp.bfloat16)
            text_key = head_norm(text_proj[:, D:2 * D].astype(jnp.float32), gains[3]).astype(jnp.bfloat16)
            fresh = jnp.concatenate([image_key, image_proj[:, 2 * D:]], axis=1)
            begin = (patch * PATCH).astype(jnp.int32)
            cache = lax.dynamic_update_slice(stale_cache[layer, request], fresh, (begin, jnp.zeros((), jnp.int32)))
            keys = jnp.concatenate([text_key, cache[:, :D]], axis=0)
            values = jnp.concatenate([text_proj[:, 2 * D:], cache[:, D:]], axis=0)
            valid = jnp.concatenate([jnp.arange(TXT, dtype=jnp.int32) < text_length[request], jnp.ones((IMG,), bool)])
            queries = jnp.concatenate([image_query, text_query], axis=0)
            attended = attention(queries, keys, values, valid)
            image_back = stored(jnp.dot(attended[:PATCH], image_from_heads[layer], preferred_element_type=jnp.float32))
            text_back = stored(jnp.dot(attended[PATCH:], text_from_heads[layer], preferred_element_type=jnp.float32))
            image_mid = image_x + modul[2] * image_back.astype(jnp.float32)
            text_out = (text_x + text_mod[2] * text_back.astype(jnp.float32)).astype(jnp.bfloat16)
            mlp_normed = modulate(image_mid, modul[3], modul[4]).astype(jnp.bfloat16)
            hidden = jax.nn.gelu(jnp.dot(mlp_normed, image_up[layer], preferred_element_type=jnp.float32), approximate=True).astype(jnp.bfloat16)
            reduced = jnp.dot(hidden, image_down[layer], preferred_element_type=jnp.float32)
            image_out = (image_mid + modul[5] * reduced).astype(jnp.bfloat16)
            image_reqs.append(image_out)
            text_reqs.append(text_out)
            cache_reqs.append(cache)
        image_layers.append(jnp.stack(image_reqs))
        text_layers.append(jnp.stack(text_reqs))
        cache_layers.append(jnp.stack(cache_reqs))
    image_stack = jnp.stack(image_layers)
    text_stack = jnp.stack(text_layers)
    fresh_cache = jnp.stack(cache_layers)
    image_handoff = jnp.roll(image_stack, 1, axis=0)
    text_handoff = jnp.roll(text_stack, 1, axis=0)
    updated = []
    for request in range(REQUESTS):
        patch_last = entry_order[request, LAYERS - 1]
        step_last = step_index[request, patch_last]
        final_mod = lax.dynamic_index_in_dim(final_modulation, step_last, 0, False).astype(jnp.float32).reshape(2, D)
        source = image_stack[LAYERS - 1, request].astype(jnp.float32)
        normed = modulate(source, final_mod[0], final_mod[1]).astype(jnp.bfloat16)
        velocity = jnp.dot(normed, final_weight, preferred_element_type=jnp.float32)
        updated.append(latents[request] + -1.0 / TSTEPS * velocity)
    latents_next = jnp.stack(updated)
    return (image_handoff, text_handoff, fresh_cache, latents_next)
```

```python
import jax
import jax.numpy as jnp
from jax import lax
from jax.sharding import PartitionSpec as P

HDIM = 128
TSTEPS = 4


eps = 1e-06
masked_score = -1e30


def from_behind(block, axis, distance):
    devices = range(lax.axis_size(axis))
    route = [((i - distance) % len(devices), i) for i in devices]
    return lax.ppermute(block, axis, route)


def layer_norm(field):
    mean = jnp.mean(field, axis=-1, keepdims=True)
    centred = field - mean
    spread = jnp.mean(centred * centred, axis=-1, keepdims=True)
    return centred * lax.rsqrt(spread + eps)


def modulate(field, shift, scale):
    return layer_norm(field) * (1.0 + scale) + shift


def head_norm(field, gain):
    height, width = field.shape
    shaped = field.reshape(height, width // HDIM, HDIM)
    power = jnp.mean(shaped * shaped, axis=-1, keepdims=True)
    return (shaped * lax.rsqrt(power + eps) * gain).reshape(height, width)


def attend(queries, keys, values, valid):
    height, width = queries.shape
    heads = width // HDIM
    scores = jnp.einsum(
        "qhd,khd->qhk",
        queries.reshape(height, heads, HDIM),
        keys.reshape(-1, heads, HDIM),
        preferred_element_type=jnp.float32,
    ) * HDIM ** (-0.5)
    scores = jnp.where(valid[None, None, :], scores, masked_score)
    highest = jnp.max(scores, axis=-1, keepdims=True)
    expo = jnp.where(valid[None, None, :], jnp.exp(scores - highest), 0.0)
    total = jnp.sum(expo, axis=-1)
    mixed = jnp.einsum(
        "qhk,khd->qhd",
        expo.astype(jnp.bfloat16),
        values.reshape(-1, heads, HDIM),
        preferred_element_type=jnp.float32,
    )
    return (mixed / total[..., None]).reshape(height, width).astype(jnp.bfloat16)


def cols_to_rows(cols):
    got = lax.all_to_all(cols, "tok", split_axis=0, concat_axis=0, tiled=True)
    count, rows, width = got.shape
    return jnp.transpose(got, (1, 0, 2)).reshape(rows, count * width)


def shards(
    image_in,
    text_in,
    text_length,
    entry_order,
    step_index,
    image_modulation,
    text_modulation,
    image_to_heads,
    text_to_heads,
    head_gain,
    image_from_heads,
    text_from_heads,
    image_up,
    image_down,
    stale_cache,
    final_modulation,
    final_weight,
    latents,
):
    section = lax.axis_index("section")
    last_section = lax.axis_size("section") - 1
    position = lax.axis_index("tok")
    devices = lax.axis_size("tok")
    image_x = image_in[0, 0].astype(jnp.float32)
    text_x = text_in[0, 0].astype(jnp.float32)
    image_rows = image_x.shape[0]
    text_rows = text_x.shape[0]
    width = image_x.shape[1]
    patch = lax.dynamic_index_in_dim(entry_order[0], section, 0, False)
    step_now = lax.dynamic_index_in_dim(step_index[0], patch, 0, False)
    modul = (
        lax.dynamic_index_in_dim(image_modulation[0], step_now, 0, False)
        .astype(jnp.float32)
        .reshape(6, width)
    )
    text_mod = (
        lax.dynamic_index_in_dim(text_modulation[0], step_now, 0, False)
        .astype(jnp.float32)
        .reshape(3, width)
    )
    image_normed = modulate(image_x, modul[0], modul[1]).astype(jnp.bfloat16)
    text_normed = modulate(text_x, text_mod[0], text_mod[1]).astype(jnp.bfloat16)
    every = lax.all_gather(
        jnp.concatenate([image_normed, text_normed], axis=0), "tok", axis=0, tiled=False
    )
    image_cols = jnp.dot(
        every[:, :image_rows].reshape(-1, width), image_to_heads[0], preferred_element_type=jnp.float32
    ).astype(jnp.bfloat16)
    text_cols = jnp.dot(
        every[:, image_rows:].reshape(-1, width), text_to_heads[0], preferred_element_type=jnp.float32
    ).astype(jnp.bfloat16)
    proj = cols_to_rows(
        jnp.concatenate(
            [
                image_cols.reshape(devices, image_rows, -1),
                text_cols.reshape(devices, text_rows, -1),
            ],
            axis=1,
        )
    )
    image_proj = proj[:image_rows]
    text_proj = proj[image_rows:]
    gains = head_gain[0]
    image_query = head_norm(image_proj[:, :width].astype(jnp.float32), gains[0]).astype(
        jnp.bfloat16
    )
    image_key = head_norm(image_proj[:, width : 2 * width].astype(jnp.float32), gains[1]).astype(
        jnp.bfloat16
    )
    text_query = head_norm(text_proj[:, :width].astype(jnp.float32), gains[2]).astype(jnp.bfloat16)
    text_key = head_norm(text_proj[:, width : 2 * width].astype(jnp.float32), gains[3]).astype(
        jnp.bfloat16
    )
    fresh_image = jnp.concatenate([image_key, image_proj[:, 2 * width :]], axis=1)
    fresh_text = jnp.concatenate([text_key, text_proj[:, 2 * width :]], axis=1)
    queries = jnp.concatenate([image_query, text_query], axis=0)
    stale = stale_cache[0, 0]
    cache_rows = stale.shape[0]
    gathered = lax.all_gather(
        jnp.concatenate([stale, fresh_image, fresh_text], axis=0), "tok", axis=0, tiled=False
    )
    stale_all = gathered[:, :cache_rows].reshape(-1, 2 * width)
    patch_all = gathered[:, cache_rows : cache_rows + image_rows].reshape(-1, 2 * width)
    text_all = gathered[:, cache_rows + image_rows :].reshape(-1, 2 * width)
    begin = patch * patch_all.shape[0]
    cache_all = lax.dynamic_update_slice_in_dim(stale_all, patch_all, begin, 0)
    current = lax.dynamic_slice_in_dim(cache_all, position * cache_rows, cache_rows, 0)
    text_count = text_length[0]
    keys_all = jnp.concatenate([cache_all, text_all], axis=0)
    valid = jnp.concatenate(
        [
            jnp.ones((cache_all.shape[0],), bool),
            jnp.arange(text_all.shape[0], dtype=jnp.int32) < text_count,
        ]
    )
    attended = attend(queries, keys_all[:, :width], keys_all[:, width:], valid)
    every_att = lax.all_gather(attended, "tok", axis=0, tiled=False)
    image_back_cols = jnp.dot(
        every_att[:, :image_rows].reshape(-1, width), image_from_heads[0], preferred_element_type=jnp.float32
    ).astype(jnp.bfloat16)
    text_back_cols = jnp.dot(
        every_att[:, image_rows:].reshape(-1, width), text_from_heads[0], preferred_element_type=jnp.float32
    ).astype(jnp.bfloat16)
    back = cols_to_rows(
        jnp.concatenate(
            [
                image_back_cols.reshape(devices, image_rows, -1),
                text_back_cols.reshape(devices, text_rows, -1),
            ],
            axis=1,
        )
    )
    image_back = back[:image_rows]
    text_back = back[image_rows:]
    image_mid = image_x + modul[2] * image_back.astype(jnp.float32)
    text_out = (text_x + text_mod[2] * text_back.astype(jnp.float32)).astype(jnp.bfloat16)
    mlp_normed = modulate(image_mid, modul[3], modul[4]).astype(jnp.bfloat16)
    up_weight = image_up[0]
    down_weight = image_down[0]
    hidden = jax.nn.gelu(
        jnp.dot(
            lax.all_gather(mlp_normed, "tok", axis=0, tiled=True),
            up_weight,
            preferred_element_type=jnp.float32,
        ),
        approximate=True,
    ).astype(jnp.bfloat16)
    partial = jnp.dot(hidden, down_weight, preferred_element_type=jnp.float32)
    reduced = jnp.sum(
        lax.all_to_all(
            partial.reshape(devices, image_rows, width), "tok", split_axis=0, concat_axis=0, tiled=True
        ),
        axis=0,
    )
    image_out = (image_mid + modul[5] * reduced).astype(jnp.bfloat16)
    joined = from_behind(jnp.concatenate([image_out, text_out], axis=0), "section", 1)
    image_next = joined[:image_rows]
    text_next = joined[image_rows:]
    final_source = jnp.where(section == last_section, image_out, image_next)
    patch_last = entry_order[0, last_section]
    step_last = lax.dynamic_index_in_dim(step_index[0], patch_last, 0, False)
    final_mod = (
        lax.dynamic_index_in_dim(final_modulation, step_last, 0, False)
        .astype(jnp.float32)
        .reshape(2, width)
    )
    normed = modulate(final_source.astype(jnp.float32), final_mod[0], final_mod[1]).astype(
        jnp.bfloat16
    )
    velocity = jnp.dot(normed, final_weight, preferred_element_type=jnp.float32)
    latents_next = latents[0] + -1.0 / TSTEPS * velocity
    return (image_next[None, None], text_next[None, None], current[None, None], latents_next[None])


def solution(mesh):
    placed = (
        P("section", "grp", "tok", None),
        P("section", "grp", "tok", None),
        P("grp"),
        P("grp", None),
        P("grp", None),
        P("section", None, None),
        P("section", None, None),
        P("section", None, "tok"),
        P("section", None, "tok"),
        P("section", None, None),
        P("section", None, "tok"),
        P("section", None, "tok"),
        P("section", None, "tok"),
        P("section", "tok", None),
        P("section", "grp", "tok", None),
        P(),
        P(None, "section"),
        P("grp", "tok", "section"),
    )
    return jax.shard_map(
        shards,
        mesh=mesh,
        in_specs=placed,
        out_specs=(
            P("section", "grp", "tok", None),
            P("section", "grp", "tok", None),
            P("section", "grp", "tok", None),
            P("grp", "tok", "section"),
        ),
        check_vma=False,
    )
```

```python
import jax
import jax.numpy as jnp
from jax import lax
from jax.sharding import PartitionSpec as P

HDIM = 128
TSTEPS = 4


TOK = ("ta", "tb")
QUAD = 4

eps = 1e-06
masked_score = -1e30


def from_behind(block, axis, distance):
    devices = range(lax.axis_size(axis))
    route = [((i - distance) % len(devices), i) for i in devices]
    return lax.ppermute(block, axis, route)


def layer_norm(field):
    mean = jnp.mean(field, axis=-1, keepdims=True)
    centred = field - mean
    spread = jnp.mean(centred * centred, axis=-1, keepdims=True)
    return centred * lax.rsqrt(spread + eps)


def modulate(field, shift, scale):
    return layer_norm(field) * (1.0 + scale) + shift


def head_norm(field, gain):
    height, width = field.shape
    shaped = field.reshape(height, width // HDIM, HDIM)
    power = jnp.mean(shaped * shaped, axis=-1, keepdims=True)
    return (shaped * lax.rsqrt(power + eps) * gain).reshape(height, width)


def attend(queries, keys, values, valid):
    height, width = queries.shape
    heads = width // HDIM
    scores = jnp.einsum(
        "qhd,khd->qhk",
        queries.reshape(height, heads, HDIM),
        keys.reshape(-1, heads, HDIM),
        preferred_element_type=jnp.float32,
    ) * HDIM ** (-0.5)
    scores = jnp.where(valid[None, None, :], scores, masked_score)
    highest = jnp.max(scores, axis=-1, keepdims=True)
    expo = jnp.where(valid[None, None, :], jnp.exp(scores - highest), 0.0)
    total = jnp.sum(expo, axis=-1)
    mixed = jnp.einsum(
        "qhk,khd->qhd",
        expo.astype(jnp.bfloat16),
        values.reshape(-1, heads, HDIM),
        preferred_element_type=jnp.float32,
    )
    return (mixed / total[..., None]).reshape(height, width).astype(jnp.bfloat16)


def cols_to_rows(cols):
    got = lax.all_to_all(cols, TOK, split_axis=0, concat_axis=0, tiled=True)
    count, rows, width = got.shape
    return jnp.transpose(got, (1, 0, 2)).reshape(rows, count * width)


def shards(
    image_in,
    text_in,
    text_length,
    entry_order,
    step_index,
    image_modulation,
    text_modulation,
    image_to_heads,
    text_to_heads,
    head_gain,
    image_from_heads,
    text_from_heads,
    image_up,
    image_down,
    stale_cache,
    final_modulation,
    final_weight,
    latents,
):
    section = lax.axis_index("section")
    last_section = lax.axis_size("section") - 1
    position = lax.axis_index("ta") * lax.axis_size("tb") + lax.axis_index("tb")
    devices = lax.axis_size("ta") * lax.axis_size("tb")
    image_x = image_in[0, 0].astype(jnp.float32)
    text_x = text_in[0, 0].astype(jnp.float32)
    image_rows = image_x.shape[0]
    text_rows = text_x.shape[0]
    width = image_x.shape[1]
    patch = lax.dynamic_index_in_dim(entry_order[0], section, 0, False)
    step_now = lax.dynamic_index_in_dim(step_index[0], patch, 0, False)
    modul = (
        lax.dynamic_index_in_dim(image_modulation[0], step_now, 0, False)
        .astype(jnp.float32)
        .reshape(6, width)
    )
    text_mod = (
        lax.dynamic_index_in_dim(text_modulation[0], step_now, 0, False)
        .astype(jnp.float32)
        .reshape(3, width)
    )
    image_normed = modulate(image_x, modul[0], modul[1]).astype(jnp.bfloat16)
    text_normed = modulate(text_x, text_mod[0], text_mod[1]).astype(jnp.bfloat16)
    every = lax.all_gather(
        jnp.concatenate([image_normed, text_normed], axis=0), TOK, axis=0, tiled=False
    )
    image_cols = jnp.dot(
        every[:, :image_rows].reshape(-1, width), image_to_heads[0], preferred_element_type=jnp.float32
    ).astype(jnp.bfloat16)
    text_cols = jnp.dot(
        every[:, image_rows:].reshape(-1, width), text_to_heads[0], preferred_element_type=jnp.float32
    ).astype(jnp.bfloat16)
    proj = cols_to_rows(
        jnp.concatenate(
            [
                image_cols.reshape(devices, image_rows, -1),
                text_cols.reshape(devices, text_rows, -1),
            ],
            axis=1,
        )
    )
    image_proj = proj[:image_rows]
    text_proj = proj[image_rows:]
    gains = head_gain[0]
    image_query = head_norm(image_proj[:, :width].astype(jnp.float32), gains[0]).astype(
        jnp.bfloat16
    )
    image_key = head_norm(image_proj[:, width : 2 * width].astype(jnp.float32), gains[1]).astype(
        jnp.bfloat16
    )
    text_query = head_norm(text_proj[:, :width].astype(jnp.float32), gains[2]).astype(jnp.bfloat16)
    text_key = head_norm(text_proj[:, width : 2 * width].astype(jnp.float32), gains[3]).astype(
        jnp.bfloat16
    )
    image_value = image_proj[:, 2 * width :]
    text_value = text_proj[:, 2 * width :]
    stale = stale_cache[0, 0]
    cache_rows = stale.shape[0]
    heads = width // HDIM
    fresh_image = jnp.concatenate([image_key, image_value], axis=1)
    quad = lax.all_gather(fresh_image, "tb", axis=0, tiled=True)
    group = lax.axis_size("tb")
    blocks = devices // group
    route = [(j * group + b, j + blocks * b) for j in range(blocks) for b in range(group)]
    moved = lax.ppermute(quad, TOK, route)
    patch_len = image_rows * devices
    per_patch = patch_len // cache_rows
    current = jnp.where(position // per_patch == patch, moved, stale)
    row_q = jnp.concatenate([image_query, text_query], axis=0)
    row_k = jnp.concatenate([image_key, text_key], axis=0)
    row_v = jnp.concatenate([image_value, text_value], axis=0)
    pieces = [row_q, row_k, row_v, stale[:, :width], stale[:, width:]]
    pack = jnp.concatenate([piece.reshape(piece.shape[0], heads, HDIM) for piece in pieces], axis=0)
    pack = jnp.transpose(pack, (1, 0, 2))
    pack = jnp.pad(pack, ((0, devices - heads), (0, 0), (0, 0)))
    got = lax.all_to_all(pack, TOK, split_axis=0, concat_axis=0, tiled=True)
    rows = image_rows + text_rows

    def part(first, count):
        return got[:, first : first + count].reshape(-1, HDIM)

    queries = jnp.concatenate([part(0, image_rows), part(image_rows, text_rows)], axis=0)
    fresh_k = part(rows, image_rows)
    text_k = part(rows + image_rows, text_rows)
    fresh_v = part(2 * rows, image_rows)
    text_v = part(2 * rows + image_rows, text_rows)
    cache_k = part(3 * rows, cache_rows)
    cache_v = part(3 * rows + cache_rows, cache_rows)
    begin = patch * patch_len
    cache_k = lax.dynamic_update_slice_in_dim(cache_k, fresh_k, begin, 0)
    cache_v = lax.dynamic_update_slice_in_dim(cache_v, fresh_v, begin, 0)
    keys = jnp.concatenate([cache_k, text_k], axis=0)
    values = jnp.concatenate([cache_v, text_v], axis=0)
    text_count = text_length[0]
    valid = jnp.concatenate(
        [
            jnp.ones((cache_k.shape[0],), bool),
            jnp.arange(text_k.shape[0], dtype=jnp.int32) < text_count,
        ]
    )
    head_out = attend(queries, keys, values, valid)
    every_head = lax.all_gather(head_out, TOK, axis=0, tiled=False)
    every_att = jnp.transpose(every_head[:heads], (1, 0, 2)).reshape(-1, width)
    image_back_cols = jnp.dot(
        every_att[:patch_len], image_from_heads[0], preferred_element_type=jnp.float32
    ).astype(jnp.bfloat16)
    text_back_cols = jnp.dot(
        every_att[patch_len:], text_from_heads[0], preferred_element_type=jnp.float32
    ).astype(jnp.bfloat16)
    back = cols_to_rows(
        jnp.concatenate(
            [
                image_back_cols.reshape(devices, image_rows, -1),
                text_back_cols.reshape(devices, text_rows, -1),
            ],
            axis=1,
        )
    )
    image_back = back[:image_rows]
    text_back = back[image_rows:]
    image_mid = image_x + modul[2] * image_back.astype(jnp.float32)
    text_out = (text_x + text_mod[2] * text_back.astype(jnp.float32)).astype(jnp.bfloat16)
    mlp_normed = modulate(image_mid, modul[3], modul[4]).astype(jnp.bfloat16)
    up_weight = image_up[0]
    down_weight = image_down[0]
    hidden = jax.nn.gelu(
        jnp.dot(
            lax.all_gather(mlp_normed, TOK, axis=0, tiled=True),
            up_weight,
            preferred_element_type=jnp.float32,
        ),
        approximate=True,
    ).astype(jnp.bfloat16)
    partial = jnp.dot(hidden, down_weight, preferred_element_type=jnp.float32)
    reduced = jnp.sum(
        lax.all_to_all(
            partial.reshape(devices, image_rows, width), TOK, split_axis=0, concat_axis=0, tiled=True
        ),
        axis=0,
    )
    image_out = (image_mid + modul[5] * reduced).astype(jnp.bfloat16)
    joined = from_behind(jnp.concatenate([image_out, text_out], axis=0), "section", 1)
    image_next = joined[:image_rows]
    text_next = joined[image_rows:]
    final_source = jnp.where(section == last_section, image_out, image_next)
    patch_last = entry_order[0, last_section]
    step_last = lax.dynamic_index_in_dim(step_index[0], patch_last, 0, False)
    final_mod = (
        lax.dynamic_index_in_dim(final_modulation, step_last, 0, False)
        .astype(jnp.float32)
        .reshape(2, width)
    )
    normed = modulate(final_source.astype(jnp.float32), final_mod[0], final_mod[1]).astype(
        jnp.bfloat16
    )
    velocity = jnp.dot(normed, final_weight, preferred_element_type=jnp.float32)
    latents_next = latents[0] + -1.0 / TSTEPS * velocity
    return (image_next[None, None], text_next[None, None], current[None, None], latents_next[None])


def solution(mesh):
    shape = mesh.devices.shape
    split = jax.sharding.Mesh(
        mesh.devices.reshape(shape[:2] + (shape[2] // QUAD, QUAD)),
        ("section", "grp", "ta", "tb"),
    )
    placed = (
        P("section", "grp", TOK, None),
        P("section", "grp", TOK, None),
        P("grp"),
        P("grp", None),
        P("grp", None),
        P("section", None, None),
        P("section", None, None),
        P("section", None, TOK),
        P("section", None, TOK),
        P("section", None, None),
        P("section", None, TOK),
        P("section", None, TOK),
        P("section", None, TOK),
        P("section", TOK, None),
        P("section", "grp", TOK, None),
        P(),
        P(None, "section"),
        P("grp", TOK, "section"),
    )
    return jax.shard_map(
        shards,
        mesh=split,
        in_specs=placed,
        out_specs=(
            P("section", "grp", TOK, None),
            P("section", "grp", TOK, None),
            P("section", "grp", TOK, None),
            P("grp", TOK, "section"),
        ),
        check_vma=False,
    )
```

```python
import jax
import jax.numpy as jnp
from jax import lax
from jax.sharding import PartitionSpec as P

HDIM = 128
TSTEPS = 4


TOK = ("ta", "tb")
QUAD = 4

eps = 1e-06
masked_score = -1e30


def from_behind(block, axis, distance):
    devices = range(lax.axis_size(axis))
    route = [((i - distance) % len(devices), i) for i in devices]
    return lax.ppermute(block, axis, route)


def layer_norm(field):
    mean = jnp.mean(field, axis=-1, keepdims=True)
    centred = field - mean
    spread = jnp.mean(centred * centred, axis=-1, keepdims=True)
    return centred * lax.rsqrt(spread + eps)


def modulate(field, shift, scale):
    return layer_norm(field) * (1.0 + scale) + shift


def head_norm(field, gain):
    height, width = field.shape
    shaped = field.reshape(height, width // HDIM, HDIM)
    power = jnp.mean(shaped * shaped, axis=-1, keepdims=True)
    return (shaped * lax.rsqrt(power + eps) * gain).reshape(height, width)


def attend(queries, keys, values, valid):
    height, width = queries.shape
    heads = width // HDIM
    scores = jnp.einsum(
        "qhd,khd->qhk",
        queries.reshape(height, heads, HDIM),
        keys.reshape(-1, heads, HDIM),
        preferred_element_type=jnp.float32,
    ) * HDIM ** (-0.5)
    scores = jnp.where(valid[None, None, :], scores, masked_score)
    highest = jnp.max(scores, axis=-1, keepdims=True)
    expo = jnp.where(valid[None, None, :], jnp.exp(scores - highest), 0.0)
    total = jnp.sum(expo, axis=-1)
    mixed = jnp.einsum(
        "qhk,khd->qhd",
        expo.astype(jnp.bfloat16),
        values.reshape(-1, heads, HDIM),
        preferred_element_type=jnp.float32,
    )
    return (mixed / total[..., None]).reshape(height, width).astype(jnp.bfloat16)


def cols_to_rows(cols):
    got = lax.all_to_all(cols, TOK, split_axis=0, concat_axis=0, tiled=True)
    count, rows, width = got.shape
    return jnp.transpose(got, (1, 0, 2)).reshape(rows, count * width)


def shards(
    image_in,
    text_in,
    text_length,
    entry_order,
    step_index,
    image_modulation,
    text_modulation,
    image_to_heads,
    text_to_heads,
    head_gain,
    image_from_heads,
    text_from_heads,
    image_up,
    image_down,
    stale_cache,
    final_modulation,
    final_weight,
    latents,
):
    section = lax.axis_index("section")
    last_section = lax.axis_size("section") - 1
    position = lax.axis_index("ta") * lax.axis_size("tb") + lax.axis_index("tb")
    devices = lax.axis_size("ta") * lax.axis_size("tb")
    image_x = image_in[0, 0].astype(jnp.float32)
    text_x = text_in[0, 0].astype(jnp.float32)
    image_rows = image_x.shape[0]
    text_rows = text_x.shape[0]
    width = image_x.shape[1]
    patch = lax.dynamic_index_in_dim(entry_order[0], section, 0, False)
    step_now = lax.dynamic_index_in_dim(step_index[0], patch, 0, False)
    modul = (
        lax.dynamic_index_in_dim(image_modulation[0], step_now, 0, False)
        .astype(jnp.float32)
        .reshape(6, width)
    )
    text_mod = (
        lax.dynamic_index_in_dim(text_modulation[0], step_now, 0, False)
        .astype(jnp.float32)
        .reshape(3, width)
    )
    image_normed = modulate(image_x, modul[0], modul[1]).astype(jnp.bfloat16)
    text_normed = modulate(text_x, text_mod[0], text_mod[1]).astype(jnp.bfloat16)
    every = lax.all_gather(
        jnp.concatenate([image_normed, text_normed], axis=0), TOK, axis=0, tiled=False
    )
    image_cols = jnp.dot(
        every[:, :image_rows].reshape(-1, width), image_to_heads[0], preferred_element_type=jnp.float32
    ).astype(jnp.bfloat16)
    text_cols = jnp.dot(
        every[:, image_rows:].reshape(-1, width), text_to_heads[0], preferred_element_type=jnp.float32
    ).astype(jnp.bfloat16)
    proj = cols_to_rows(
        jnp.concatenate(
            [
                image_cols.reshape(devices, image_rows, -1),
                text_cols.reshape(devices, text_rows, -1),
            ],
            axis=1,
        )
    )
    image_proj = proj[:image_rows]
    text_proj = proj[image_rows:]
    gains = head_gain[0]
    image_query = head_norm(image_proj[:, :width].astype(jnp.float32), gains[0]).astype(
        jnp.bfloat16
    )
    image_key = head_norm(image_proj[:, width : 2 * width].astype(jnp.float32), gains[1]).astype(
        jnp.bfloat16
    )
    text_query = head_norm(text_proj[:, :width].astype(jnp.float32), gains[2]).astype(jnp.bfloat16)
    text_key = head_norm(text_proj[:, width : 2 * width].astype(jnp.float32), gains[3]).astype(
        jnp.bfloat16
    )
    image_value = image_proj[:, 2 * width :]
    text_value = text_proj[:, 2 * width :]
    stale = stale_cache[0, 0]
    cache_rows = stale.shape[0]
    heads = width // HDIM
    fresh_image = jnp.concatenate([image_key, image_value], axis=1)
    group = lax.axis_size("tb")
    blocks = devices // group
    mine = lax.axis_index("tb")
    quad = [fresh_image]
    for shift in range(1, group):
        turn = [(j * group + b, j * group + (b + shift) % group) for j in range(blocks) for b in range(group)]
        quad.append(lax.ppermute(fresh_image, TOK, turn))
    quad = jnp.stack(quad)
    order = (mine - jnp.arange(group)) % group
    quad = jnp.zeros_like(quad).at[order].set(quad).reshape(-1, fresh_image.shape[1])
    route = [(j * group + b, j + blocks * b) for j in range(blocks) for b in range(group)]
    moved = lax.ppermute(quad, TOK, route)
    patch_len = image_rows * devices
    per_patch = patch_len // cache_rows
    current = jnp.where(position // per_patch == patch, moved, stale)
    row_q = jnp.concatenate([image_query, text_query], axis=0)
    row_k = jnp.concatenate([image_key, text_key], axis=0)
    row_v = jnp.concatenate([image_value, text_value], axis=0)
    pieces = [row_q, row_k, row_v, stale[:, :width], stale[:, width:]]
    pack = jnp.concatenate([piece.reshape(piece.shape[0], heads, HDIM) for piece in pieces], axis=0)
    pack = jnp.transpose(pack, (1, 0, 2))
    pack = jnp.pad(pack, ((0, devices - heads), (0, 0), (0, 0)))
    got = lax.all_to_all(pack, TOK, split_axis=0, concat_axis=0, tiled=True)
    rows = image_rows + text_rows

    def part(first, count):
        return got[:, first : first + count].reshape(-1, HDIM)

    queries = jnp.concatenate([part(0, image_rows), part(image_rows, text_rows)], axis=0)
    fresh_k = part(rows, image_rows)
    text_k = part(rows + image_rows, text_rows)
    fresh_v = part(2 * rows, image_rows)
    text_v = part(2 * rows + image_rows, text_rows)
    cache_k = part(3 * rows, cache_rows)
    cache_v = part(3 * rows + cache_rows, cache_rows)
    begin = patch * patch_len
    cache_k = lax.dynamic_update_slice_in_dim(cache_k, fresh_k, begin, 0)
    cache_v = lax.dynamic_update_slice_in_dim(cache_v, fresh_v, begin, 0)
    keys = jnp.concatenate([cache_k, text_k], axis=0)
    values = jnp.concatenate([cache_v, text_v], axis=0)
    text_count = text_length[0]
    valid = jnp.concatenate(
        [
            jnp.ones((cache_k.shape[0],), bool),
            jnp.arange(text_k.shape[0], dtype=jnp.int32) < text_count,
        ]
    )
    head_out = attend(queries, keys, values, valid)
    image_heads = lax.all_gather(head_out[:patch_len], TOK, axis=0, tiled=False)
    text_heads = lax.all_gather(head_out[patch_len:], TOK, axis=0, tiled=False)
    image_att = jnp.transpose(image_heads[:heads], (1, 0, 2)).reshape(-1, width)
    text_att = jnp.transpose(text_heads[:heads], (1, 0, 2)).reshape(-1, width)
    image_back = cols_to_rows(
        jnp.dot(image_att, image_from_heads[0], preferred_element_type=jnp.float32)
        .astype(jnp.bfloat16)
        .reshape(devices, image_rows, -1)
    )
    text_back = cols_to_rows(
        jnp.dot(text_att, text_from_heads[0], preferred_element_type=jnp.float32)
        .astype(jnp.bfloat16)
        .reshape(devices, text_rows, -1)
    )
    image_mid = image_x + modul[2] * image_back.astype(jnp.float32)
    text_out = (text_x + text_mod[2] * text_back.astype(jnp.float32)).astype(jnp.bfloat16)
    mlp_normed = modulate(image_mid, modul[3], modul[4]).astype(jnp.bfloat16)
    up_weight = image_up[0]
    down_weight = image_down[0]
    hidden = jax.nn.gelu(
        jnp.dot(
            lax.all_gather(mlp_normed, TOK, axis=0, tiled=True),
            up_weight,
            preferred_element_type=jnp.float32,
        ),
        approximate=True,
    ).astype(jnp.bfloat16)
    partial = jnp.dot(hidden, down_weight, preferred_element_type=jnp.float32)
    reduced = jnp.sum(
        lax.all_to_all(
            partial.reshape(devices, image_rows, width), TOK, split_axis=0, concat_axis=0, tiled=True
        ),
        axis=0,
    )
    image_out = (image_mid + modul[5] * reduced).astype(jnp.bfloat16)
    text_next = from_behind(text_out, "section", 1)
    image_next = from_behind(image_out, "section", 1)
    final_source = jnp.where(section == last_section, image_out, image_next)
    patch_last = entry_order[0, last_section]
    step_last = lax.dynamic_index_in_dim(step_index[0], patch_last, 0, False)
    final_mod = (
        lax.dynamic_index_in_dim(final_modulation, step_last, 0, False)
        .astype(jnp.float32)
        .reshape(2, width)
    )
    normed = modulate(final_source.astype(jnp.float32), final_mod[0], final_mod[1]).astype(
        jnp.bfloat16
    )
    velocity = jnp.dot(normed, final_weight, preferred_element_type=jnp.float32)
    latents_next = latents[0] + -1.0 / TSTEPS * velocity
    return (image_next[None, None], text_next[None, None], current[None, None], latents_next[None])


def solution(mesh):
    shape = mesh.devices.shape
    split = jax.sharding.Mesh(
        mesh.devices.reshape(shape[:2] + (shape[2] // QUAD, QUAD)),
        ("section", "grp", "ta", "tb"),
    )
    placed = (
        P("section", "grp", TOK, None),
        P("section", "grp", TOK, None),
        P("grp"),
        P("grp", None),
        P("grp", None),
        P("section", None, None),
        P("section", None, None),
        P("section", None, TOK),
        P("section", None, TOK),
        P("section", None, None),
        P("section", None, TOK),
        P("section", None, TOK),
        P("section", None, TOK),
        P("section", TOK, None),
        P("section", "grp", TOK, None),
        P(),
        P(None, "section"),
        P("grp", TOK, "section"),
    )
    return jax.shard_map(
        shards,
        mesh=split,
        in_specs=placed,
        out_specs=(
            P("section", "grp", TOK, None),
            P("section", "grp", TOK, None),
            P("section", "grp", TOK, None),
            P("grp", TOK, "section"),
        ),
        check_vma=False,
    )
```

```python
import jax
import jax.numpy as jnp
from jax import lax
from jax.sharding import PartitionSpec as P

HDIM = 128
TSTEPS = 4


TOK = ("ta", "tb")
QUAD = 4

eps = 1e-06
masked_score = -1e30


def from_behind(block, axis, distance):
    devices = range(lax.axis_size(axis))
    route = [((i - distance) % len(devices), i) for i in devices]
    return lax.ppermute(block, axis, route)


def layer_norm(field):
    mean = jnp.mean(field, axis=-1, keepdims=True)
    centred = field - mean
    spread = jnp.mean(centred * centred, axis=-1, keepdims=True)
    return centred * lax.rsqrt(spread + eps)


def modulate(field, shift, scale):
    return layer_norm(field) * (1.0 + scale) + shift


def head_norm(field, gain):
    height, width = field.shape
    shaped = field.reshape(height, width // HDIM, HDIM)
    power = jnp.mean(shaped * shaped, axis=-1, keepdims=True)
    return (shaped * lax.rsqrt(power + eps) * gain).reshape(height, width)


def attend(queries, keys, values, valid):
    height, width = queries.shape
    heads = width // HDIM
    scores = jnp.einsum(
        "qhd,khd->qhk",
        queries.reshape(height, heads, HDIM),
        keys.reshape(-1, heads, HDIM),
        preferred_element_type=jnp.float32,
    ) * HDIM ** (-0.5)
    scores = jnp.where(valid[None, None, :], scores, masked_score)
    highest = jnp.max(scores, axis=-1, keepdims=True)
    expo = jnp.where(valid[None, None, :], jnp.exp(scores - highest), 0.0)
    total = jnp.sum(expo, axis=-1)
    mixed = jnp.einsum(
        "qhk,khd->qhd",
        expo.astype(jnp.bfloat16),
        values.reshape(-1, heads, HDIM),
        preferred_element_type=jnp.float32,
    )
    return (mixed / total[..., None]).reshape(height, width).astype(jnp.bfloat16)


def cols_to_rows(cols):
    got = lax.all_to_all(cols, TOK, split_axis=0, concat_axis=0, tiled=True)
    count, rows, width = got.shape
    return jnp.transpose(got, (1, 0, 2)).reshape(rows, count * width)


def shards(
    image_in,
    text_in,
    text_length,
    entry_order,
    step_index,
    image_modulation,
    text_modulation,
    image_to_heads,
    text_to_heads,
    head_gain,
    image_from_heads,
    text_from_heads,
    image_up,
    image_down,
    stale_cache,
    final_modulation,
    final_weight,
    latents,
):
    section = lax.axis_index("section")
    last_section = lax.axis_size("section") - 1
    position = lax.axis_index("ta") * lax.axis_size("tb") + lax.axis_index("tb")
    devices = lax.axis_size("ta") * lax.axis_size("tb")
    image_x = image_in[0, 0].astype(jnp.float32)
    text_x = text_in[0, 0].astype(jnp.float32)
    image_rows = image_x.shape[0]
    text_rows = text_x.shape[0]
    width = image_x.shape[1]
    patch = lax.dynamic_index_in_dim(entry_order[0], section, 0, False)
    step_now = lax.dynamic_index_in_dim(step_index[0], patch, 0, False)
    modul = (
        lax.dynamic_index_in_dim(image_modulation[0], step_now, 0, False)
        .astype(jnp.float32)
        .reshape(6, width)
    )
    text_mod = (
        lax.dynamic_index_in_dim(text_modulation[0], step_now, 0, False)
        .astype(jnp.float32)
        .reshape(3, width)
    )
    image_normed = modulate(image_x, modul[0], modul[1]).astype(jnp.bfloat16)
    text_normed = modulate(text_x, text_mod[0], text_mod[1]).astype(jnp.bfloat16)
    every = lax.all_gather(
        jnp.concatenate([image_normed, text_normed], axis=0), TOK, axis=0, tiled=False
    )
    image_cols = jnp.dot(
        every[:, :image_rows].reshape(-1, width), image_to_heads[0], preferred_element_type=jnp.float32
    ).astype(jnp.bfloat16)
    text_cols = jnp.dot(
        every[:, image_rows:].reshape(-1, width), text_to_heads[0], preferred_element_type=jnp.float32
    ).astype(jnp.bfloat16)
    proj = cols_to_rows(
        jnp.concatenate(
            [
                image_cols.reshape(devices, image_rows, -1),
                text_cols.reshape(devices, text_rows, -1),
            ],
            axis=1,
        )
    )
    image_proj = proj[:image_rows]
    text_proj = proj[image_rows:]
    gains = head_gain[0]
    image_query = head_norm(image_proj[:, :width].astype(jnp.float32), gains[0]).astype(
        jnp.bfloat16
    )
    image_key = head_norm(image_proj[:, width : 2 * width].astype(jnp.float32), gains[1]).astype(
        jnp.bfloat16
    )
    text_query = head_norm(text_proj[:, :width].astype(jnp.float32), gains[2]).astype(jnp.bfloat16)
    text_key = head_norm(text_proj[:, width : 2 * width].astype(jnp.float32), gains[3]).astype(
        jnp.bfloat16
    )
    image_value = image_proj[:, 2 * width :]
    text_value = text_proj[:, 2 * width :]
    stale = stale_cache[0, 0]
    cache_rows = stale.shape[0]
    heads = width // HDIM
    fresh_image = jnp.concatenate([image_key, image_value], axis=1)
    group = lax.axis_size("tb")
    blocks = devices // group
    mine = lax.axis_index("tb")
    quad = [fresh_image]
    for shift in range(1, group):
        turn = [(j * group + b, j * group + (b + shift) % group) for j in range(blocks) for b in range(group)]
        quad.append(lax.ppermute(fresh_image, TOK, turn))
    quad = jnp.stack(quad)
    order = (mine - jnp.arange(group)) % group
    quad = jnp.zeros_like(quad).at[order].set(quad).reshape(-1, fresh_image.shape[1])
    route = [(j * group + b, j + blocks * b) for j in range(blocks) for b in range(group)]
    moved = lax.ppermute(quad, TOK, route)
    patch_len = image_rows * devices
    per_patch = patch_len // cache_rows
    current = jnp.where(position // per_patch == patch, moved, stale)
    row_q = jnp.concatenate([image_query, text_query], axis=0)
    row_k = jnp.concatenate([image_key, text_key], axis=0)
    row_v = jnp.concatenate([image_value, text_value], axis=0)
    def by_head(pieces):
        pack = jnp.concatenate(
            [piece.reshape(piece.shape[0], heads, HDIM) for piece in pieces], axis=0
        )
        pack = jnp.transpose(pack, (1, 0, 2))
        pack = jnp.pad(pack, ((0, devices - heads), (0, 0), (0, 0)))
        return lax.all_to_all(pack, TOK, split_axis=0, concat_axis=0, tiled=True)

    got_cache = by_head([stale[:, :width], stale[:, width:]])
    got = by_head([row_q, row_k, row_v])
    rows = image_rows + text_rows

    def part(first, count, source=got):
        return source[:, first : first + count].reshape(-1, HDIM)

    queries = jnp.concatenate([part(0, image_rows), part(image_rows, text_rows)], axis=0)
    fresh_k = part(rows, image_rows)
    text_k = part(rows + image_rows, text_rows)
    fresh_v = part(2 * rows, image_rows)
    text_v = part(2 * rows + image_rows, text_rows)
    cache_k = part(0, cache_rows, got_cache)
    cache_v = part(cache_rows, cache_rows, got_cache)
    begin = patch * patch_len
    cache_k = lax.dynamic_update_slice_in_dim(cache_k, fresh_k, begin, 0)
    cache_v = lax.dynamic_update_slice_in_dim(cache_v, fresh_v, begin, 0)
    keys = jnp.concatenate([cache_k, text_k], axis=0)
    values = jnp.concatenate([cache_v, text_v], axis=0)
    text_count = text_length[0]
    valid = jnp.concatenate(
        [
            jnp.ones((cache_k.shape[0],), bool),
            jnp.arange(text_k.shape[0], dtype=jnp.int32) < text_count,
        ]
    )
    head_out = attend(queries, keys, values, valid)
    image_block = head_out[:patch_len]
    image_heads = lax.all_to_all(
        jnp.broadcast_to(image_block[None], (devices,) + image_block.shape),
        TOK,
        split_axis=0,
        concat_axis=0,
        tiled=True,
    )
    text_heads = lax.all_gather(head_out[patch_len:], TOK, axis=0, tiled=False)
    image_att = jnp.transpose(image_heads[:heads], (1, 0, 2)).reshape(-1, width)
    text_att = jnp.transpose(text_heads[:heads], (1, 0, 2)).reshape(-1, width)
    image_back = cols_to_rows(
        jnp.dot(image_att, image_from_heads[0], preferred_element_type=jnp.float32)
        .astype(jnp.bfloat16)
        .reshape(devices, image_rows, -1)
    )
    text_back = cols_to_rows(
        jnp.dot(text_att, text_from_heads[0], preferred_element_type=jnp.float32)
        .astype(jnp.bfloat16)
        .reshape(devices, text_rows, -1)
    )
    image_mid = image_x + modul[2] * image_back.astype(jnp.float32)
    text_out = (text_x + text_mod[2] * text_back.astype(jnp.float32)).astype(jnp.bfloat16)
    mlp_normed = modulate(image_mid, modul[3], modul[4]).astype(jnp.bfloat16)
    up_weight = image_up[0]
    down_weight = image_down[0]
    hidden = jax.nn.gelu(
        jnp.dot(
            lax.all_gather(mlp_normed, TOK, axis=0, tiled=True),
            up_weight,
            preferred_element_type=jnp.float32,
        ),
        approximate=True,
    ).astype(jnp.bfloat16)
    partial = jnp.dot(hidden, down_weight, preferred_element_type=jnp.float32)
    reduced = jnp.sum(
        lax.all_to_all(
            partial.reshape(devices, image_rows, width), TOK, split_axis=0, concat_axis=0, tiled=True
        ),
        axis=0,
    )
    image_out = (image_mid + modul[5] * reduced).astype(jnp.bfloat16)
    text_next = from_behind(text_out, "section", 1)
    image_next = from_behind(image_out, "section", 1)
    final_source = jnp.where(section == last_section, image_out, image_next)
    patch_last = entry_order[0, last_section]
    step_last = lax.dynamic_index_in_dim(step_index[0], patch_last, 0, False)
    final_mod = (
        lax.dynamic_index_in_dim(final_modulation, step_last, 0, False)
        .astype(jnp.float32)
        .reshape(2, width)
    )
    normed = modulate(final_source.astype(jnp.float32), final_mod[0], final_mod[1]).astype(
        jnp.bfloat16
    )
    velocity = jnp.dot(normed, final_weight, preferred_element_type=jnp.float32)
    latents_next = latents[0] + -1.0 / TSTEPS * velocity
    return (image_next[None, None], text_next[None, None], current[None, None], latents_next[None])


def solution(mesh):
    shape = mesh.devices.shape
    split = jax.sharding.Mesh(
        mesh.devices.reshape(shape[:2] + (shape[2] // QUAD, QUAD)),
        ("section", "grp", "ta", "tb"),
    )
    placed = (
        P("section", "grp", TOK, None),
        P("section", "grp", TOK, None),
        P("grp"),
        P("grp", None),
        P("grp", None),
        P("section", None, None),
        P("section", None, None),
        P("section", None, TOK),
        P("section", None, TOK),
        P("section", None, None),
        P("section", None, TOK),
        P("section", None, TOK),
        P("section", None, TOK),
        P("section", TOK, None),
        P("section", "grp", TOK, None),
        P(),
        P(None, "section"),
        P("grp", TOK, "section"),
    )
    return jax.shard_map(
        shards,
        mesh=split,
        in_specs=placed,
        out_specs=(
            P("section", "grp", TOK, None),
            P("section", "grp", TOK, None),
            P("section", "grp", TOK, None),
            P("grp", TOK, "section"),
        ),
        check_vma=False,
    )
```

```python
import jax
import jax.numpy as jnp
from jax import lax
from jax.sharding import PartitionSpec as P

HDIM = 128
TSTEPS = 4


TOK = ("ta", "tb")
QUAD = 4

eps = 1e-06
masked_score = -1e30


def from_behind(block, axis, distance):
    devices = range(lax.axis_size(axis))
    route = [((i - distance) % len(devices), i) for i in devices]
    return lax.ppermute(block, axis, route)


def layer_norm(field):
    mean = jnp.mean(field, axis=-1, keepdims=True)
    centred = field - mean
    spread = jnp.mean(centred * centred, axis=-1, keepdims=True)
    return centred * lax.rsqrt(spread + eps)


def modulate(field, shift, scale):
    return layer_norm(field) * (1.0 + scale) + shift


def head_norm(field, gain):
    height, width = field.shape
    shaped = field.reshape(height, width // HDIM, HDIM)
    power = jnp.mean(shaped * shaped, axis=-1, keepdims=True)
    return (shaped * lax.rsqrt(power + eps) * gain).reshape(height, width)


def attend(queries, keys, values, valid):
    height, width = queries.shape
    heads = width // HDIM
    scores = jnp.einsum(
        "qhd,khd->qhk",
        queries.reshape(height, heads, HDIM),
        keys.reshape(-1, heads, HDIM),
        preferred_element_type=jnp.float32,
    ) * HDIM ** (-0.5)
    scores = jnp.where(valid[None, None, :], scores, masked_score)
    highest = jnp.max(scores, axis=-1, keepdims=True)
    expo = jnp.where(valid[None, None, :], jnp.exp(scores - highest), 0.0)
    total = jnp.sum(expo, axis=-1)
    mixed = jnp.einsum(
        "qhk,khd->qhd",
        expo.astype(jnp.bfloat16),
        values.reshape(-1, heads, HDIM),
        preferred_element_type=jnp.float32,
    )
    return (mixed / total[..., None]).reshape(height, width).astype(jnp.bfloat16)


def cols_to_rows(cols):
    got = lax.all_to_all(cols, TOK, split_axis=0, concat_axis=0, tiled=True)
    count, rows, width = got.shape
    return jnp.transpose(got, (1, 0, 2)).reshape(rows, count * width)


def broadcast_rows(block, devices):
    copies = jnp.broadcast_to(block[None], (devices,) + block.shape)
    got = lax.all_to_all(copies, TOK, split_axis=0, concat_axis=0, tiled=True)
    return got.reshape(-1, block.shape[-1])


def shards(
    image_in,
    text_in,
    text_length,
    entry_order,
    step_index,
    image_modulation,
    text_modulation,
    image_to_heads,
    text_to_heads,
    head_gain,
    image_from_heads,
    text_from_heads,
    image_up,
    image_down,
    stale_cache,
    final_modulation,
    final_weight,
    latents,
):
    section = lax.axis_index("section")
    last_section = lax.axis_size("section") - 1
    position = lax.axis_index("ta") * lax.axis_size("tb") + lax.axis_index("tb")
    devices = lax.axis_size("ta") * lax.axis_size("tb")
    image_x = image_in[0, 0].astype(jnp.float32)
    text_x = text_in[0, 0].astype(jnp.float32)
    image_rows = image_x.shape[0]
    text_rows = text_x.shape[0]
    width = image_x.shape[1]
    patch = lax.dynamic_index_in_dim(entry_order[0], section, 0, False)
    step_now = lax.dynamic_index_in_dim(step_index[0], patch, 0, False)
    modul = (
        lax.dynamic_index_in_dim(image_modulation[0], step_now, 0, False)
        .astype(jnp.float32)
        .reshape(6, width)
    )
    text_mod = (
        lax.dynamic_index_in_dim(text_modulation[0], step_now, 0, False)
        .astype(jnp.float32)
        .reshape(3, width)
    )
    image_normed = modulate(image_x, modul[0], modul[1]).astype(jnp.bfloat16)
    text_normed = modulate(text_x, text_mod[0], text_mod[1]).astype(jnp.bfloat16)
    stale = stale_cache[0, 0]
    cache_rows = stale.shape[0]
    heads = width // HDIM

    def by_head(pieces):
        pack = jnp.concatenate(
            [piece.reshape(piece.shape[0], heads, HDIM) for piece in pieces], axis=0
        )
        pack = jnp.transpose(pack, (1, 0, 2))
        pack = jnp.pad(pack, ((0, devices - heads), (0, 0), (0, 0)))
        return lax.all_to_all(pack, TOK, split_axis=0, concat_axis=0, tiled=True)

    got_cache = by_head([stale[:, :width], stale[:, width:]])
    got_cache, image_normed, text_normed = lax.optimization_barrier(
        (got_cache, image_normed, text_normed)
    )
    every = lax.all_gather(
        jnp.concatenate([image_normed, text_normed], axis=0), TOK, axis=0, tiled=False
    )
    image_cols = jnp.dot(
        every[:, :image_rows].reshape(-1, width), image_to_heads[0], preferred_element_type=jnp.float32
    ).astype(jnp.bfloat16)
    text_cols = jnp.dot(
        every[:, image_rows:].reshape(-1, width), text_to_heads[0], preferred_element_type=jnp.float32
    ).astype(jnp.bfloat16)
    proj = cols_to_rows(
        jnp.concatenate(
            [
                image_cols.reshape(devices, image_rows, -1),
                text_cols.reshape(devices, text_rows, -1),
            ],
            axis=1,
        )
    )
    image_proj = proj[:image_rows]
    text_proj = proj[image_rows:]
    gains = head_gain[0]
    image_query = head_norm(image_proj[:, :width].astype(jnp.float32), gains[0]).astype(
        jnp.bfloat16
    )
    image_key = head_norm(image_proj[:, width : 2 * width].astype(jnp.float32), gains[1]).astype(
        jnp.bfloat16
    )
    text_query = head_norm(text_proj[:, :width].astype(jnp.float32), gains[2]).astype(jnp.bfloat16)
    text_key = head_norm(text_proj[:, width : 2 * width].astype(jnp.float32), gains[3]).astype(
        jnp.bfloat16
    )
    image_value = image_proj[:, 2 * width :]
    text_value = text_proj[:, 2 * width :]
    fresh_image = jnp.concatenate([image_key, image_value], axis=1)
    group = lax.axis_size("tb")
    blocks = devices // group
    mine = lax.axis_index("tb")
    quad = [fresh_image]
    for shift in range(1, group):
        turn = [(j * group + b, j * group + (b + shift) % group) for j in range(blocks) for b in range(group)]
        quad.append(lax.ppermute(fresh_image, TOK, turn))
    quad = jnp.stack(quad)
    order = (mine - jnp.arange(group)) % group
    quad = jnp.zeros_like(quad).at[order].set(quad).reshape(-1, fresh_image.shape[1])
    route = [(j * group + b, j + blocks * b) for j in range(blocks) for b in range(group)]
    moved = lax.ppermute(quad, TOK, route)
    patch_len = image_rows * devices
    per_patch = patch_len // cache_rows
    current = jnp.where(position // per_patch == patch, moved, stale)
    row_q = jnp.concatenate([image_query, text_query], axis=0)
    row_k = jnp.concatenate([image_key, text_key], axis=0)
    row_v = jnp.concatenate([image_value, text_value], axis=0)
    got = by_head([row_q, row_k, row_v])
    rows = image_rows + text_rows

    def part(first, count, source=got):
        return source[:, first : first + count].reshape(-1, HDIM)

    queries = jnp.concatenate([part(0, image_rows), part(image_rows, text_rows)], axis=0)
    fresh_k = part(rows, image_rows)
    text_k = part(rows + image_rows, text_rows)
    fresh_v = part(2 * rows, image_rows)
    text_v = part(2 * rows + image_rows, text_rows)
    cache_k = part(0, cache_rows, got_cache)
    cache_v = part(cache_rows, cache_rows, got_cache)
    begin = patch * patch_len
    cache_k = lax.dynamic_update_slice_in_dim(cache_k, fresh_k, begin, 0)
    cache_v = lax.dynamic_update_slice_in_dim(cache_v, fresh_v, begin, 0)
    keys = jnp.concatenate([cache_k, text_k], axis=0)
    values = jnp.concatenate([cache_v, text_v], axis=0)
    text_count = text_length[0]
    valid = jnp.concatenate(
        [
            jnp.ones((cache_k.shape[0],), bool),
            jnp.arange(text_k.shape[0], dtype=jnp.int32) < text_count,
        ]
    )
    head_out = attend(queries, keys, values, valid)
    image_heads = broadcast_rows(head_out[:patch_len], devices).reshape(devices, patch_len, HDIM)
    text_heads = lax.all_gather(head_out[patch_len:], TOK, axis=0, tiled=False)
    image_att = jnp.transpose(image_heads[:heads], (1, 0, 2)).reshape(-1, width)
    text_att = jnp.transpose(text_heads[:heads], (1, 0, 2)).reshape(-1, width)
    image_back = cols_to_rows(
        jnp.dot(image_att, image_from_heads[0], preferred_element_type=jnp.float32)
        .astype(jnp.bfloat16)
        .reshape(devices, image_rows, -1)
    )
    text_back = cols_to_rows(
        jnp.dot(text_att, text_from_heads[0], preferred_element_type=jnp.float32)
        .astype(jnp.bfloat16)
        .reshape(devices, text_rows, -1)
    )
    image_mid = image_x + modul[2] * image_back.astype(jnp.float32)
    text_out = (text_x + text_mod[2] * text_back.astype(jnp.float32)).astype(jnp.bfloat16)
    mlp_normed = modulate(image_mid, modul[3], modul[4]).astype(jnp.bfloat16)
    up_weight = image_up[0]
    down_weight = image_down[0]
    hidden = jax.nn.gelu(
        jnp.dot(
            broadcast_rows(mlp_normed, devices),
            up_weight,
            preferred_element_type=jnp.float32,
        ),
        approximate=True,
    ).astype(jnp.bfloat16)
    partial = jnp.dot(hidden, down_weight, preferred_element_type=jnp.float32)
    reduced = jnp.sum(
        lax.all_to_all(
            partial.reshape(devices, image_rows, width), TOK, split_axis=0, concat_axis=0, tiled=True
        ),
        axis=0,
    )
    image_out = (image_mid + modul[5] * reduced).astype(jnp.bfloat16)
    text_next = from_behind(text_out, "section", 1)
    image_next = from_behind(image_out, "section", 1)
    final_source = jnp.where(section == last_section, image_out, image_next)
    patch_last = entry_order[0, last_section]
    step_last = lax.dynamic_index_in_dim(step_index[0], patch_last, 0, False)
    final_mod = (
        lax.dynamic_index_in_dim(final_modulation, step_last, 0, False)
        .astype(jnp.float32)
        .reshape(2, width)
    )
    normed = modulate(final_source.astype(jnp.float32), final_mod[0], final_mod[1]).astype(
        jnp.bfloat16
    )
    velocity = jnp.dot(normed, final_weight, preferred_element_type=jnp.float32)
    latents_next = latents[0] + -1.0 / TSTEPS * velocity
    return (image_next[None, None], text_next[None, None], current[None, None], latents_next[None])


def solution(mesh):
    shape = mesh.devices.shape
    split = jax.sharding.Mesh(
        mesh.devices.reshape(shape[:2] + (shape[2] // QUAD, QUAD)),
        ("section", "grp", "ta", "tb"),
    )
    placed = (
        P("section", "grp", TOK, None),
        P("section", "grp", TOK, None),
        P("grp"),
        P("grp", None),
        P("grp", None),
        P("section", None, None),
        P("section", None, None),
        P("section", None, TOK),
        P("section", None, TOK),
        P("section", None, None),
        P("section", None, TOK),
        P("section", None, TOK),
        P("section", None, TOK),
        P("section", TOK, None),
        P("section", "grp", TOK, None),
        P(),
        P(None, "section"),
        P("grp", TOK, "section"),
    )
    return jax.shard_map(
        shards,
        mesh=split,
        in_specs=placed,
        out_specs=(
            P("section", "grp", TOK, None),
            P("section", "grp", TOK, None),
            P("section", "grp", TOK, None),
            P("grp", TOK, "section"),
        ),
        check_vma=False,
    )
```

```python
import jax
import jax.numpy as jnp
from jax import lax
from jax.sharding import PartitionSpec as P

HDIM = 128
TSTEPS = 4


TOK = ("ta", "tb")
QUAD = 4

eps = 1e-06
masked_score = -1e30


def from_behind(block, axis, distance):
    devices = range(lax.axis_size(axis))
    route = [((i - distance) % len(devices), i) for i in devices]
    return lax.ppermute(block, axis, route)


def layer_norm(field):
    mean = jnp.mean(field, axis=-1, keepdims=True)
    centred = field - mean
    spread = jnp.mean(centred * centred, axis=-1, keepdims=True)
    return centred * lax.rsqrt(spread + eps)


def modulate(field, shift, scale):
    return layer_norm(field) * (1.0 + scale) + shift


def head_norm(field, gain):
    height, width = field.shape
    shaped = field.reshape(height, width // HDIM, HDIM)
    power = jnp.mean(shaped * shaped, axis=-1, keepdims=True)
    return (shaped * lax.rsqrt(power + eps) * gain).reshape(height, width)


def attend(queries, keys, values, valid):
    height, width = queries.shape
    heads = width // HDIM
    scores = jnp.einsum(
        "qhd,khd->qhk",
        queries.reshape(height, heads, HDIM),
        keys.reshape(-1, heads, HDIM),
        preferred_element_type=jnp.float32,
    ) * HDIM ** (-0.5)
    scores = jnp.where(valid[None, None, :], scores, masked_score)
    highest = jnp.max(scores, axis=-1, keepdims=True)
    expo = jnp.where(valid[None, None, :], jnp.exp(scores - highest), 0.0)
    total = jnp.sum(expo, axis=-1)
    mixed = jnp.einsum(
        "qhk,khd->qhd",
        expo.astype(jnp.bfloat16),
        values.reshape(-1, heads, HDIM),
        preferred_element_type=jnp.float32,
    )
    return (mixed / total[..., None]).reshape(height, width).astype(jnp.bfloat16)


def cols_to_rows(cols):
    got = lax.all_to_all(cols, TOK, split_axis=0, concat_axis=0, tiled=True)
    count, rows, width = got.shape
    return jnp.transpose(got, (1, 0, 2)).reshape(rows, count * width)


def broadcast_rows(block, devices):
    copies = jnp.broadcast_to(block[None], (devices,) + block.shape)
    got = lax.all_to_all(copies, TOK, split_axis=0, concat_axis=0, tiled=True)
    return got.reshape(-1, block.shape[-1])


def shards(
    image_in,
    text_in,
    text_length,
    entry_order,
    step_index,
    image_modulation,
    text_modulation,
    image_to_heads,
    text_to_heads,
    head_gain,
    image_from_heads,
    text_from_heads,
    image_up,
    image_down,
    stale_cache,
    final_modulation,
    final_weight,
    latents,
):
    section = lax.axis_index("section")
    last_section = lax.axis_size("section") - 1
    position = lax.axis_index("ta") * lax.axis_size("tb") + lax.axis_index("tb")
    devices = lax.axis_size("ta") * lax.axis_size("tb")
    image_x = image_in[0, 0].astype(jnp.float32)
    text_x = text_in[0, 0].astype(jnp.float32)
    image_rows = image_x.shape[0]
    text_rows = text_x.shape[0]
    width = image_x.shape[1]
    patch = lax.dynamic_index_in_dim(entry_order[0], section, 0, False)
    step_now = lax.dynamic_index_in_dim(step_index[0], patch, 0, False)
    modul = (
        lax.dynamic_index_in_dim(image_modulation[0], step_now, 0, False)
        .astype(jnp.float32)
        .reshape(6, width)
    )
    text_mod = (
        lax.dynamic_index_in_dim(text_modulation[0], step_now, 0, False)
        .astype(jnp.float32)
        .reshape(3, width)
    )
    image_normed = modulate(image_x, modul[0], modul[1]).astype(jnp.bfloat16)
    text_normed = modulate(text_x, text_mod[0], text_mod[1]).astype(jnp.bfloat16)
    stale = stale_cache[0, 0]
    cache_rows = stale.shape[0]
    heads = width // HDIM

    def by_head(pieces):
        pack = jnp.concatenate(
            [piece.reshape(piece.shape[0], heads, HDIM) for piece in pieces], axis=0
        )
        pack = jnp.transpose(pack, (1, 0, 2))
        pack = jnp.pad(pack, ((0, devices - heads), (0, 0), (0, 0)))
        return lax.all_to_all(pack, TOK, split_axis=0, concat_axis=0, tiled=True)

    got_cache = by_head([stale[:, :width], stale[:, width:]])
    got_cache, image_normed, text_normed = lax.optimization_barrier(
        (got_cache, image_normed, text_normed)
    )
    every = lax.all_gather(
        jnp.concatenate([image_normed, text_normed], axis=0), TOK, axis=0, tiled=False
    )
    image_cols = jnp.dot(
        every[:, :image_rows].reshape(-1, width), image_to_heads[0], preferred_element_type=jnp.float32
    ).astype(jnp.bfloat16)
    text_cols = jnp.dot(
        every[:, image_rows:].reshape(-1, width), text_to_heads[0], preferred_element_type=jnp.float32
    ).astype(jnp.bfloat16)
    proj = cols_to_rows(
        jnp.concatenate(
            [
                image_cols.reshape(devices, image_rows, -1),
                text_cols.reshape(devices, text_rows, -1),
            ],
            axis=1,
        )
    )
    image_proj = proj[:image_rows]
    text_proj = proj[image_rows:]
    gains = head_gain[0]
    image_query = head_norm(image_proj[:, :width].astype(jnp.float32), gains[0]).astype(
        jnp.bfloat16
    )
    image_key = head_norm(image_proj[:, width : 2 * width].astype(jnp.float32), gains[1]).astype(
        jnp.bfloat16
    )
    text_query = head_norm(text_proj[:, :width].astype(jnp.float32), gains[2]).astype(jnp.bfloat16)
    text_key = head_norm(text_proj[:, width : 2 * width].astype(jnp.float32), gains[3]).astype(
        jnp.bfloat16
    )
    image_value = image_proj[:, 2 * width :]
    text_value = text_proj[:, 2 * width :]
    fresh_image = jnp.concatenate([image_key, image_value], axis=1)
    patch_len = image_rows * devices
    per_patch = patch_len // cache_rows
    row_q = jnp.concatenate([image_query, text_query], axis=0)
    row_k = jnp.concatenate([image_key, text_key], axis=0)
    row_v = jnp.concatenate([image_value, text_value], axis=0)
    got = by_head([row_q, row_k, row_v])
    rows = image_rows + text_rows

    def part(first, count, source=got):
        return source[:, first : first + count].reshape(-1, HDIM)

    queries = jnp.concatenate([part(0, image_rows), part(image_rows, text_rows)], axis=0)
    fresh_k = part(rows, image_rows)
    text_k = part(rows + image_rows, text_rows)
    fresh_v = part(2 * rows, image_rows)
    text_v = part(2 * rows + image_rows, text_rows)
    cache_k = part(0, cache_rows, got_cache)
    cache_v = part(cache_rows, cache_rows, got_cache)
    begin = patch * patch_len
    cache_k = lax.dynamic_update_slice_in_dim(cache_k, fresh_k, begin, 0)
    cache_v = lax.dynamic_update_slice_in_dim(cache_v, fresh_v, begin, 0)
    keys = jnp.concatenate([cache_k, text_k], axis=0)
    values = jnp.concatenate([cache_v, text_v], axis=0)
    text_count = text_length[0]
    valid = jnp.concatenate(
        [
            jnp.ones((cache_k.shape[0],), bool),
            jnp.arange(text_k.shape[0], dtype=jnp.int32) < text_count,
        ]
    )
    head_out = attend(queries, keys, values, valid)
    image_heads = broadcast_rows(head_out[:patch_len], devices).reshape(devices, patch_len, HDIM)
    riders = fresh_image.reshape(-1, HDIM)
    text_heads = lax.all_gather(
        jnp.concatenate([head_out[patch_len:], riders], axis=0), TOK, axis=0, tiled=False
    )
    text_len = head_out.shape[0] - patch_len
    fresh_all = text_heads[:, text_len:].reshape(patch_len, -1)
    text_heads = text_heads[:, :text_len]
    moved = lax.dynamic_slice_in_dim(
        fresh_all, (position % per_patch) * cache_rows, cache_rows, 0
    )
    current = jnp.where(position // per_patch == patch, moved, stale)
    image_att = jnp.transpose(image_heads[:heads], (1, 0, 2)).reshape(-1, width)
    text_att = jnp.transpose(text_heads[:heads], (1, 0, 2)).reshape(-1, width)
    image_back = cols_to_rows(
        jnp.dot(image_att, image_from_heads[0], preferred_element_type=jnp.float32)
        .astype(jnp.bfloat16)
        .reshape(devices, image_rows, -1)
    )
    text_back = cols_to_rows(
        jnp.dot(text_att, text_from_heads[0], preferred_element_type=jnp.float32)
        .astype(jnp.bfloat16)
        .reshape(devices, text_rows, -1)
    )
    image_mid = image_x + modul[2] * image_back.astype(jnp.float32)
    text_out = (text_x + text_mod[2] * text_back.astype(jnp.float32)).astype(jnp.bfloat16)
    mlp_normed = modulate(image_mid, modul[3], modul[4]).astype(jnp.bfloat16)
    up_weight = image_up[0]
    down_weight = image_down[0]
    hidden = jax.nn.gelu(
        jnp.dot(
            broadcast_rows(mlp_normed, devices),
            up_weight,
            preferred_element_type=jnp.float32,
        ),
        approximate=True,
    ).astype(jnp.bfloat16)
    partial = jnp.dot(hidden, down_weight, preferred_element_type=jnp.float32)
    reduced = jnp.sum(
        lax.all_to_all(
            partial.reshape(devices, image_rows, width), TOK, split_axis=0, concat_axis=0, tiled=True
        ),
        axis=0,
    )
    image_out = (image_mid + modul[5] * reduced).astype(jnp.bfloat16)
    text_next = from_behind(text_out, "section", 1)
    image_next = from_behind(image_out, "section", 1)
    final_source = jnp.where(section == last_section, image_out, image_next)
    patch_last = entry_order[0, last_section]
    step_last = lax.dynamic_index_in_dim(step_index[0], patch_last, 0, False)
    final_mod = (
        lax.dynamic_index_in_dim(final_modulation, step_last, 0, False)
        .astype(jnp.float32)
        .reshape(2, width)
    )
    normed = modulate(final_source.astype(jnp.float32), final_mod[0], final_mod[1]).astype(
        jnp.bfloat16
    )
    velocity = jnp.dot(normed, final_weight, preferred_element_type=jnp.float32)
    latents_next = latents[0] + -1.0 / TSTEPS * velocity
    return (image_next[None, None], text_next[None, None], current[None, None], latents_next[None])


def solution(mesh):
    shape = mesh.devices.shape
    split = jax.sharding.Mesh(
        mesh.devices.reshape(shape[:2] + (shape[2] // QUAD, QUAD)),
        ("section", "grp", "ta", "tb"),
    )
    placed = (
        P("section", "grp", TOK, None),
        P("section", "grp", TOK, None),
        P("grp"),
        P("grp", None),
        P("grp", None),
        P("section", None, None),
        P("section", None, None),
        P("section", None, TOK),
        P("section", None, TOK),
        P("section", None, None),
        P("section", None, TOK),
        P("section", None, TOK),
        P("section", None, TOK),
        P("section", TOK, None),
        P("section", "grp", TOK, None),
        P(),
        P(None, "section"),
        P("grp", TOK, "section"),
    )
    return jax.shard_map(
        shards,
        mesh=split,
        in_specs=placed,
        out_specs=(
            P("section", "grp", TOK, None),
            P("section", "grp", TOK, None),
            P("section", "grp", TOK, None),
            P("grp", TOK, "section"),
        ),
        check_vma=False,
    )
```

```python
import jax
import jax.numpy as jnp
from jax import lax
from jax.sharding import PartitionSpec as P

HDIM = 128
TSTEPS = 4


TOK = ("ta", "tb")
QUAD = 4

eps = 1e-06
masked_score = -1e30


def from_behind(block, axis, distance):
    devices = range(lax.axis_size(axis))
    route = [((i - distance) % len(devices), i) for i in devices]
    return lax.ppermute(block, axis, route)


def layer_norm(field):
    mean = jnp.mean(field, axis=-1, keepdims=True)
    centred = field - mean
    spread = jnp.mean(centred * centred, axis=-1, keepdims=True)
    return centred * lax.rsqrt(spread + eps)


def modulate(field, shift, scale):
    return layer_norm(field) * (1.0 + scale) + shift


def head_norm(field, gain):
    height, width = field.shape
    shaped = field.reshape(height, width // HDIM, HDIM)
    power = jnp.mean(shaped * shaped, axis=-1, keepdims=True)
    return (shaped * lax.rsqrt(power + eps) * gain).reshape(height, width)


def attend(queries, keys, values, valid):
    height, width = queries.shape
    heads = width // HDIM
    scores = jnp.einsum(
        "qhd,khd->qhk",
        queries.reshape(height, heads, HDIM),
        keys.reshape(-1, heads, HDIM),
        preferred_element_type=jnp.float32,
    ) * HDIM ** (-0.5)
    scores = jnp.where(valid[None, None, :], scores, masked_score)
    highest = jnp.max(scores, axis=-1, keepdims=True)
    expo = jnp.where(valid[None, None, :], jnp.exp(scores - highest), 0.0)
    total = jnp.sum(expo, axis=-1)
    mixed = jnp.einsum(
        "qhk,khd->qhd",
        expo.astype(jnp.bfloat16),
        values.reshape(-1, heads, HDIM),
        preferred_element_type=jnp.float32,
    )
    return (mixed / total[..., None]).reshape(height, width).astype(jnp.bfloat16)


def cols_to_rows(cols):
    got = lax.all_to_all(cols, TOK, split_axis=0, concat_axis=0, tiled=True)
    count, rows, width = got.shape
    return jnp.transpose(got, (1, 0, 2)).reshape(rows, count * width)


def broadcast_rows(block, devices):
    copies = jnp.broadcast_to(block[None], (devices,) + block.shape)
    got = lax.all_to_all(copies, TOK, split_axis=0, concat_axis=0, tiled=True)
    return got.reshape(-1, block.shape[-1])


def shards(
    image_in,
    text_in,
    text_length,
    entry_order,
    step_index,
    image_modulation,
    text_modulation,
    image_to_heads,
    text_to_heads,
    head_gain,
    image_from_heads,
    text_from_heads,
    image_up,
    image_down,
    stale_cache,
    final_modulation,
    final_weight,
    latents,
):
    section = lax.axis_index("section")
    last_section = lax.axis_size("section") - 1
    position = lax.axis_index("ta") * lax.axis_size("tb") + lax.axis_index("tb")
    devices = lax.axis_size("ta") * lax.axis_size("tb")
    image_x = image_in[0, 0].astype(jnp.float32)
    text_x = text_in[0, 0].astype(jnp.float32)
    image_rows = image_x.shape[0]
    text_rows = text_x.shape[0]
    width = image_x.shape[1]
    patch = lax.dynamic_index_in_dim(entry_order[0], section, 0, False)
    step_now = lax.dynamic_index_in_dim(step_index[0], patch, 0, False)
    modul = (
        lax.dynamic_index_in_dim(image_modulation[0], step_now, 0, False)
        .astype(jnp.float32)
        .reshape(6, width)
    )
    text_mod = (
        lax.dynamic_index_in_dim(text_modulation[0], step_now, 0, False)
        .astype(jnp.float32)
        .reshape(3, width)
    )
    image_normed = modulate(image_x, modul[0], modul[1]).astype(jnp.bfloat16)
    text_normed = modulate(text_x, text_mod[0], text_mod[1]).astype(jnp.bfloat16)
    stale = stale_cache[0, 0]
    cache_rows = stale.shape[0]
    heads = width // HDIM

    def by_head(pieces):
        pack = jnp.concatenate(
            [piece.reshape(piece.shape[0], heads, HDIM) for piece in pieces], axis=0
        )
        pack = jnp.transpose(pack, (1, 0, 2))
        pack = jnp.pad(pack, ((0, devices - heads), (0, 0), (0, 0)))
        return lax.all_to_all(pack, TOK, split_axis=0, concat_axis=0, tiled=True)

    got_cache = by_head([stale[:, :width], stale[:, width:]])
    got_cache, image_normed, text_normed = lax.optimization_barrier(
        (got_cache, image_normed, text_normed)
    )
    every = lax.all_gather(
        jnp.concatenate([image_normed, text_normed], axis=0), TOK, axis=0, tiled=False
    )
    image_cols = jnp.dot(
        every[:, :image_rows].reshape(-1, width), image_to_heads[0], preferred_element_type=jnp.float32
    ).astype(jnp.bfloat16)
    text_cols = jnp.dot(
        every[:, image_rows:].reshape(-1, width), text_to_heads[0], preferred_element_type=jnp.float32
    ).astype(jnp.bfloat16)
    proj = cols_to_rows(
        jnp.concatenate(
            [
                image_cols.reshape(devices, image_rows, -1),
                text_cols.reshape(devices, text_rows, -1),
            ],
            axis=1,
        )
    )
    image_proj = proj[:image_rows]
    text_proj = proj[image_rows:]
    gains = head_gain[0]
    image_query = head_norm(image_proj[:, :width].astype(jnp.float32), gains[0]).astype(
        jnp.bfloat16
    )
    image_key = head_norm(image_proj[:, width : 2 * width].astype(jnp.float32), gains[1]).astype(
        jnp.bfloat16
    )
    text_query = head_norm(text_proj[:, :width].astype(jnp.float32), gains[2]).astype(jnp.bfloat16)
    text_key = head_norm(text_proj[:, width : 2 * width].astype(jnp.float32), gains[3]).astype(
        jnp.bfloat16
    )
    image_value = image_proj[:, 2 * width :]
    text_value = text_proj[:, 2 * width :]
    fresh_image = jnp.concatenate([image_key, image_value], axis=1)
    patch_len = image_rows * devices
    per_patch = patch_len // cache_rows
    row_q = jnp.concatenate([image_query, text_query], axis=0)
    row_k = jnp.concatenate([image_key, text_key], axis=0)
    row_v = jnp.concatenate([image_value, text_value], axis=0)
    got = by_head([row_q, row_k, row_v])
    rows = image_rows + text_rows

    def part(first, count, source=got):
        return source[:, first : first + count].reshape(-1, HDIM)

    queries = jnp.concatenate([part(0, image_rows), part(image_rows, text_rows)], axis=0)
    fresh_k = part(rows, image_rows)
    text_k = part(rows + image_rows, text_rows)
    fresh_v = part(2 * rows, image_rows)
    text_v = part(2 * rows + image_rows, text_rows)
    cache_k = part(0, cache_rows, got_cache)
    cache_v = part(cache_rows, cache_rows, got_cache)
    begin = patch * patch_len
    cache_k = lax.dynamic_update_slice_in_dim(cache_k, fresh_k, begin, 0)
    cache_v = lax.dynamic_update_slice_in_dim(cache_v, fresh_v, begin, 0)
    keys = jnp.concatenate([cache_k, text_k], axis=0)
    values = jnp.concatenate([cache_v, text_v], axis=0)
    text_count = text_length[0]
    valid = jnp.concatenate(
        [
            jnp.ones((cache_k.shape[0],), bool),
            jnp.arange(text_k.shape[0], dtype=jnp.int32) < text_count,
        ]
    )
    head_out = attend(queries, keys, values, valid)
    image_heads = broadcast_rows(head_out[:patch_len], devices).reshape(devices, patch_len, HDIM)
    riders = fresh_image.reshape(-1, HDIM)
    text_heads = lax.all_gather(
        jnp.concatenate([head_out[patch_len:], riders], axis=0), TOK, axis=0, tiled=False
    )
    text_len = head_out.shape[0] - patch_len
    fresh_all = text_heads[:, text_len:].reshape(patch_len, -1)
    text_heads = text_heads[:, :text_len]
    moved = lax.dynamic_slice_in_dim(
        fresh_all, (position % per_patch) * cache_rows, cache_rows, 0
    )
    current = jnp.where(position // per_patch == patch, moved, stale)
    image_att = jnp.transpose(image_heads[:heads], (1, 0, 2)).reshape(-1, width)
    text_att = jnp.transpose(text_heads[:heads], (1, 0, 2)).reshape(-1, width)
    image_back = cols_to_rows(
        jnp.dot(image_att, image_from_heads[0], preferred_element_type=jnp.float32)
        .astype(jnp.bfloat16)
        .reshape(devices, image_rows, -1)
    )
    text_back = cols_to_rows(
        jnp.dot(text_att, text_from_heads[0], preferred_element_type=jnp.float32)
        .astype(jnp.bfloat16)
        .reshape(devices, text_rows, -1)
    )
    image_mid = image_x + modul[2] * image_back.astype(jnp.float32)
    text_out = (text_x + text_mod[2] * text_back.astype(jnp.float32)).astype(jnp.bfloat16)
    mlp_normed = modulate(image_mid, modul[3], modul[4]).astype(jnp.bfloat16)
    up_weight = image_up[0]
    down_weight = image_down[0]
    hidden = jax.nn.gelu(
        jnp.dot(
            broadcast_rows(mlp_normed, devices),
            up_weight,
            preferred_element_type=jnp.float32,
        ),
        approximate=True,
    ).astype(jnp.bfloat16)
    partial = jnp.dot(hidden, down_weight, preferred_element_type=jnp.float32)
    reduced = jnp.sum(
        lax.all_to_all(
            partial.astype(jnp.bfloat16).reshape(devices, image_rows, width),
            TOK,
            split_axis=0,
            concat_axis=0,
            tiled=True,
        ).astype(jnp.float32),
        axis=0,
    )
    image_out = (image_mid + modul[5] * reduced).astype(jnp.bfloat16)
    text_next = from_behind(text_out, "section", 1)
    image_next = from_behind(image_out, "section", 1)
    final_source = jnp.where(section == last_section, image_out, image_next)
    patch_last = entry_order[0, last_section]
    step_last = lax.dynamic_index_in_dim(step_index[0], patch_last, 0, False)
    final_mod = (
        lax.dynamic_index_in_dim(final_modulation, step_last, 0, False)
        .astype(jnp.float32)
        .reshape(2, width)
    )
    normed = modulate(final_source.astype(jnp.float32), final_mod[0], final_mod[1]).astype(
        jnp.bfloat16
    )
    velocity = jnp.dot(normed, final_weight, preferred_element_type=jnp.float32)
    latents_next = latents[0] + -1.0 / TSTEPS * velocity
    return (image_next[None, None], text_next[None, None], current[None, None], latents_next[None])


def solution(mesh):
    shape = mesh.devices.shape
    split = jax.sharding.Mesh(
        mesh.devices.reshape(shape[:2] + (shape[2] // QUAD, QUAD)),
        ("section", "grp", "ta", "tb"),
    )
    placed = (
        P("section", "grp", TOK, None),
        P("section", "grp", TOK, None),
        P("grp"),
        P("grp", None),
        P("grp", None),
        P("section", None, None),
        P("section", None, None),
        P("section", None, TOK),
        P("section", None, TOK),
        P("section", None, None),
        P("section", None, TOK),
        P("section", None, TOK),
        P("section", None, TOK),
        P("section", TOK, None),
        P("section", "grp", TOK, None),
        P(),
        P(None, "section"),
        P("grp", TOK, "section"),
    )
    return jax.shard_map(
        shards,
        mesh=split,
        in_specs=placed,
        out_specs=(
            P("section", "grp", TOK, None),
            P("section", "grp", TOK, None),
            P("section", "grp", TOK, None),
            P("grp", TOK, "section"),
        ),
        check_vma=False,
    )
```

```python
import jax
import jax.numpy as jnp
from jax import lax
from jax.sharding import PartitionSpec as P

HDIM = 128
TSTEPS = 4


TOK = ("ta", "tb")
QUAD = 4

eps = 1e-06
masked_score = -1e30


def from_behind(block, axis, distance):
    devices = range(lax.axis_size(axis))
    route = [((i - distance) % len(devices), i) for i in devices]
    return lax.ppermute(block, axis, route)


def layer_norm(field):
    mean = jnp.mean(field, axis=-1, keepdims=True)
    centred = field - mean
    spread = jnp.mean(centred * centred, axis=-1, keepdims=True)
    return centred * lax.rsqrt(spread + eps)


def modulate(field, shift, scale):
    return layer_norm(field) * (1.0 + scale) + shift


def head_norm(field, gain):
    height, width = field.shape
    shaped = field.reshape(height, width // HDIM, HDIM)
    power = jnp.mean(shaped * shaped, axis=-1, keepdims=True)
    return (shaped * lax.rsqrt(power + eps) * gain).reshape(height, width)


def attend(queries, keys, values, valid):
    height, width = queries.shape
    heads = width // HDIM
    scores = jnp.einsum(
        "qhd,khd->qhk",
        queries.reshape(height, heads, HDIM),
        keys.reshape(-1, heads, HDIM),
        preferred_element_type=jnp.float32,
    ) * HDIM ** (-0.5)
    scores = jnp.where(valid[None, None, :], scores, masked_score)
    highest = jnp.max(scores, axis=-1, keepdims=True)
    expo = jnp.where(valid[None, None, :], jnp.exp(scores - highest), 0.0)
    total = jnp.sum(expo, axis=-1)
    mixed = jnp.einsum(
        "qhk,khd->qhd",
        expo.astype(jnp.bfloat16),
        values.reshape(-1, heads, HDIM),
        preferred_element_type=jnp.float32,
    )
    return (mixed / total[..., None]).reshape(height, width).astype(jnp.bfloat16)


def attend_columns(queries, keys, values, valid):
    scores = jnp.dot(queries, keys.T, preferred_element_type=jnp.float32) * HDIM ** (-0.5)
    scores = jnp.where(valid[None, :], scores, masked_score)
    highest = jnp.max(scores, axis=-1, keepdims=True)
    expo = jnp.where(valid[None, :], jnp.exp(scores - highest), 0.0)
    total = jnp.sum(expo, axis=-1, keepdims=True)
    mixed = jnp.dot(expo.astype(jnp.bfloat16), values, preferred_element_type=jnp.float32)
    return mixed / total


def cols_to_rows(cols):
    got = lax.all_to_all(cols, TOK, split_axis=0, concat_axis=0, tiled=True)
    count, rows, width = got.shape
    return jnp.transpose(got, (1, 0, 2)).reshape(rows, count * width)


def broadcast_rows(block, devices):
    copies = jnp.broadcast_to(block[None], (devices,) + block.shape)
    got = lax.all_to_all(copies, TOK, split_axis=0, concat_axis=0, tiled=True)
    return got.reshape(-1, block.shape[-1])


def shards(
    image_in,
    text_in,
    text_length,
    entry_order,
    step_index,
    image_modulation,
    text_modulation,
    image_to_heads,
    text_to_heads,
    head_gain,
    image_from_heads,
    text_from_heads,
    image_up,
    image_down,
    stale_cache,
    final_modulation,
    final_weight,
    latents,
):
    section = lax.axis_index("section")
    last_section = lax.axis_size("section") - 1
    position = lax.axis_index("ta") * lax.axis_size("tb") + lax.axis_index("tb")
    devices = lax.axis_size("ta") * lax.axis_size("tb")
    image_x = image_in[0, 0].astype(jnp.float32)
    text_x = text_in[0, 0].astype(jnp.float32)
    image_rows = image_x.shape[0]
    text_rows = text_x.shape[0]
    width = image_x.shape[1]
    patch = lax.dynamic_index_in_dim(entry_order[0], section, 0, False)
    step_now = lax.dynamic_index_in_dim(step_index[0], patch, 0, False)
    modul = (
        lax.dynamic_index_in_dim(image_modulation[0], step_now, 0, False)
        .astype(jnp.float32)
        .reshape(6, width)
    )
    text_mod = (
        lax.dynamic_index_in_dim(text_modulation[0], step_now, 0, False)
        .astype(jnp.float32)
        .reshape(3, width)
    )
    image_normed = modulate(image_x, modul[0], modul[1]).astype(jnp.bfloat16)
    text_normed = modulate(text_x, text_mod[0], text_mod[1]).astype(jnp.bfloat16)
    stale = stale_cache[0, 0]
    cache_rows = stale.shape[0]
    heads = width // HDIM

    span = width // devices
    first = [span * t // HDIM for t in range(devices)]
    second = [(span * t + span - 1) // HDIM for t in range(devices)]

    def by_columns(head_pieces, column_pieces):
        parts = []
        for piece in head_pieces:
            shaped = piece.reshape(piece.shape[0], heads, HDIM)
            parts += [shaped[:, jnp.array(first)], shaped[:, jnp.array(second)]]
        parts += [piece.reshape(piece.shape[0], devices, span) for piece in column_pieces]
        pack = jnp.transpose(jnp.concatenate(parts, axis=-1), (1, 0, 2))
        return lax.all_to_all(pack, TOK, split_axis=0, concat_axis=0, tiled=True)

    got_cache = by_columns([stale[:, :width]], [stale[:, width:]])
    got_cache, image_normed, text_normed = lax.optimization_barrier(
        (got_cache, image_normed, text_normed)
    )
    every = lax.all_gather(
        jnp.concatenate([image_normed, text_normed], axis=0), TOK, axis=0, tiled=False
    )
    image_cols = jnp.dot(
        every[:, :image_rows].reshape(-1, width), image_to_heads[0], preferred_element_type=jnp.float32
    ).astype(jnp.bfloat16)
    text_cols = jnp.dot(
        every[:, image_rows:].reshape(-1, width), text_to_heads[0], preferred_element_type=jnp.float32
    ).astype(jnp.bfloat16)
    proj = cols_to_rows(
        jnp.concatenate(
            [
                image_cols.reshape(devices, image_rows, -1),
                text_cols.reshape(devices, text_rows, -1),
            ],
            axis=1,
        )
    )
    image_proj = proj[:image_rows]
    text_proj = proj[image_rows:]
    gains = head_gain[0]
    image_query = head_norm(image_proj[:, :width].astype(jnp.float32), gains[0]).astype(
        jnp.bfloat16
    )
    image_key = head_norm(image_proj[:, width : 2 * width].astype(jnp.float32), gains[1]).astype(
        jnp.bfloat16
    )
    text_query = head_norm(text_proj[:, :width].astype(jnp.float32), gains[2]).astype(jnp.bfloat16)
    text_key = head_norm(text_proj[:, width : 2 * width].astype(jnp.float32), gains[3]).astype(
        jnp.bfloat16
    )
    image_value = image_proj[:, 2 * width :]
    text_value = text_proj[:, 2 * width :]
    fresh_image = jnp.concatenate([image_key, image_value], axis=1)
    patch_len = image_rows * devices
    per_patch = patch_len // cache_rows
    row_q = jnp.concatenate([image_query, text_query], axis=0)
    row_k = jnp.concatenate([image_key, text_key], axis=0)
    row_v = jnp.concatenate([image_value, text_value], axis=0)
    got = by_columns([row_q, row_k], [row_v])

    def part(source, first_col, count, first_row, row_count):
        block = source[:, first_row : first_row + row_count, first_col : first_col + count]
        return block.reshape(-1, count)

    def rows_of(first_col, count):
        return (
            part(got, first_col, count, 0, image_rows),
            part(got, first_col, count, image_rows, text_rows),
        )

    begin = patch * patch_len
    text_count = text_length[0]
    cache_len = cache_rows * devices
    valid = jnp.concatenate(
        [
            jnp.ones((cache_len,), bool),
            jnp.arange(text_rows * devices, dtype=jnp.int32) < text_count,
        ]
    )

    def keys_of(first_col, count, cache_col):
        fresh, text = rows_of(first_col, count)
        cache = part(got_cache, cache_col, count, 0, cache_rows)
        cache = lax.dynamic_update_slice_in_dim(cache, fresh, begin, 0)
        return jnp.concatenate([cache, text], axis=0)

    values = keys_of(4 * HDIM, span, 2 * HDIM)
    mixed = []
    for which in range(2):
        queries = jnp.concatenate(rows_of(which * HDIM, HDIM), axis=0)
        keys = keys_of(2 * HDIM + which * HDIM, HDIM, which * HDIM)
        mixed.append(attend_columns(queries, keys, values, valid))
    split = jnp.minimum(span, HDIM * (span * position // HDIM + 1) - span * position)
    head_out = jnp.where(jnp.arange(span) < split, mixed[0], mixed[1]).astype(jnp.bfloat16)
    image_heads = broadcast_rows(head_out[:patch_len], devices).reshape(devices, patch_len, span)
    riders = fresh_image.reshape(-1, span)
    text_heads = lax.all_gather(
        jnp.concatenate([head_out[patch_len:], riders], axis=0), TOK, axis=0, tiled=False
    )
    text_len = head_out.shape[0] - patch_len
    fresh_all = text_heads[:, text_len:].reshape(patch_len, -1)
    text_heads = text_heads[:, :text_len]
    moved = lax.dynamic_slice_in_dim(
        fresh_all, (position % per_patch) * cache_rows, cache_rows, 0
    )
    current = jnp.where(position // per_patch == patch, moved, stale)
    image_att = jnp.transpose(image_heads, (1, 0, 2)).reshape(-1, width)
    text_att = jnp.transpose(text_heads, (1, 0, 2)).reshape(-1, width)
    image_back = cols_to_rows(
        jnp.dot(image_att, image_from_heads[0], preferred_element_type=jnp.float32)
        .astype(jnp.bfloat16)
        .reshape(devices, image_rows, -1)
    )
    text_back = cols_to_rows(
        jnp.dot(text_att, text_from_heads[0], preferred_element_type=jnp.float32)
        .astype(jnp.bfloat16)
        .reshape(devices, text_rows, -1)
    )
    image_mid = image_x + modul[2] * image_back.astype(jnp.float32)
    text_out = (text_x + text_mod[2] * text_back.astype(jnp.float32)).astype(jnp.bfloat16)
    mlp_normed = modulate(image_mid, modul[3], modul[4]).astype(jnp.bfloat16)
    up_weight = image_up[0]
    down_weight = image_down[0]
    hidden = jax.nn.gelu(
        jnp.dot(
            broadcast_rows(mlp_normed, devices),
            up_weight,
            preferred_element_type=jnp.float32,
        ),
        approximate=True,
    ).astype(jnp.bfloat16)
    partial = jnp.dot(hidden, down_weight, preferred_element_type=jnp.float32)
    reduced = jnp.sum(
        lax.all_to_all(
            partial.astype(jnp.bfloat16).reshape(devices, image_rows, width),
            TOK,
            split_axis=0,
            concat_axis=0,
            tiled=True,
        ).astype(jnp.float32),
        axis=0,
    )
    image_out = (image_mid + modul[5] * reduced).astype(jnp.bfloat16)
    text_next = from_behind(text_out, "section", 1)
    image_next = from_behind(image_out, "section", 1)
    final_source = jnp.where(section == last_section, image_out, image_next)
    patch_last = entry_order[0, last_section]
    step_last = lax.dynamic_index_in_dim(step_index[0], patch_last, 0, False)
    final_mod = (
        lax.dynamic_index_in_dim(final_modulation, step_last, 0, False)
        .astype(jnp.float32)
        .reshape(2, width)
    )
    normed = modulate(final_source.astype(jnp.float32), final_mod[0], final_mod[1]).astype(
        jnp.bfloat16
    )
    velocity = jnp.dot(normed, final_weight, preferred_element_type=jnp.float32)
    latents_next = latents[0] + -1.0 / TSTEPS * velocity
    return (image_next[None, None], text_next[None, None], current[None, None], latents_next[None])


def solution(mesh):
    shape = mesh.devices.shape
    split = jax.sharding.Mesh(
        mesh.devices.reshape(shape[:2] + (shape[2] // QUAD, QUAD)),
        ("section", "grp", "ta", "tb"),
    )
    placed = (
        P("section", "grp", TOK, None),
        P("section", "grp", TOK, None),
        P("grp"),
        P("grp", None),
        P("grp", None),
        P("section", None, None),
        P("section", None, None),
        P("section", None, TOK),
        P("section", None, TOK),
        P("section", None, None),
        P("section", None, TOK),
        P("section", None, TOK),
        P("section", None, TOK),
        P("section", TOK, None),
        P("section", "grp", TOK, None),
        P(),
        P(None, "section"),
        P("grp", TOK, "section"),
    )
    return jax.shard_map(
        shards,
        mesh=split,
        in_specs=placed,
        out_specs=(
            P("section", "grp", TOK, None),
            P("section", "grp", TOK, None),
            P("section", "grp", TOK, None),
            P("grp", TOK, "section"),
        ),
        check_vma=False,
    )
```

```python
import jax
import jax.numpy as jnp
from jax import lax
from jax.sharding import PartitionSpec as P

HDIM = 128
TSTEPS = 4


TOK = ("ta", "tb")
QUAD = 4

eps = 1e-06
masked_score = -1e30


def from_behind(block, axis, distance):
    devices = range(lax.axis_size(axis))
    route = [((i - distance) % len(devices), i) for i in devices]
    return lax.ppermute(block, axis, route)


def layer_norm(field):
    mean = jnp.mean(field, axis=-1, keepdims=True)
    centred = field - mean
    spread = jnp.mean(centred * centred, axis=-1, keepdims=True)
    return centred * lax.rsqrt(spread + eps)


def modulate(field, shift, scale):
    return layer_norm(field) * (1.0 + scale) + shift


def head_norm(field, gain):
    height, width = field.shape
    shaped = field.reshape(height, width // HDIM, HDIM)
    power = jnp.mean(shaped * shaped, axis=-1, keepdims=True)
    return (shaped * lax.rsqrt(power + eps) * gain).reshape(height, width)


def attend(queries, keys, values, valid):
    height, width = queries.shape
    heads = width // HDIM
    scores = jnp.einsum(
        "qhd,khd->qhk",
        queries.reshape(height, heads, HDIM),
        keys.reshape(-1, heads, HDIM),
        preferred_element_type=jnp.float32,
    ) * HDIM ** (-0.5)
    scores = jnp.where(valid[None, None, :], scores, masked_score)
    highest = jnp.max(scores, axis=-1, keepdims=True)
    expo = jnp.where(valid[None, None, :], jnp.exp(scores - highest), 0.0)
    total = jnp.sum(expo, axis=-1)
    mixed = jnp.einsum(
        "qhk,khd->qhd",
        expo.astype(jnp.bfloat16),
        values.reshape(-1, heads, HDIM),
        preferred_element_type=jnp.float32,
    )
    return (mixed / total[..., None]).reshape(height, width).astype(jnp.bfloat16)


def cols_to_rows(cols):
    got = lax.all_to_all(cols, TOK, split_axis=0, concat_axis=0, tiled=True)
    count, rows, width = got.shape
    return jnp.transpose(got, (1, 0, 2)).reshape(rows, count * width)


def broadcast_rows(block, devices):
    copies = jnp.broadcast_to(block[None], (devices,) + block.shape)
    got = lax.all_to_all(copies, TOK, split_axis=0, concat_axis=0, tiled=True)
    return got.reshape(-1, block.shape[-1])


def shards(
    image_in,
    text_in,
    text_length,
    entry_order,
    step_index,
    image_modulation,
    text_modulation,
    image_to_heads,
    text_to_heads,
    head_gain,
    image_from_heads,
    text_from_heads,
    image_up,
    image_down,
    stale_cache,
    final_modulation,
    final_weight,
    latents,
):
    section = lax.axis_index("section")
    last_section = lax.axis_size("section") - 1
    position = lax.axis_index("ta") * lax.axis_size("tb") + lax.axis_index("tb")
    devices = lax.axis_size("ta") * lax.axis_size("tb")
    image_x = image_in[0, 0].astype(jnp.float32)
    text_x = text_in[0, 0].astype(jnp.float32)
    image_rows = image_x.shape[0]
    text_rows = text_x.shape[0]
    width = image_x.shape[1]
    patch = lax.dynamic_index_in_dim(entry_order[0], section, 0, False)
    step_now = lax.dynamic_index_in_dim(step_index[0], patch, 0, False)
    modul = (
        lax.dynamic_index_in_dim(image_modulation[0], step_now, 0, False)
        .astype(jnp.float32)
        .reshape(6, width)
    )
    text_mod = (
        lax.dynamic_index_in_dim(text_modulation[0], step_now, 0, False)
        .astype(jnp.float32)
        .reshape(3, width)
    )
    image_normed = modulate(image_x, modul[0], modul[1]).astype(jnp.bfloat16)
    text_normed = modulate(text_x, text_mod[0], text_mod[1]).astype(jnp.bfloat16)
    stale = stale_cache[0, 0]
    cache_rows = stale.shape[0]
    heads = width // HDIM

    def by_head(pieces):
        pack = jnp.concatenate(
            [piece.reshape(piece.shape[0], heads, HDIM) for piece in pieces], axis=0
        )
        pack = jnp.transpose(pack, (1, 0, 2))
        pack = jnp.pad(pack, ((0, devices - heads), (0, 0), (0, 0)))
        return lax.all_to_all(pack, TOK, split_axis=0, concat_axis=0, tiled=True)

    got_cache = by_head([stale[:, :width], stale[:, width:]])
    got_cache, image_normed, text_normed = lax.optimization_barrier(
        (got_cache, image_normed, text_normed)
    )
    every = lax.all_gather(
        jnp.concatenate([image_normed, text_normed], axis=0), TOK, axis=0, tiled=False
    )
    image_cols = jnp.dot(
        every[:, :image_rows].reshape(-1, width), image_to_heads[0], preferred_element_type=jnp.float32
    ).astype(jnp.bfloat16)
    text_cols = jnp.dot(
        every[:, image_rows:].reshape(-1, width), text_to_heads[0], preferred_element_type=jnp.float32
    ).astype(jnp.bfloat16)
    proj = cols_to_rows(
        jnp.concatenate(
            [
                image_cols.reshape(devices, image_rows, -1),
                text_cols.reshape(devices, text_rows, -1),
            ],
            axis=1,
        )
    )
    image_proj = proj[:image_rows]
    text_proj = proj[image_rows:]
    gains = head_gain[0]
    image_query = head_norm(image_proj[:, :width].astype(jnp.float32), gains[0]).astype(
        jnp.bfloat16
    )
    image_key = head_norm(image_proj[:, width : 2 * width].astype(jnp.float32), gains[1]).astype(
        jnp.bfloat16
    )
    text_query = head_norm(text_proj[:, :width].astype(jnp.float32), gains[2]).astype(jnp.bfloat16)
    text_key = head_norm(text_proj[:, width : 2 * width].astype(jnp.float32), gains[3]).astype(
        jnp.bfloat16
    )
    image_value = image_proj[:, 2 * width :]
    text_value = text_proj[:, 2 * width :]
    fresh_image = jnp.concatenate([image_key, image_value], axis=1)
    patch_len = image_rows * devices
    per_patch = patch_len // cache_rows
    row_q = jnp.concatenate([image_query, text_query], axis=0)
    row_k = jnp.concatenate([image_key, text_key], axis=0)
    row_v = jnp.concatenate([image_value, text_value], axis=0)
    got = by_head([row_q, row_k, row_v])
    rows = image_rows + text_rows

    def part(first, count, source=got):
        return source[:, first : first + count].reshape(-1, HDIM)

    queries = jnp.concatenate([part(0, image_rows), part(image_rows, text_rows)], axis=0)
    fresh_k = part(rows, image_rows)
    text_k = part(rows + image_rows, text_rows)
    fresh_v = part(2 * rows, image_rows)
    text_v = part(2 * rows + image_rows, text_rows)
    cache_k = part(0, cache_rows, got_cache)
    cache_v = part(cache_rows, cache_rows, got_cache)
    begin = patch * patch_len
    cache_k = lax.dynamic_update_slice_in_dim(cache_k, fresh_k, begin, 0)
    cache_v = lax.dynamic_update_slice_in_dim(cache_v, fresh_v, begin, 0)
    keys = jnp.concatenate([cache_k, text_k], axis=0)
    values = jnp.concatenate([cache_v, text_v], axis=0)
    text_count = text_length[0]
    valid = jnp.concatenate(
        [
            jnp.ones((cache_k.shape[0],), bool),
            jnp.arange(text_k.shape[0], dtype=jnp.int32) < text_count,
        ]
    )
    head_out = attend(queries, keys, values, valid)
    image_heads = broadcast_rows(head_out[:patch_len], devices).reshape(devices, patch_len, HDIM)
    riders = fresh_image.reshape(-1, HDIM)
    text_heads = lax.all_gather(
        jnp.concatenate([head_out[patch_len:], riders], axis=0), TOK, axis=0, tiled=False
    )
    text_len = head_out.shape[0] - patch_len
    fresh_all = text_heads[:, text_len:].reshape(patch_len, -1)
    text_heads = text_heads[:, :text_len]
    moved = lax.dynamic_slice_in_dim(
        fresh_all, (position % per_patch) * cache_rows, cache_rows, 0
    )
    current = jnp.where(position // per_patch == patch, moved, stale)
    image_att = jnp.transpose(image_heads[:heads], (1, 0, 2)).reshape(-1, width)
    text_att = jnp.transpose(text_heads[:heads], (1, 0, 2)).reshape(-1, width)
    image_back = cols_to_rows(
        jnp.dot(image_att, image_from_heads[0], preferred_element_type=jnp.float32)
        .astype(jnp.bfloat16)
        .reshape(devices, image_rows, -1)
    )
    text_back = cols_to_rows(
        jnp.dot(text_att, text_from_heads[0], preferred_element_type=jnp.float32)
        .astype(jnp.bfloat16)
        .reshape(devices, text_rows, -1)
    )
    image_mid = image_x + modul[2] * image_back.astype(jnp.float32)
    text_out = (text_x + text_mod[2] * text_back.astype(jnp.float32)).astype(jnp.bfloat16)
    mlp_normed = modulate(image_mid, modul[3], modul[4]).astype(jnp.bfloat16)
    up_weight = image_up[0]
    down_weight = image_down[0]
    hidden = jax.nn.gelu(
        jnp.dot(
            broadcast_rows(mlp_normed, devices),
            up_weight,
            preferred_element_type=jnp.float32,
        ),
        approximate=True,
    ).astype(jnp.bfloat16)
    partial = jnp.dot(hidden, down_weight, preferred_element_type=jnp.float32)
    partial, text_back = lax.optimization_barrier((partial, text_back))
    reduced = jnp.sum(
        lax.all_to_all(
            partial.astype(jnp.bfloat16).reshape(devices, image_rows, width),
            TOK,
            split_axis=0,
            concat_axis=0,
            tiled=True,
        ).astype(jnp.float32),
        axis=0,
    )
    image_out = (image_mid + modul[5] * reduced).astype(jnp.bfloat16)
    text_next = from_behind(text_out, "section", 1)
    image_next = from_behind(image_out, "section", 1)
    final_source = jnp.where(section == last_section, image_out, image_next)
    patch_last = entry_order[0, last_section]
    step_last = lax.dynamic_index_in_dim(step_index[0], patch_last, 0, False)
    final_mod = (
        lax.dynamic_index_in_dim(final_modulation, step_last, 0, False)
        .astype(jnp.float32)
        .reshape(2, width)
    )
    normed = modulate(final_source.astype(jnp.float32), final_mod[0], final_mod[1]).astype(
        jnp.bfloat16
    )
    velocity = jnp.dot(normed, final_weight, preferred_element_type=jnp.float32)
    latents_next = latents[0] + -1.0 / TSTEPS * velocity
    return (image_next[None, None], text_next[None, None], current[None, None], latents_next[None])


def solution(mesh):
    shape = mesh.devices.shape
    split = jax.sharding.Mesh(
        mesh.devices.reshape(shape[:2] + (shape[2] // QUAD, QUAD)),
        ("section", "grp", "ta", "tb"),
    )
    placed = (
        P("section", "grp", TOK, None),
        P("section", "grp", TOK, None),
        P("grp"),
        P("grp", None),
        P("grp", None),
        P("section", None, None),
        P("section", None, None),
        P("section", None, TOK),
        P("section", None, TOK),
        P("section", None, None),
        P("section", None, TOK),
        P("section", None, TOK),
        P("section", None, TOK),
        P("section", TOK, None),
        P("section", "grp", TOK, None),
        P(),
        P(None, "section"),
        P("grp", TOK, "section"),
    )
    return jax.shard_map(
        shards,
        mesh=split,
        in_specs=placed,
        out_specs=(
            P("section", "grp", TOK, None),
            P("section", "grp", TOK, None),
            P("section", "grp", TOK, None),
            P("grp", TOK, "section"),
        ),
        check_vma=False,
    )
```

```python
import jax
import jax.numpy as jnp
from jax import lax
from jax.sharding import PartitionSpec as P

HDIM = 128
TSTEPS = 4


TOK = ("ta", "tb")
QUAD = 4

eps = 1e-06
masked_score = -1e30


def from_behind(block, axis, distance):
    devices = range(lax.axis_size(axis))
    route = [((i - distance) % len(devices), i) for i in devices]
    return lax.ppermute(block, axis, route)


def layer_norm(field):
    mean = jnp.mean(field, axis=-1, keepdims=True)
    centred = field - mean
    spread = jnp.mean(centred * centred, axis=-1, keepdims=True)
    return centred * lax.rsqrt(spread + eps)


def modulate(field, shift, scale):
    return layer_norm(field) * (1.0 + scale) + shift


def head_norm(field, gain):
    height, width = field.shape
    shaped = field.reshape(height, width // HDIM, HDIM)
    power = jnp.mean(shaped * shaped, axis=-1, keepdims=True)
    return (shaped * lax.rsqrt(power + eps) * gain).reshape(height, width)


def attend(queries, keys, values, valid):
    height, width = queries.shape
    heads = width // HDIM
    scores = jnp.einsum(
        "qhd,khd->qhk",
        queries.reshape(height, heads, HDIM),
        keys.reshape(-1, heads, HDIM),
        preferred_element_type=jnp.float32,
    ) * HDIM ** (-0.5)
    scores = jnp.where(valid[None, None, :], scores, masked_score)
    highest = jnp.max(scores, axis=-1, keepdims=True)
    expo = jnp.where(valid[None, None, :], jnp.exp(scores - highest), 0.0)
    total = jnp.sum(expo, axis=-1)
    mixed = jnp.einsum(
        "qhk,khd->qhd",
        expo.astype(jnp.bfloat16),
        values.reshape(-1, heads, HDIM),
        preferred_element_type=jnp.float32,
    )
    return (mixed / total[..., None]).reshape(height, width).astype(jnp.bfloat16)


def cols_to_rows(cols):
    got = lax.all_to_all(cols, TOK, split_axis=0, concat_axis=0, tiled=True)
    count, rows, width = got.shape
    return jnp.transpose(got, (1, 0, 2)).reshape(rows, count * width)


def broadcast_rows(block, devices):
    copies = jnp.broadcast_to(block[None], (devices,) + block.shape)
    got = lax.all_to_all(copies, TOK, split_axis=0, concat_axis=0, tiled=True)
    return got.reshape(-1, block.shape[-1])


def shards(
    image_in,
    text_in,
    text_length,
    entry_order,
    step_index,
    image_modulation,
    text_modulation,
    image_to_heads,
    text_to_heads,
    head_gain,
    image_from_heads,
    text_from_heads,
    image_up,
    image_down,
    stale_cache,
    final_modulation,
    final_weight,
    latents,
):
    section = lax.axis_index("section")
    last_section = lax.axis_size("section") - 1
    position = lax.axis_index("ta") * lax.axis_size("tb") + lax.axis_index("tb")
    devices = lax.axis_size("ta") * lax.axis_size("tb")
    image_x = image_in[0, 0].astype(jnp.float32)
    text_x = text_in[0, 0].astype(jnp.float32)
    image_rows = image_x.shape[0]
    text_rows = text_x.shape[0]
    width = image_x.shape[1]
    patch = lax.dynamic_index_in_dim(entry_order[0], section, 0, False)
    step_now = lax.dynamic_index_in_dim(step_index[0], patch, 0, False)
    modul = (
        lax.dynamic_index_in_dim(image_modulation[0], step_now, 0, False)
        .astype(jnp.float32)
        .reshape(6, width)
    )
    text_mod = (
        lax.dynamic_index_in_dim(text_modulation[0], step_now, 0, False)
        .astype(jnp.float32)
        .reshape(3, width)
    )
    image_normed = modulate(image_x, modul[0], modul[1]).astype(jnp.bfloat16)
    text_normed = modulate(text_x, text_mod[0], text_mod[1]).astype(jnp.bfloat16)
    stale = stale_cache[0, 0]
    cache_rows = stale.shape[0]
    heads = width // HDIM

    def by_head(pieces):
        pack = jnp.concatenate(
            [piece.reshape(piece.shape[0], heads, HDIM) for piece in pieces], axis=0
        )
        pack = jnp.transpose(pack, (1, 0, 2))
        pack = jnp.pad(pack, ((0, devices - heads), (0, 0), (0, 0)))
        return lax.all_to_all(pack, TOK, split_axis=0, concat_axis=0, tiled=True)

    got_cache = by_head([stale[:, :width], stale[:, width:]])
    got_cache, image_normed, text_normed = lax.optimization_barrier(
        (got_cache, image_normed, text_normed)
    )
    every = lax.all_gather(
        jnp.concatenate([image_normed, text_normed], axis=0), TOK, axis=0, tiled=False
    )
    flat = every.reshape(-1, width)
    image_cols = jnp.dot(flat, image_to_heads[0], preferred_element_type=jnp.float32)
    text_cols = jnp.dot(flat, text_to_heads[0], preferred_element_type=jnp.float32)
    is_image = (jnp.arange(image_rows + text_rows) < image_rows)[None, :, None]
    proj = cols_to_rows(
        jnp.where(
            is_image,
            image_cols.reshape(devices, image_rows + text_rows, -1),
            text_cols.reshape(devices, image_rows + text_rows, -1),
        ).astype(jnp.bfloat16)
    )
    image_proj = proj[:image_rows]
    text_proj = proj[image_rows:]
    gains = head_gain[0]
    image_query = head_norm(image_proj[:, :width].astype(jnp.float32), gains[0]).astype(
        jnp.bfloat16
    )
    image_key = head_norm(image_proj[:, width : 2 * width].astype(jnp.float32), gains[1]).astype(
        jnp.bfloat16
    )
    text_query = head_norm(text_proj[:, :width].astype(jnp.float32), gains[2]).astype(jnp.bfloat16)
    text_key = head_norm(text_proj[:, width : 2 * width].astype(jnp.float32), gains[3]).astype(
        jnp.bfloat16
    )
    image_value = image_proj[:, 2 * width :]
    text_value = text_proj[:, 2 * width :]
    fresh_image = jnp.concatenate([image_key, image_value], axis=1)
    patch_len = image_rows * devices
    per_patch = patch_len // cache_rows
    row_q = jnp.concatenate([image_query, text_query], axis=0)
    row_k = jnp.concatenate([image_key, text_key], axis=0)
    row_v = jnp.concatenate([image_value, text_value], axis=0)
    got = by_head([row_q, row_k, row_v])
    rows = image_rows + text_rows

    def part(first, count, source=got):
        return source[:, first : first + count].reshape(-1, HDIM)

    queries = jnp.concatenate([part(0, image_rows), part(image_rows, text_rows)], axis=0)
    fresh_k = part(rows, image_rows)
    text_k = part(rows + image_rows, text_rows)
    fresh_v = part(2 * rows, image_rows)
    text_v = part(2 * rows + image_rows, text_rows)
    cache_k = part(0, cache_rows, got_cache)
    cache_v = part(cache_rows, cache_rows, got_cache)
    begin = patch * patch_len
    cache_k = lax.dynamic_update_slice_in_dim(cache_k, fresh_k, begin, 0)
    cache_v = lax.dynamic_update_slice_in_dim(cache_v, fresh_v, begin, 0)
    keys = jnp.concatenate([cache_k, text_k], axis=0)
    values = jnp.concatenate([cache_v, text_v], axis=0)
    text_count = text_length[0]
    valid = jnp.concatenate(
        [
            jnp.ones((cache_k.shape[0],), bool),
            jnp.arange(text_k.shape[0], dtype=jnp.int32) < text_count,
        ]
    )
    head_out = attend(queries, keys, values, valid)
    image_heads = broadcast_rows(head_out[:patch_len], devices).reshape(devices, patch_len, HDIM)
    riders = fresh_image.reshape(-1, HDIM)
    text_heads = lax.all_gather(
        jnp.concatenate([head_out[patch_len:], riders], axis=0), TOK, axis=0, tiled=False
    )
    text_len = head_out.shape[0] - patch_len
    fresh_all = text_heads[:, text_len:].reshape(patch_len, -1)
    text_heads = text_heads[:, :text_len]
    moved = lax.dynamic_slice_in_dim(
        fresh_all, (position % per_patch) * cache_rows, cache_rows, 0
    )
    current = jnp.where(position // per_patch == patch, moved, stale)
    def from_heads(blocks, weight):
        return jnp.einsum(
            "hrd,hdc->rc",
            blocks[:heads],
            weight.reshape(heads, HDIM, -1),
            preferred_element_type=jnp.float32,
        ).astype(jnp.bfloat16)

    image_back = cols_to_rows(
        from_heads(image_heads, image_from_heads[0]).reshape(devices, image_rows, -1)
    )
    text_back = cols_to_rows(
        from_heads(text_heads, text_from_heads[0]).reshape(devices, text_rows, -1)
    )
    image_mid = image_x + modul[2] * image_back.astype(jnp.float32)
    text_out = (text_x + text_mod[2] * text_back.astype(jnp.float32)).astype(jnp.bfloat16)
    mlp_normed = modulate(image_mid, modul[3], modul[4]).astype(jnp.bfloat16)
    up_weight = image_up[0]
    down_weight = image_down[0]
    hidden = jax.nn.gelu(
        jnp.dot(
            broadcast_rows(mlp_normed, devices),
            up_weight,
            preferred_element_type=jnp.float32,
        ),
        approximate=True,
    ).astype(jnp.bfloat16)
    partial = jnp.dot(hidden, down_weight, preferred_element_type=jnp.float32)
    partial, text_back = lax.optimization_barrier((partial, text_back))
    reduced = jnp.sum(
        lax.all_to_all(
            partial.astype(jnp.bfloat16).reshape(devices, image_rows, width),
            TOK,
            split_axis=0,
            concat_axis=0,
            tiled=True,
        ).astype(jnp.float32),
        axis=0,
    )
    image_out = (image_mid + modul[5] * reduced).astype(jnp.bfloat16)
    text_next = from_behind(text_out, "section", 1)
    image_next = from_behind(image_out, "section", 1)
    final_source = jnp.where(section == last_section, image_out, image_next)
    patch_last = entry_order[0, last_section]
    step_last = lax.dynamic_index_in_dim(step_index[0], patch_last, 0, False)
    final_mod = (
        lax.dynamic_index_in_dim(final_modulation, step_last, 0, False)
        .astype(jnp.float32)
        .reshape(2, width)
    )
    normed = modulate(final_source.astype(jnp.float32), final_mod[0], final_mod[1]).astype(
        jnp.bfloat16
    )
    velocity = jnp.dot(normed, final_weight, preferred_element_type=jnp.float32)
    latents_next = latents[0] + -1.0 / TSTEPS * velocity
    return (image_next[None, None], text_next[None, None], current[None, None], latents_next[None])


def solution(mesh):
    shape = mesh.devices.shape
    split = jax.sharding.Mesh(
        mesh.devices.reshape(shape[:2] + (shape[2] // QUAD, QUAD)),
        ("section", "grp", "ta", "tb"),
    )
    placed = (
        P("section", "grp", TOK, None),
        P("section", "grp", TOK, None),
        P("grp"),
        P("grp", None),
        P("grp", None),
        P("section", None, None),
        P("section", None, None),
        P("section", None, TOK),
        P("section", None, TOK),
        P("section", None, None),
        P("section", None, TOK),
        P("section", None, TOK),
        P("section", None, TOK),
        P("section", TOK, None),
        P("section", "grp", TOK, None),
        P(),
        P(None, "section"),
        P("grp", TOK, "section"),
    )
    return jax.shard_map(
        shards,
        mesh=split,
        in_specs=placed,
        out_specs=(
            P("section", "grp", TOK, None),
            P("section", "grp", TOK, None),
            P("section", "grp", TOK, None),
            P("grp", TOK, "section"),
        ),
        check_vma=False,
    )
```

```python
import jax
import jax.numpy as jnp
from jax import lax
from jax.sharding import PartitionSpec as P

HDIM = 128
TSTEPS = 4


TOK = ("ta", "tb")
QUAD = 4

eps = 1e-06
masked_score = -1e30


def from_behind(block, axis, distance):
    devices = range(lax.axis_size(axis))
    route = [((i - distance) % len(devices), i) for i in devices]
    return lax.ppermute(block, axis, route)


def layer_norm(field):
    mean = jnp.mean(field, axis=-1, keepdims=True)
    centred = field - mean
    spread = jnp.mean(centred * centred, axis=-1, keepdims=True)
    return centred * lax.rsqrt(spread + eps)


def modulate(field, shift, scale):
    return layer_norm(field) * (1.0 + scale) + shift


def head_norm(field, gain):
    height, width = field.shape
    shaped = field.reshape(height, width // HDIM, HDIM)
    power = jnp.mean(shaped * shaped, axis=-1, keepdims=True)
    return (shaped * lax.rsqrt(power + eps) * gain).reshape(height, width)


def attend(queries, keys, values, valid):
    height, width = queries.shape
    heads = width // HDIM
    scores = jnp.einsum(
        "qhd,khd->qhk",
        queries.reshape(height, heads, HDIM),
        keys.reshape(-1, heads, HDIM),
        preferred_element_type=jnp.float32,
    ) * HDIM ** (-0.5)
    scores = jnp.where(valid[None, None, :], scores, masked_score)
    highest = jnp.max(scores, axis=-1, keepdims=True)
    expo = jnp.where(valid[None, None, :], jnp.exp(scores - highest), 0.0)
    total = jnp.sum(expo, axis=-1)
    mixed = jnp.einsum(
        "qhk,khd->qhd",
        expo.astype(jnp.bfloat16),
        values.reshape(-1, heads, HDIM),
        preferred_element_type=jnp.float32,
    )
    return (mixed / total[..., None]).reshape(height, width).astype(jnp.bfloat16)


def cols_to_rows(cols):
    got = lax.all_to_all(cols, TOK, split_axis=0, concat_axis=0, tiled=True)
    count, rows, width = got.shape
    return jnp.transpose(got, (1, 0, 2)).reshape(rows, count * width)


def broadcast_rows(block, devices):
    copies = jnp.broadcast_to(block[None], (devices,) + block.shape)
    got = lax.all_to_all(copies, TOK, split_axis=0, concat_axis=0, tiled=True)
    return got.reshape(-1, block.shape[-1])


def shards(
    image_in,
    text_in,
    text_length,
    entry_order,
    step_index,
    image_modulation,
    text_modulation,
    image_to_heads,
    text_to_heads,
    head_gain,
    image_from_heads,
    text_from_heads,
    image_up,
    image_down,
    stale_cache,
    final_modulation,
    final_weight,
    latents,
):
    section = lax.axis_index("section")
    last_section = lax.axis_size("section") - 1
    position = lax.axis_index("ta") * lax.axis_size("tb") + lax.axis_index("tb")
    devices = lax.axis_size("ta") * lax.axis_size("tb")
    image_x = image_in[0, 0].astype(jnp.float32)
    text_x = text_in[0, 0].astype(jnp.float32)
    image_rows = image_x.shape[0]
    text_rows = text_x.shape[0]
    width = image_x.shape[1]
    patch = lax.dynamic_index_in_dim(entry_order[0], section, 0, False)
    step_now = lax.dynamic_index_in_dim(step_index[0], patch, 0, False)
    modul = (
        lax.dynamic_index_in_dim(image_modulation[0], step_now, 0, False)
        .astype(jnp.float32)
        .reshape(6, width)
    )
    text_mod = (
        lax.dynamic_index_in_dim(text_modulation[0], step_now, 0, False)
        .astype(jnp.float32)
        .reshape(3, width)
    )
    image_normed = modulate(image_x, modul[0], modul[1]).astype(jnp.bfloat16)
    text_normed = modulate(text_x, text_mod[0], text_mod[1]).astype(jnp.bfloat16)
    stale = stale_cache[0, 0]
    cache_rows = stale.shape[0]
    heads = width // HDIM

    def by_head(pieces):
        pack = jnp.concatenate(
            [piece.reshape(piece.shape[0], heads, HDIM) for piece in pieces], axis=0
        )
        pack = jnp.transpose(pack, (1, 0, 2))
        pack = jnp.pad(pack, ((0, devices - heads), (0, 0), (0, 0)))
        return lax.all_to_all(pack, TOK, split_axis=0, concat_axis=0, tiled=True)

    got_cache = by_head([stale[:, :width], stale[:, width:]])
    got_cache, image_normed, text_normed = lax.optimization_barrier(
        (got_cache, image_normed, text_normed)
    )
    every = lax.all_gather(
        jnp.concatenate([image_normed, text_normed], axis=0), TOK, axis=0, tiled=False
    )
    flat = every.reshape(-1, width)
    image_cols = jnp.dot(flat, image_to_heads[0], preferred_element_type=jnp.float32)
    text_cols = jnp.dot(flat, text_to_heads[0], preferred_element_type=jnp.float32)
    is_image = (jnp.arange(image_rows + text_rows) < image_rows)[None, :, None]
    proj = cols_to_rows(
        jnp.where(
            is_image,
            image_cols.reshape(devices, image_rows + text_rows, -1),
            text_cols.reshape(devices, image_rows + text_rows, -1),
        ).astype(jnp.bfloat16)
    )
    image_proj = proj[:image_rows]
    text_proj = proj[image_rows:]
    gains = head_gain[0]
    image_query = head_norm(image_proj[:, :width].astype(jnp.float32), gains[0]).astype(
        jnp.bfloat16
    )
    image_key = head_norm(image_proj[:, width : 2 * width].astype(jnp.float32), gains[1]).astype(
        jnp.bfloat16
    )
    text_query = head_norm(text_proj[:, :width].astype(jnp.float32), gains[2]).astype(jnp.bfloat16)
    text_key = head_norm(text_proj[:, width : 2 * width].astype(jnp.float32), gains[3]).astype(
        jnp.bfloat16
    )
    image_value = image_proj[:, 2 * width :]
    text_value = text_proj[:, 2 * width :]
    fresh_image = jnp.concatenate([image_key, image_value], axis=1)
    group = lax.axis_size("tb")
    blocks = devices // group
    mine = lax.axis_index("tb")
    quad = [fresh_image]
    for shift in range(1, group):
        turn = [(j * group + b, j * group + (b + shift) % group) for j in range(blocks) for b in range(group)]
        quad.append(lax.ppermute(fresh_image, TOK, turn))
    quad = jnp.stack(quad)
    quad = jnp.take(quad, (mine - jnp.arange(group)) % group, axis=0).reshape(-1, fresh_image.shape[1])
    route = [(j * group + b, j + blocks * b) for j in range(blocks) for b in range(group)]
    moved = lax.ppermute(quad, TOK, route)
    patch_len = image_rows * devices
    per_patch = patch_len // cache_rows
    current = jnp.where(position // per_patch == patch, moved, stale)
    row_q = jnp.concatenate([image_query, text_query], axis=0)
    row_k = jnp.concatenate([image_key, text_key], axis=0)
    row_v = jnp.concatenate([image_value, text_value], axis=0)
    got = by_head([row_q, row_k, row_v])
    got, current = lax.optimization_barrier((got, current))
    rows = image_rows + text_rows

    def part(first, count, source=got):
        return source[:, first : first + count].reshape(-1, HDIM)

    queries = jnp.concatenate([part(0, image_rows), part(image_rows, text_rows)], axis=0)
    fresh_k = part(rows, image_rows)
    text_k = part(rows + image_rows, text_rows)
    fresh_v = part(2 * rows, image_rows)
    text_v = part(2 * rows + image_rows, text_rows)
    cache_k = part(0, cache_rows, got_cache)
    cache_v = part(cache_rows, cache_rows, got_cache)
    begin = patch * patch_len
    cache_k = lax.dynamic_update_slice_in_dim(cache_k, fresh_k, begin, 0)
    cache_v = lax.dynamic_update_slice_in_dim(cache_v, fresh_v, begin, 0)
    keys = jnp.concatenate([cache_k, text_k], axis=0)
    values = jnp.concatenate([cache_v, text_v], axis=0)
    text_count = text_length[0]
    valid = jnp.concatenate(
        [
            jnp.ones((cache_k.shape[0],), bool),
            jnp.arange(text_k.shape[0], dtype=jnp.int32) < text_count,
        ]
    )
    head_out = attend(queries, keys, values, valid)
    image_heads = broadcast_rows(head_out[:patch_len], devices).reshape(devices, patch_len, HDIM)
    text_heads = lax.all_gather(head_out[patch_len:], TOK, axis=0, tiled=False)
    def from_heads(blocks, weight):
        return jnp.einsum(
            "hrd,hdc->rc",
            blocks[:heads],
            weight.reshape(heads, HDIM, -1),
            preferred_element_type=jnp.float32,
        ).astype(jnp.bfloat16)

    image_back = cols_to_rows(
        from_heads(image_heads, image_from_heads[0]).reshape(devices, image_rows, -1)
    )
    text_back = cols_to_rows(
        from_heads(text_heads, text_from_heads[0]).reshape(devices, text_rows, -1)
    )
    image_mid = image_x + modul[2] * image_back.astype(jnp.float32)
    text_out = (text_x + text_mod[2] * text_back.astype(jnp.float32)).astype(jnp.bfloat16)
    mlp_normed = modulate(image_mid, modul[3], modul[4]).astype(jnp.bfloat16)
    up_weight = image_up[0]
    down_weight = image_down[0]
    hidden = jax.nn.gelu(
        jnp.dot(
            broadcast_rows(mlp_normed, devices),
            up_weight,
            preferred_element_type=jnp.float32,
        ),
        approximate=True,
    ).astype(jnp.bfloat16)
    partial = jnp.dot(hidden, down_weight, preferred_element_type=jnp.float32)
    partial, text_back = lax.optimization_barrier((partial, text_back))
    reduced = jnp.sum(
        lax.all_to_all(
            partial.astype(jnp.bfloat16).reshape(devices, image_rows, width),
            TOK,
            split_axis=0,
            concat_axis=0,
            tiled=True,
        ).astype(jnp.float32),
        axis=0,
    )
    image_out = (image_mid + modul[5] * reduced).astype(jnp.bfloat16)
    text_next = from_behind(text_out, "section", 1)
    image_next = from_behind(image_out, "section", 1)
    final_source = jnp.where(section == last_section, image_out, image_next)
    patch_last = entry_order[0, last_section]
    step_last = lax.dynamic_index_in_dim(step_index[0], patch_last, 0, False)
    final_mod = (
        lax.dynamic_index_in_dim(final_modulation, step_last, 0, False)
        .astype(jnp.float32)
        .reshape(2, width)
    )
    normed = modulate(final_source.astype(jnp.float32), final_mod[0], final_mod[1]).astype(
        jnp.bfloat16
    )
    velocity = jnp.dot(normed, final_weight, preferred_element_type=jnp.float32)
    latents_next = latents[0] + -1.0 / TSTEPS * velocity
    return (image_next[None, None], text_next[None, None], current[None, None], latents_next[None])


def solution(mesh):
    shape = mesh.devices.shape
    split = jax.sharding.Mesh(
        mesh.devices.reshape(shape[:2] + (shape[2] // QUAD, QUAD)),
        ("section", "grp", "ta", "tb"),
    )
    placed = (
        P("section", "grp", TOK, None),
        P("section", "grp", TOK, None),
        P("grp"),
        P("grp", None),
        P("grp", None),
        P("section", None, None),
        P("section", None, None),
        P("section", None, TOK),
        P("section", None, TOK),
        P("section", None, None),
        P("section", None, TOK),
        P("section", None, TOK),
        P("section", None, TOK),
        P("section", TOK, None),
        P("section", "grp", TOK, None),
        P(),
        P(None, "section"),
        P("grp", TOK, "section"),
    )
    return jax.shard_map(
        shards,
        mesh=split,
        in_specs=placed,
        out_specs=(
            P("section", "grp", TOK, None),
            P("section", "grp", TOK, None),
            P("section", "grp", TOK, None),
            P("grp", TOK, "section"),
        ),
        check_vma=False,
    )
```

```python
import jax
import jax.numpy as jnp
from jax import lax
from jax.sharding import PartitionSpec as P

HDIM = 128
TSTEPS = 4


TOK = ("ta", "tb")
QUAD = 4

eps = 1e-06
masked_score = -1e30


def from_behind(block, axis, distance):
    devices = range(lax.axis_size(axis))
    route = [((i - distance) % len(devices), i) for i in devices]
    return lax.ppermute(block, axis, route)


def layer_norm(field):
    mean = jnp.mean(field, axis=-1, keepdims=True)
    centred = field - mean
    spread = jnp.mean(centred * centred, axis=-1, keepdims=True)
    return centred * lax.rsqrt(spread + eps)


def modulate(field, shift, scale):
    return layer_norm(field) * (1.0 + scale) + shift


def head_norm(field, gain):
    height, width = field.shape
    shaped = field.reshape(height, width // HDIM, HDIM)
    power = jnp.mean(shaped * shaped, axis=-1, keepdims=True)
    return (shaped * lax.rsqrt(power + eps) * gain).reshape(height, width)


def attend(queries, keys, values, valid):
    height, width = queries.shape
    heads = width // HDIM
    scores = jnp.einsum(
        "qhd,khd->qhk",
        queries.reshape(height, heads, HDIM),
        keys.reshape(-1, heads, HDIM),
        preferred_element_type=jnp.float32,
    ) * HDIM ** (-0.5)
    scores = jnp.where(valid[None, None, :], scores, masked_score)
    highest = jnp.max(scores, axis=-1, keepdims=True)
    expo = jnp.where(valid[None, None, :], jnp.exp(scores - highest), 0.0)
    total = jnp.sum(expo, axis=-1)
    mixed = jnp.einsum(
        "qhk,khd->qhd",
        expo.astype(jnp.bfloat16),
        values.reshape(-1, heads, HDIM),
        preferred_element_type=jnp.float32,
    )
    return (mixed / total[..., None]).reshape(height, width).astype(jnp.bfloat16)


def cols_to_rows(cols):
    got = lax.all_to_all(cols, TOK, split_axis=0, concat_axis=0, tiled=True)
    count, rows, width = got.shape
    return jnp.transpose(got, (1, 0, 2)).reshape(rows, count * width)


def broadcast_rows(block, devices):
    copies = jnp.broadcast_to(block[None], (devices,) + block.shape)
    got = lax.all_to_all(copies, TOK, split_axis=0, concat_axis=0, tiled=True)
    return got.reshape(-1, block.shape[-1])


def shards(
    image_in,
    text_in,
    text_length,
    entry_order,
    step_index,
    image_modulation,
    text_modulation,
    image_to_heads,
    text_to_heads,
    head_gain,
    image_from_heads,
    text_from_heads,
    image_up,
    image_down,
    stale_cache,
    final_modulation,
    final_weight,
    latents,
):
    section = lax.axis_index("section")
    last_section = lax.axis_size("section") - 1
    position = lax.axis_index("ta") * lax.axis_size("tb") + lax.axis_index("tb")
    devices = lax.axis_size("ta") * lax.axis_size("tb")
    image_x = image_in[0, 0].astype(jnp.float32)
    text_x = text_in[0, 0].astype(jnp.float32)
    image_rows = image_x.shape[0]
    text_rows = text_x.shape[0]
    width = image_x.shape[1]
    patch = lax.dynamic_index_in_dim(entry_order[0], section, 0, False)
    step_now = lax.dynamic_index_in_dim(step_index[0], patch, 0, False)
    modul = (
        lax.dynamic_index_in_dim(image_modulation[0], step_now, 0, False)
        .astype(jnp.float32)
        .reshape(6, width)
    )
    text_mod = (
        lax.dynamic_index_in_dim(text_modulation[0], step_now, 0, False)
        .astype(jnp.float32)
        .reshape(3, width)
    )
    image_normed = modulate(image_x, modul[0], modul[1]).astype(jnp.bfloat16)
    text_normed = modulate(text_x, text_mod[0], text_mod[1]).astype(jnp.bfloat16)
    stale = stale_cache[0, 0]
    cache_rows = stale.shape[0]
    heads = width // HDIM

    def by_head(pieces):
        pack = jnp.concatenate(
            [piece.reshape(piece.shape[0], heads, HDIM) for piece in pieces], axis=0
        )
        pack = jnp.transpose(pack, (1, 0, 2))
        pack = jnp.pad(pack, ((0, devices - heads), (0, 0), (0, 0)))
        return lax.all_to_all(pack, TOK, split_axis=0, concat_axis=0, tiled=True)

    got_cache = by_head([stale[:, :width], stale[:, width:]])
    got_cache, image_normed, text_normed = lax.optimization_barrier(
        (got_cache, image_normed, text_normed)
    )
    every = lax.all_gather(
        jnp.concatenate([image_normed, text_normed], axis=0), TOK, axis=0, tiled=False
    )
    flat = every.reshape(-1, width)
    image_cols = jnp.dot(flat, image_to_heads[0], preferred_element_type=jnp.float32)
    text_cols = jnp.dot(flat, text_to_heads[0], preferred_element_type=jnp.float32)
    is_image = (jnp.arange(image_rows + text_rows) < image_rows)[None, :, None]
    proj = cols_to_rows(
        jnp.where(
            is_image,
            image_cols.reshape(devices, image_rows + text_rows, -1),
            text_cols.reshape(devices, image_rows + text_rows, -1),
        ).astype(jnp.bfloat16)
    )
    image_proj = proj[:image_rows]
    text_proj = proj[image_rows:]
    gains = head_gain[0]
    image_query = head_norm(image_proj[:, :width].astype(jnp.float32), gains[0]).astype(
        jnp.bfloat16
    )
    image_key = head_norm(image_proj[:, width : 2 * width].astype(jnp.float32), gains[1]).astype(
        jnp.bfloat16
    )
    text_query = head_norm(text_proj[:, :width].astype(jnp.float32), gains[2]).astype(jnp.bfloat16)
    text_key = head_norm(text_proj[:, width : 2 * width].astype(jnp.float32), gains[3]).astype(
        jnp.bfloat16
    )
    image_value = image_proj[:, 2 * width :]
    text_value = text_proj[:, 2 * width :]
    fresh_image = jnp.concatenate([image_key, image_value], axis=1)
    group = lax.axis_size("tb")
    blocks = devices // group
    mine = lax.axis_index("tb")
    quad = [fresh_image]
    for shift in range(1, group):
        turn = [(j * group + b, j * group + (b + shift) % group) for j in range(blocks) for b in range(group)]
        quad.append(lax.ppermute(fresh_image, TOK, turn))
    quad = jnp.stack(quad)
    quad = jnp.take(quad, (mine - jnp.arange(group)) % group, axis=0).reshape(-1, fresh_image.shape[1])
    route = [(j * group + b, j + blocks * b) for j in range(blocks) for b in range(group)]
    moved = lax.ppermute(quad, TOK, route)
    patch_len = image_rows * devices
    per_patch = patch_len // cache_rows
    current = jnp.where(position // per_patch == patch, moved, stale)
    row_q = jnp.concatenate([image_query, text_query], axis=0)
    row_k = jnp.concatenate([image_key, text_key], axis=0)
    row_v = jnp.concatenate([image_value, text_value], axis=0)
    got = by_head([row_q, row_k, row_v])
    got, current = lax.optimization_barrier((got, current))
    rows = image_rows + text_rows

    def part(first, count, source=got):
        return source[:, first : first + count].reshape(-1, HDIM)

    queries = jnp.concatenate([part(0, image_rows), part(image_rows, text_rows)], axis=0)
    fresh_k = part(rows, image_rows)
    text_k = part(rows + image_rows, text_rows)
    fresh_v = part(2 * rows, image_rows)
    text_v = part(2 * rows + image_rows, text_rows)
    cache_k = part(0, cache_rows, got_cache)
    cache_v = part(cache_rows, cache_rows, got_cache)
    begin = patch * patch_len
    cache_k = lax.dynamic_update_slice_in_dim(cache_k, fresh_k, begin, 0)
    cache_v = lax.dynamic_update_slice_in_dim(cache_v, fresh_v, begin, 0)
    keys = jnp.concatenate([cache_k, text_k], axis=0)
    values = jnp.concatenate([cache_v, text_v], axis=0)
    text_count = text_length[0]
    valid = jnp.concatenate(
        [
            jnp.ones((cache_k.shape[0],), bool),
            jnp.arange(text_k.shape[0], dtype=jnp.int32) < text_count,
        ]
    )
    head_out = attend(queries, keys, values, valid)
    image_heads = broadcast_rows(head_out[:patch_len], devices).reshape(devices, patch_len, HDIM)
    text_heads = lax.all_gather(head_out[patch_len:], TOK, axis=0, tiled=False)
    def from_heads(blocks, weight):
        return jnp.einsum(
            "hrd,hdc->rc",
            blocks[:heads],
            weight.reshape(heads, HDIM, -1),
            preferred_element_type=jnp.float32,
        ).astype(jnp.bfloat16)

    image_back = cols_to_rows(
        from_heads(image_heads, image_from_heads[0]).reshape(devices, image_rows, -1)
    )
    text_back_cols = from_heads(text_heads, text_from_heads[0]).reshape(devices, -1)
    image_mid = image_x + modul[2] * image_back.astype(jnp.float32)
    mlp_normed = modulate(image_mid, modul[3], modul[4]).astype(jnp.bfloat16)
    up_weight = image_up[0]
    down_weight = image_down[0]
    hidden = jax.nn.gelu(
        jnp.dot(
            broadcast_rows(mlp_normed, devices),
            up_weight,
            preferred_element_type=jnp.float32,
        ),
        approximate=True,
    ).astype(jnp.bfloat16)
    partial = jnp.dot(hidden, down_weight, preferred_element_type=jnp.float32)
    sums = partial.astype(jnp.bfloat16).reshape(devices, -1)
    both = lax.all_to_all(
        jnp.concatenate([sums, text_back_cols], axis=1),
        TOK,
        split_axis=0,
        concat_axis=0,
        tiled=True,
    )
    reduced = jnp.sum(
        both[:, : sums.shape[1]].reshape(devices, image_rows, width).astype(jnp.float32), axis=0
    )
    text_back = jnp.transpose(
        both[:, sums.shape[1] :].reshape(devices, text_rows, -1), (1, 0, 2)
    ).reshape(text_rows, width)
    text_out = (text_x + text_mod[2] * text_back.astype(jnp.float32)).astype(jnp.bfloat16)
    image_out = (image_mid + modul[5] * reduced).astype(jnp.bfloat16)
    text_next = from_behind(text_out, "section", 1)
    image_next = from_behind(image_out, "section", 1)
    final_source = jnp.where(section == last_section, image_out, image_next)
    patch_last = entry_order[0, last_section]
    step_last = lax.dynamic_index_in_dim(step_index[0], patch_last, 0, False)
    final_mod = (
        lax.dynamic_index_in_dim(final_modulation, step_last, 0, False)
        .astype(jnp.float32)
        .reshape(2, width)
    )
    normed = modulate(final_source.astype(jnp.float32), final_mod[0], final_mod[1]).astype(
        jnp.bfloat16
    )
    velocity = jnp.dot(normed, final_weight, preferred_element_type=jnp.float32)
    latents_next = latents[0] + -1.0 / TSTEPS * velocity
    return (image_next[None, None], text_next[None, None], current[None, None], latents_next[None])


def solution(mesh):
    shape = mesh.devices.shape
    split = jax.sharding.Mesh(
        mesh.devices.reshape(shape[:2] + (shape[2] // QUAD, QUAD)),
        ("section", "grp", "ta", "tb"),
    )
    placed = (
        P("section", "grp", TOK, None),
        P("section", "grp", TOK, None),
        P("grp"),
        P("grp", None),
        P("grp", None),
        P("section", None, None),
        P("section", None, None),
        P("section", None, TOK),
        P("section", None, TOK),
        P("section", None, None),
        P("section", None, TOK),
        P("section", None, TOK),
        P("section", None, TOK),
        P("section", TOK, None),
        P("section", "grp", TOK, None),
        P(),
        P(None, "section"),
        P("grp", TOK, "section"),
    )
    return jax.shard_map(
        shards,
        mesh=split,
        in_specs=placed,
        out_specs=(
            P("section", "grp", TOK, None),
            P("section", "grp", TOK, None),
            P("section", "grp", TOK, None),
            P("grp", TOK, "section"),
        ),
        check_vma=False,
    )
```

```python
import jax
import jax.numpy as jnp
from jax import lax
from jax.sharding import PartitionSpec as P

HDIM = 128
TSTEPS = 4


TOK = ("ta", "tb")
QUAD = 4

eps = 1e-06
masked_score = -1e30


def from_behind(block, axis, distance):
    devices = range(lax.axis_size(axis))
    route = [((i - distance) % len(devices), i) for i in devices]
    return lax.ppermute(block, axis, route)


def layer_norm(field):
    mean = jnp.mean(field, axis=-1, keepdims=True)
    centred = field - mean
    spread = jnp.mean(centred * centred, axis=-1, keepdims=True)
    return centred * lax.rsqrt(spread + eps)


def modulate(field, shift, scale):
    return layer_norm(field) * (1.0 + scale) + shift


def head_norm(field, gain):
    height, width = field.shape
    shaped = field.reshape(height, width // HDIM, HDIM)
    power = jnp.mean(shaped * shaped, axis=-1, keepdims=True)
    return (shaped * lax.rsqrt(power + eps) * gain).reshape(height, width)


def attend(queries, keys, values, valid):
    height, width = queries.shape
    heads = width // HDIM
    scores = jnp.einsum(
        "qhd,khd->qhk",
        queries.reshape(height, heads, HDIM),
        keys.reshape(-1, heads, HDIM),
        preferred_element_type=jnp.float32,
    ) * HDIM ** (-0.5)
    scores = jnp.where(valid[None, None, :], scores, masked_score)
    highest = jnp.max(scores, axis=-1, keepdims=True)
    expo = jnp.where(valid[None, None, :], jnp.exp(scores - highest), 0.0)
    total = jnp.sum(expo, axis=-1)
    mixed = jnp.einsum(
        "qhk,khd->qhd",
        expo.astype(jnp.bfloat16),
        values.reshape(-1, heads, HDIM),
        preferred_element_type=jnp.float32,
    )
    return (mixed / total[..., None]).reshape(height, width).astype(jnp.bfloat16)


def cols_to_rows(cols):
    got = lax.all_to_all(cols, TOK, split_axis=0, concat_axis=0, tiled=True)
    count, rows, width = got.shape
    return jnp.transpose(got, (1, 0, 2)).reshape(rows, count * width)


def broadcast_rows(block, devices):
    copies = jnp.broadcast_to(block[None], (devices,) + block.shape)
    got = lax.all_to_all(copies, TOK, split_axis=0, concat_axis=0, tiled=True)
    return got.reshape(-1, block.shape[-1])


def shards(
    image_in,
    text_in,
    text_length,
    entry_order,
    step_index,
    image_modulation,
    text_modulation,
    image_to_heads,
    text_to_heads,
    head_gain,
    image_from_heads,
    text_from_heads,
    image_up,
    image_down,
    stale_cache,
    final_modulation,
    final_weight,
    latents,
):
    section = lax.axis_index("section")
    last_section = lax.axis_size("section") - 1
    position = lax.axis_index("ta") * lax.axis_size("tb") + lax.axis_index("tb")
    devices = lax.axis_size("ta") * lax.axis_size("tb")
    image_x = image_in[0, 0].astype(jnp.float32)
    text_x = text_in[0, 0].astype(jnp.float32)
    image_rows = image_x.shape[0]
    text_rows = text_x.shape[0]
    width = image_x.shape[1]
    patch = lax.dynamic_index_in_dim(entry_order[0], section, 0, False)
    step_now = lax.dynamic_index_in_dim(step_index[0], patch, 0, False)
    modul = (
        lax.dynamic_index_in_dim(image_modulation[0], step_now, 0, False)
        .astype(jnp.float32)
        .reshape(6, width)
    )
    text_mod = (
        lax.dynamic_index_in_dim(text_modulation[0], step_now, 0, False)
        .astype(jnp.float32)
        .reshape(3, width)
    )
    image_normed = modulate(image_x, modul[0], modul[1]).astype(jnp.bfloat16)
    text_normed = modulate(text_x, text_mod[0], text_mod[1]).astype(jnp.bfloat16)
    stale = stale_cache[0, 0]
    cache_rows = stale.shape[0]
    heads = width // HDIM

    def by_head(pieces):
        pack = jnp.concatenate(
            [piece.reshape(piece.shape[0], heads, HDIM) for piece in pieces], axis=0
        )
        pack = jnp.transpose(pack, (1, 0, 2))
        pack = jnp.pad(pack, ((0, devices - heads), (0, 0), (0, 0)))
        return lax.all_to_all(pack, TOK, split_axis=0, concat_axis=0, tiled=True)

    got_cache = by_head([stale[:, :width], stale[:, width:]])
    got_cache, image_normed, text_normed = lax.optimization_barrier(
        (got_cache, image_normed, text_normed)
    )
    every_text = lax.all_gather(text_normed, TOK, axis=0, tiled=True)
    every_image = broadcast_rows(image_normed, devices)
    image_cols = jnp.dot(every_image, image_to_heads[0], preferred_element_type=jnp.float32)
    text_cols = jnp.dot(every_text, text_to_heads[0], preferred_element_type=jnp.float32)
    proj = cols_to_rows(
        jnp.concatenate(
            [
                image_cols.reshape(devices, image_rows, -1),
                text_cols.reshape(devices, text_rows, -1),
            ],
            axis=1,
        ).astype(jnp.bfloat16)
    )
    image_proj = proj[:image_rows]
    text_proj = proj[image_rows:]
    gains = head_gain[0]
    image_query = head_norm(image_proj[:, :width].astype(jnp.float32), gains[0]).astype(
        jnp.bfloat16
    )
    image_key = head_norm(image_proj[:, width : 2 * width].astype(jnp.float32), gains[1]).astype(
        jnp.bfloat16
    )
    text_query = head_norm(text_proj[:, :width].astype(jnp.float32), gains[2]).astype(jnp.bfloat16)
    text_key = head_norm(text_proj[:, width : 2 * width].astype(jnp.float32), gains[3]).astype(
        jnp.bfloat16
    )
    image_value = image_proj[:, 2 * width :]
    text_value = text_proj[:, 2 * width :]
    fresh_image = jnp.concatenate([image_key, image_value], axis=1)
    group = lax.axis_size("tb")
    blocks = devices // group
    mine = lax.axis_index("tb")
    quad = [fresh_image]
    for shift in range(1, group):
        turn = [(j * group + b, j * group + (b + shift) % group) for j in range(blocks) for b in range(group)]
        quad.append(lax.ppermute(fresh_image, TOK, turn))
    quad = jnp.stack(quad)
    quad = jnp.take(quad, (mine - jnp.arange(group)) % group, axis=0).reshape(-1, fresh_image.shape[1])
    route = [(j * group + b, j + blocks * b) for j in range(blocks) for b in range(group)]
    moved = lax.ppermute(quad, TOK, route)
    patch_len = image_rows * devices
    per_patch = patch_len // cache_rows
    current = jnp.where(position // per_patch == patch, moved, stale)
    row_q = jnp.concatenate([image_query, text_query], axis=0)
    row_k = jnp.concatenate([image_key, text_key], axis=0)
    row_v = jnp.concatenate([image_value, text_value], axis=0)
    got = by_head([row_q, row_k, row_v])
    got, current = lax.optimization_barrier((got, current))
    rows = image_rows + text_rows

    def part(first, count, source=got):
        return source[:, first : first + count].reshape(-1, HDIM)

    queries = jnp.concatenate([part(0, image_rows), part(image_rows, text_rows)], axis=0)
    fresh_k = part(rows, image_rows)
    text_k = part(rows + image_rows, text_rows)
    fresh_v = part(2 * rows, image_rows)
    text_v = part(2 * rows + image_rows, text_rows)
    cache_k = part(0, cache_rows, got_cache)
    cache_v = part(cache_rows, cache_rows, got_cache)
    begin = patch * patch_len
    cache_k = lax.dynamic_update_slice_in_dim(cache_k, fresh_k, begin, 0)
    cache_v = lax.dynamic_update_slice_in_dim(cache_v, fresh_v, begin, 0)
    keys = jnp.concatenate([cache_k, text_k], axis=0)
    values = jnp.concatenate([cache_v, text_v], axis=0)
    text_count = text_length[0]
    valid = jnp.concatenate(
        [
            jnp.ones((cache_k.shape[0],), bool),
            jnp.arange(text_k.shape[0], dtype=jnp.int32) < text_count,
        ]
    )
    head_out = attend(queries, keys, values, valid)
    image_heads = broadcast_rows(head_out[:patch_len], devices).reshape(devices, patch_len, HDIM)
    text_heads = lax.all_gather(head_out[patch_len:], TOK, axis=0, tiled=False)
    def from_heads(blocks, weight):
        return jnp.einsum(
            "hrd,hdc->rc",
            blocks[:heads],
            weight.reshape(heads, HDIM, -1),
            preferred_element_type=jnp.float32,
        ).astype(jnp.bfloat16)

    image_back = cols_to_rows(
        from_heads(image_heads, image_from_heads[0]).reshape(devices, image_rows, -1)
    )
    text_back = cols_to_rows(
        from_heads(text_heads, text_from_heads[0]).reshape(devices, text_rows, -1)
    )
    image_mid = image_x + modul[2] * image_back.astype(jnp.float32)
    text_out = (text_x + text_mod[2] * text_back.astype(jnp.float32)).astype(jnp.bfloat16)
    mlp_normed = modulate(image_mid, modul[3], modul[4]).astype(jnp.bfloat16)
    up_weight = image_up[0]
    down_weight = image_down[0]
    hidden = jax.nn.gelu(
        jnp.dot(
            broadcast_rows(mlp_normed, devices),
            up_weight,
            preferred_element_type=jnp.float32,
        ),
        approximate=True,
    ).astype(jnp.bfloat16)
    partial = jnp.dot(hidden, down_weight, preferred_element_type=jnp.float32)
    partial, text_back = lax.optimization_barrier((partial, text_back))
    reduced = jnp.sum(
        lax.all_to_all(
            partial.astype(jnp.bfloat16).reshape(devices, image_rows, width),
            TOK,
            split_axis=0,
            concat_axis=0,
            tiled=True,
        ).astype(jnp.float32),
        axis=0,
    )
    image_out = (image_mid + modul[5] * reduced).astype(jnp.bfloat16)
    text_next = from_behind(text_out, "section", 1)
    image_next = from_behind(image_out, "section", 1)
    final_source = jnp.where(section == last_section, image_out, image_next)
    patch_last = entry_order[0, last_section]
    step_last = lax.dynamic_index_in_dim(step_index[0], patch_last, 0, False)
    final_mod = (
        lax.dynamic_index_in_dim(final_modulation, step_last, 0, False)
        .astype(jnp.float32)
        .reshape(2, width)
    )
    normed = modulate(final_source.astype(jnp.float32), final_mod[0], final_mod[1]).astype(
        jnp.bfloat16
    )
    velocity = jnp.dot(normed, final_weight, preferred_element_type=jnp.float32)
    latents_next = latents[0] + -1.0 / TSTEPS * velocity
    return (image_next[None, None], text_next[None, None], current[None, None], latents_next[None])


def solution(mesh):
    shape = mesh.devices.shape
    split = jax.sharding.Mesh(
        mesh.devices.reshape(shape[:2] + (shape[2] // QUAD, QUAD)),
        ("section", "grp", "ta", "tb"),
    )
    placed = (
        P("section", "grp", TOK, None),
        P("section", "grp", TOK, None),
        P("grp"),
        P("grp", None),
        P("grp", None),
        P("section", None, None),
        P("section", None, None),
        P("section", None, TOK),
        P("section", None, TOK),
        P("section", None, None),
        P("section", None, TOK),
        P("section", None, TOK),
        P("section", None, TOK),
        P("section", TOK, None),
        P("section", "grp", TOK, None),
        P(),
        P(None, "section"),
        P("grp", TOK, "section"),
    )
    return jax.shard_map(
        shards,
        mesh=split,
        in_specs=placed,
        out_specs=(
            P("section", "grp", TOK, None),
            P("section", "grp", TOK, None),
            P("section", "grp", TOK, None),
            P("grp", TOK, "section"),
        ),
        check_vma=False,
    )
```

```python
import jax
import jax.numpy as jnp
from jax import lax
from jax.sharding import PartitionSpec as P

HDIM = 128
TSTEPS = 4


TOK = ("ta", "tb")
QUAD = 4

eps = 1e-06
masked_score = -1e30


def from_behind(block, axis, distance):
    devices = range(lax.axis_size(axis))
    route = [((i - distance) % len(devices), i) for i in devices]
    return lax.ppermute(block, axis, route)


def layer_norm(field):
    mean = jnp.mean(field, axis=-1, keepdims=True)
    centred = field - mean
    spread = jnp.mean(centred * centred, axis=-1, keepdims=True)
    return centred * lax.rsqrt(spread + eps)


def modulate(field, shift, scale):
    return layer_norm(field) * (1.0 + scale) + shift


def head_norm(field, gain):
    height, width = field.shape
    shaped = field.reshape(height, width // HDIM, HDIM)
    power = jnp.mean(shaped * shaped, axis=-1, keepdims=True)
    return (shaped * lax.rsqrt(power + eps) * gain).reshape(height, width)


def attend(queries, keys, values, valid):
    height, width = queries.shape
    heads = width // HDIM
    scores = jnp.einsum(
        "qhd,khd->qhk",
        queries.reshape(height, heads, HDIM),
        keys.reshape(-1, heads, HDIM),
        preferred_element_type=jnp.float32,
    ) * HDIM ** (-0.5)
    scores = jnp.where(valid[None, None, :], scores, masked_score)
    highest = jnp.max(scores, axis=-1, keepdims=True)
    expo = jnp.where(valid[None, None, :], jnp.exp(scores - highest), 0.0)
    total = jnp.sum(expo, axis=-1)
    mixed = jnp.einsum(
        "qhk,khd->qhd",
        expo.astype(jnp.bfloat16),
        values.reshape(-1, heads, HDIM),
        preferred_element_type=jnp.float32,
    )
    return (mixed / total[..., None]).reshape(height, width).astype(jnp.bfloat16)


def cols_to_rows(cols):
    got = lax.all_to_all(cols, TOK, split_axis=0, concat_axis=0, tiled=True)
    count, rows, width = got.shape
    return jnp.transpose(got, (1, 0, 2)).reshape(rows, count * width)


def broadcast_rows(block, devices):
    copies = jnp.broadcast_to(block[None], (devices,) + block.shape)
    got = lax.all_to_all(copies, TOK, split_axis=0, concat_axis=0, tiled=True)
    return got.reshape(-1, block.shape[-1])


def shards(
    image_in,
    text_in,
    text_length,
    entry_order,
    step_index,
    image_modulation,
    text_modulation,
    image_to_heads,
    text_to_heads,
    head_gain,
    image_from_heads,
    text_from_heads,
    image_up,
    image_down,
    stale_cache,
    final_modulation,
    final_weight,
    latents,
):
    section = lax.axis_index("section")
    last_section = lax.axis_size("section") - 1
    position = lax.axis_index("ta") * lax.axis_size("tb") + lax.axis_index("tb")
    devices = lax.axis_size("ta") * lax.axis_size("tb")
    image_x = image_in[0, 0].astype(jnp.float32)
    text_x = text_in[0, 0].astype(jnp.float32)
    image_rows = image_x.shape[0]
    text_rows = text_x.shape[0]
    width = image_x.shape[1]
    patch = lax.dynamic_index_in_dim(entry_order[0], section, 0, False)
    step_now = lax.dynamic_index_in_dim(step_index[0], patch, 0, False)
    modul = (
        lax.dynamic_index_in_dim(image_modulation[0], step_now, 0, False)
        .astype(jnp.float32)
        .reshape(6, width)
    )
    text_mod = (
        lax.dynamic_index_in_dim(text_modulation[0], step_now, 0, False)
        .astype(jnp.float32)
        .reshape(3, width)
    )
    image_normed = modulate(image_x, modul[0], modul[1]).astype(jnp.bfloat16)
    text_normed = modulate(text_x, text_mod[0], text_mod[1]).astype(jnp.bfloat16)
    stale = stale_cache[0, 0]
    cache_rows = stale.shape[0]
    heads = width // HDIM

    def by_head(pieces):
        pack = jnp.concatenate(
            [piece.reshape(piece.shape[0], heads, HDIM) for piece in pieces], axis=0
        )
        pack = jnp.transpose(pack, (1, 0, 2))
        pack = jnp.pad(pack, ((0, devices - heads), (0, 0), (0, 0)))
        return lax.all_to_all(pack, TOK, split_axis=0, concat_axis=0, tiled=True)

    every_text = lax.all_gather(text_normed, TOK, axis=0, tiled=True)
    every_image = broadcast_rows(image_normed, devices)
    stale_late, every_image = lax.optimization_barrier((stale, every_image))
    got_cache = by_head([stale_late[:, :width], stale_late[:, width:]])
    image_cols = jnp.dot(every_image, image_to_heads[0], preferred_element_type=jnp.float32)
    text_cols = jnp.dot(every_text, text_to_heads[0], preferred_element_type=jnp.float32)
    proj = cols_to_rows(
        jnp.concatenate(
            [
                image_cols.reshape(devices, image_rows, -1),
                text_cols.reshape(devices, text_rows, -1),
            ],
            axis=1,
        ).astype(jnp.bfloat16)
    )
    image_proj = proj[:image_rows]
    text_proj = proj[image_rows:]
    gains = head_gain[0]
    image_query = head_norm(image_proj[:, :width].astype(jnp.float32), gains[0]).astype(
        jnp.bfloat16
    )
    image_key = head_norm(image_proj[:, width : 2 * width].astype(jnp.float32), gains[1]).astype(
        jnp.bfloat16
    )
    text_query = head_norm(text_proj[:, :width].astype(jnp.float32), gains[2]).astype(jnp.bfloat16)
    text_key = head_norm(text_proj[:, width : 2 * width].astype(jnp.float32), gains[3]).astype(
        jnp.bfloat16
    )
    image_value = image_proj[:, 2 * width :]
    text_value = text_proj[:, 2 * width :]
    fresh_image = jnp.concatenate([image_key, image_value], axis=1)
    group = lax.axis_size("tb")
    blocks = devices // group
    mine = lax.axis_index("tb")
    quad = [fresh_image]
    for shift in range(1, group):
        turn = [(j * group + b, j * group + (b + shift) % group) for j in range(blocks) for b in range(group)]
        quad.append(lax.ppermute(fresh_image, TOK, turn))
    quad = jnp.stack(quad)
    quad = jnp.take(quad, (mine - jnp.arange(group)) % group, axis=0).reshape(-1, fresh_image.shape[1])
    route = [(j * group + b, j + blocks * b) for j in range(blocks) for b in range(group)]
    moved = lax.ppermute(quad, TOK, route)
    patch_len = image_rows * devices
    per_patch = patch_len // cache_rows
    current = jnp.where(position // per_patch == patch, moved, stale)
    row_q = jnp.concatenate([image_query, text_query], axis=0)
    row_k = jnp.concatenate([image_key, text_key], axis=0)
    row_v = jnp.concatenate([image_value, text_value], axis=0)
    got = by_head([row_q, row_k, row_v])
    got, current = lax.optimization_barrier((got, current))
    rows = image_rows + text_rows

    def part(first, count, source=got):
        return source[:, first : first + count].reshape(-1, HDIM)

    queries = jnp.concatenate([part(0, image_rows), part(image_rows, text_rows)], axis=0)
    fresh_k = part(rows, image_rows)
    text_k = part(rows + image_rows, text_rows)
    fresh_v = part(2 * rows, image_rows)
    text_v = part(2 * rows + image_rows, text_rows)
    cache_k = part(0, cache_rows, got_cache)
    cache_v = part(cache_rows, cache_rows, got_cache)
    begin = patch * patch_len
    cache_k = lax.dynamic_update_slice_in_dim(cache_k, fresh_k, begin, 0)
    cache_v = lax.dynamic_update_slice_in_dim(cache_v, fresh_v, begin, 0)
    keys = jnp.concatenate([cache_k, text_k], axis=0)
    values = jnp.concatenate([cache_v, text_v], axis=0)
    text_count = text_length[0]
    valid = jnp.concatenate(
        [
            jnp.ones((cache_k.shape[0],), bool),
            jnp.arange(text_k.shape[0], dtype=jnp.int32) < text_count,
        ]
    )
    head_out = attend(queries, keys, values, valid)
    image_heads = broadcast_rows(head_out[:patch_len], devices).reshape(devices, patch_len, HDIM)
    text_heads = lax.all_gather(head_out[patch_len:], TOK, axis=0, tiled=False)
    def from_heads(blocks, weight):
        return jnp.einsum(
            "hrd,hdc->rc",
            blocks[:heads],
            weight.reshape(heads, HDIM, -1),
            preferred_element_type=jnp.float32,
        ).astype(jnp.bfloat16)

    image_back = cols_to_rows(
        from_heads(image_heads, image_from_heads[0]).reshape(devices, image_rows, -1)
    )
    text_back = cols_to_rows(
        from_heads(text_heads, text_from_heads[0]).reshape(devices, text_rows, -1)
    )
    image_mid = image_x + modul[2] * image_back.astype(jnp.float32)
    text_out = (text_x + text_mod[2] * text_back.astype(jnp.float32)).astype(jnp.bfloat16)
    mlp_normed = modulate(image_mid, modul[3], modul[4]).astype(jnp.bfloat16)
    up_weight = image_up[0]
    down_weight = image_down[0]
    hidden = jax.nn.gelu(
        jnp.dot(
            broadcast_rows(mlp_normed, devices),
            up_weight,
            preferred_element_type=jnp.float32,
        ),
        approximate=True,
    ).astype(jnp.bfloat16)
    partial = jnp.dot(hidden, down_weight, preferred_element_type=jnp.float32)
    partial, text_back = lax.optimization_barrier((partial, text_back))
    reduced = jnp.sum(
        lax.all_to_all(
            partial.astype(jnp.bfloat16).reshape(devices, image_rows, width),
            TOK,
            split_axis=0,
            concat_axis=0,
            tiled=True,
        ).astype(jnp.float32),
        axis=0,
    )
    image_out = (image_mid + modul[5] * reduced).astype(jnp.bfloat16)
    text_next = from_behind(text_out, "section", 1)
    image_next = from_behind(image_out, "section", 1)
    final_source = jnp.where(section == last_section, image_out, image_next)
    patch_last = entry_order[0, last_section]
    step_last = lax.dynamic_index_in_dim(step_index[0], patch_last, 0, False)
    final_mod = (
        lax.dynamic_index_in_dim(final_modulation, step_last, 0, False)
        .astype(jnp.float32)
        .reshape(2, width)
    )
    normed = modulate(final_source.astype(jnp.float32), final_mod[0], final_mod[1]).astype(
        jnp.bfloat16
    )
    velocity = jnp.dot(normed, final_weight, preferred_element_type=jnp.float32)
    latents_next = latents[0] + -1.0 / TSTEPS * velocity
    return (image_next[None, None], text_next[None, None], current[None, None], latents_next[None])


def solution(mesh):
    shape = mesh.devices.shape
    split = jax.sharding.Mesh(
        mesh.devices.reshape(shape[:2] + (shape[2] // QUAD, QUAD)),
        ("section", "grp", "ta", "tb"),
    )
    placed = (
        P("section", "grp", TOK, None),
        P("section", "grp", TOK, None),
        P("grp"),
        P("grp", None),
        P("grp", None),
        P("section", None, None),
        P("section", None, None),
        P("section", None, TOK),
        P("section", None, TOK),
        P("section", None, None),
        P("section", None, TOK),
        P("section", None, TOK),
        P("section", None, TOK),
        P("section", TOK, None),
        P("section", "grp", TOK, None),
        P(),
        P(None, "section"),
        P("grp", TOK, "section"),
    )
    return jax.shard_map(
        shards,
        mesh=split,
        in_specs=placed,
        out_specs=(
            P("section", "grp", TOK, None),
            P("section", "grp", TOK, None),
            P("section", "grp", TOK, None),
            P("grp", TOK, "section"),
        ),
        check_vma=False,
    )
```

```python
import jax
import jax.numpy as jnp
from jax import lax
from jax.sharding import PartitionSpec as P

HDIM = 128
TSTEPS = 4


TOK = ("ta", "tb")
QUAD = 4

eps = 1e-06
masked_score = -1e30


def from_behind(block, axis, distance):
    devices = range(lax.axis_size(axis))
    route = [((i - distance) % len(devices), i) for i in devices]
    return lax.ppermute(block, axis, route)


def layer_norm(field):
    mean = jnp.mean(field, axis=-1, keepdims=True)
    centred = field - mean
    spread = jnp.mean(centred * centred, axis=-1, keepdims=True)
    return centred * lax.rsqrt(spread + eps)


def modulate(field, shift, scale):
    return layer_norm(field) * (1.0 + scale) + shift


def head_norm(field, gain):
    height, width = field.shape
    shaped = field.reshape(height, width // HDIM, HDIM)
    power = jnp.mean(shaped * shaped, axis=-1, keepdims=True)
    return (shaped * lax.rsqrt(power + eps) * gain).reshape(height, width)


def attend(queries, keys, values, valid):
    height, width = queries.shape
    heads = width // HDIM
    scores = jnp.einsum(
        "qhd,khd->qhk",
        queries.reshape(height, heads, HDIM),
        keys.reshape(-1, heads, HDIM),
        preferred_element_type=jnp.float32,
    ) * HDIM ** (-0.5)
    scores = jnp.where(valid[None, None, :], scores, masked_score)
    highest = jnp.max(scores, axis=-1, keepdims=True)
    expo = jnp.where(valid[None, None, :], jnp.exp(scores - highest), 0.0)
    total = jnp.sum(expo, axis=-1)
    mixed = jnp.einsum(
        "qhk,khd->qhd",
        expo.astype(jnp.bfloat16),
        values.reshape(-1, heads, HDIM),
        preferred_element_type=jnp.float32,
    )
    return (mixed / total[..., None]).reshape(height, width).astype(jnp.bfloat16)


def cols_to_rows(cols):
    got = lax.all_to_all(cols, TOK, split_axis=0, concat_axis=0, tiled=True)
    count, rows, width = got.shape
    return jnp.transpose(got, (1, 0, 2)).reshape(rows, count * width)


def broadcast_rows(block, devices):
    copies = jnp.broadcast_to(block[None], (devices,) + block.shape)
    got = lax.all_to_all(copies, TOK, split_axis=0, concat_axis=0, tiled=True)
    return got.reshape(-1, block.shape[-1])


def shards(
    image_in,
    text_in,
    text_length,
    entry_order,
    step_index,
    image_modulation,
    text_modulation,
    image_to_heads,
    text_to_heads,
    head_gain,
    image_from_heads,
    text_from_heads,
    image_up,
    image_down,
    stale_cache,
    final_modulation,
    final_weight,
    latents,
):
    section = lax.axis_index("section")
    last_section = lax.axis_size("section") - 1
    position = lax.axis_index("ta") * lax.axis_size("tb") + lax.axis_index("tb")
    devices = lax.axis_size("ta") * lax.axis_size("tb")
    image_x = image_in[0, 0].astype(jnp.float32)
    text_x = text_in[0, 0].astype(jnp.float32)
    image_rows = image_x.shape[0]
    text_rows = text_x.shape[0]
    width = image_x.shape[1]
    patch = lax.dynamic_index_in_dim(entry_order[0], section, 0, False)
    step_now = lax.dynamic_index_in_dim(step_index[0], patch, 0, False)
    modul = (
        lax.dynamic_index_in_dim(image_modulation[0], step_now, 0, False)
        .astype(jnp.float32)
        .reshape(6, width)
    )
    text_mod = (
        lax.dynamic_index_in_dim(text_modulation[0], step_now, 0, False)
        .astype(jnp.float32)
        .reshape(3, width)
    )
    image_normed = modulate(image_x, modul[0], modul[1]).astype(jnp.bfloat16)
    text_normed = modulate(text_x, text_mod[0], text_mod[1]).astype(jnp.bfloat16)
    stale = stale_cache[0, 0]
    cache_rows = stale.shape[0]
    heads = width // HDIM

    def by_head(pieces):
        pack = jnp.concatenate(
            [piece.reshape(piece.shape[0], heads, HDIM) for piece in pieces], axis=0
        )
        pack = jnp.transpose(pack, (1, 0, 2))
        pack = jnp.pad(pack, ((0, devices - heads), (0, 0), (0, 0)))
        return lax.all_to_all(pack, TOK, split_axis=0, concat_axis=0, tiled=True)

    every_text = lax.all_gather(text_normed, TOK, axis=0, tiled=True)
    every_image = broadcast_rows(image_normed, devices)
    stale_late, every_image = lax.optimization_barrier((stale, every_image))
    got_cache = by_head([stale_late[:, :width], stale_late[:, width:]])
    image_cols = jnp.dot(every_image, image_to_heads[0], preferred_element_type=jnp.float32)
    text_cols = jnp.dot(every_text, text_to_heads[0], preferred_element_type=jnp.float32)
    image_proj = cols_to_rows(image_cols.astype(jnp.bfloat16).reshape(devices, image_rows, -1))
    text_proj = cols_to_rows(text_cols.astype(jnp.bfloat16).reshape(devices, text_rows, -1))
    gains = head_gain[0]
    image_query = head_norm(image_proj[:, :width].astype(jnp.float32), gains[0]).astype(
        jnp.bfloat16
    )
    image_key = head_norm(image_proj[:, width : 2 * width].astype(jnp.float32), gains[1]).astype(
        jnp.bfloat16
    )
    text_query = head_norm(text_proj[:, :width].astype(jnp.float32), gains[2]).astype(jnp.bfloat16)
    text_key = head_norm(text_proj[:, width : 2 * width].astype(jnp.float32), gains[3]).astype(
        jnp.bfloat16
    )
    image_value = image_proj[:, 2 * width :]
    text_value = text_proj[:, 2 * width :]
    fresh_image = jnp.concatenate([image_key, image_value], axis=1)
    group = lax.axis_size("tb")
    blocks = devices // group
    mine = lax.axis_index("tb")
    quad = [fresh_image]
    for shift in range(1, group):
        turn = [(j * group + b, j * group + (b + shift) % group) for j in range(blocks) for b in range(group)]
        quad.append(lax.ppermute(fresh_image, TOK, turn))
    quad = jnp.stack(quad)
    quad = jnp.take(quad, (mine - jnp.arange(group)) % group, axis=0).reshape(-1, fresh_image.shape[1])
    route = [(j * group + b, j + blocks * b) for j in range(blocks) for b in range(group)]
    moved = lax.ppermute(quad, TOK, route)
    patch_len = image_rows * devices
    per_patch = patch_len // cache_rows
    current = jnp.where(position // per_patch == patch, moved, stale)
    row_q = jnp.concatenate([image_query, text_query], axis=0)
    row_k = jnp.concatenate([image_key, text_key], axis=0)
    row_v = jnp.concatenate([image_value, text_value], axis=0)
    got = by_head([row_q, row_k, row_v])
    got, current = lax.optimization_barrier((got, current))
    rows = image_rows + text_rows

    def part(first, count, source=got):
        return source[:, first : first + count].reshape(-1, HDIM)

    queries = jnp.concatenate([part(0, image_rows), part(image_rows, text_rows)], axis=0)
    fresh_k = part(rows, image_rows)
    text_k = part(rows + image_rows, text_rows)
    fresh_v = part(2 * rows, image_rows)
    text_v = part(2 * rows + image_rows, text_rows)
    cache_k = part(0, cache_rows, got_cache)
    cache_v = part(cache_rows, cache_rows, got_cache)
    begin = patch * patch_len
    cache_k = lax.dynamic_update_slice_in_dim(cache_k, fresh_k, begin, 0)
    cache_v = lax.dynamic_update_slice_in_dim(cache_v, fresh_v, begin, 0)
    keys = jnp.concatenate([cache_k, text_k], axis=0)
    values = jnp.concatenate([cache_v, text_v], axis=0)
    text_count = text_length[0]
    valid = jnp.concatenate(
        [
            jnp.ones((cache_k.shape[0],), bool),
            jnp.arange(text_k.shape[0], dtype=jnp.int32) < text_count,
        ]
    )
    head_out = attend(queries, keys, values, valid)
    image_heads = broadcast_rows(head_out[:patch_len], devices).reshape(devices, patch_len, HDIM)
    text_heads = lax.all_gather(head_out[patch_len:], TOK, axis=0, tiled=False)
    def from_heads(blocks, weight):
        return jnp.einsum(
            "hrd,hdc->rc",
            blocks[:heads],
            weight.reshape(heads, HDIM, -1),
            preferred_element_type=jnp.float32,
        ).astype(jnp.bfloat16)

    image_back = cols_to_rows(
        from_heads(image_heads, image_from_heads[0]).reshape(devices, image_rows, -1)
    )
    text_back = cols_to_rows(
        from_heads(text_heads, text_from_heads[0]).reshape(devices, text_rows, -1)
    )
    image_mid = image_x + modul[2] * image_back.astype(jnp.float32)
    text_out = (text_x + text_mod[2] * text_back.astype(jnp.float32)).astype(jnp.bfloat16)
    mlp_normed = modulate(image_mid, modul[3], modul[4]).astype(jnp.bfloat16)
    up_weight = image_up[0]
    down_weight = image_down[0]
    hidden = jax.nn.gelu(
        jnp.dot(
            broadcast_rows(mlp_normed, devices),
            up_weight,
            preferred_element_type=jnp.float32,
        ),
        approximate=True,
    ).astype(jnp.bfloat16)
    partial = jnp.dot(hidden, down_weight, preferred_element_type=jnp.float32)
    partial, text_back = lax.optimization_barrier((partial, text_back))
    reduced = jnp.sum(
        lax.all_to_all(
            partial.astype(jnp.bfloat16).reshape(devices, image_rows, width),
            TOK,
            split_axis=0,
            concat_axis=0,
            tiled=True,
        ).astype(jnp.float32),
        axis=0,
    )
    image_out = (image_mid + modul[5] * reduced).astype(jnp.bfloat16)
    text_next = from_behind(text_out, "section", 1)
    image_next = from_behind(image_out, "section", 1)
    final_source = jnp.where(section == last_section, image_out, image_next)
    patch_last = entry_order[0, last_section]
    step_last = lax.dynamic_index_in_dim(step_index[0], patch_last, 0, False)
    final_mod = (
        lax.dynamic_index_in_dim(final_modulation, step_last, 0, False)
        .astype(jnp.float32)
        .reshape(2, width)
    )
    normed = modulate(final_source.astype(jnp.float32), final_mod[0], final_mod[1]).astype(
        jnp.bfloat16
    )
    velocity = jnp.dot(normed, final_weight, preferred_element_type=jnp.float32)
    latents_next = latents[0] + -1.0 / TSTEPS * velocity
    return (image_next[None, None], text_next[None, None], current[None, None], latents_next[None])


def solution(mesh):
    shape = mesh.devices.shape
    split = jax.sharding.Mesh(
        mesh.devices.reshape(shape[:2] + (shape[2] // QUAD, QUAD)),
        ("section", "grp", "ta", "tb"),
    )
    placed = (
        P("section", "grp", TOK, None),
        P("section", "grp", TOK, None),
        P("grp"),
        P("grp", None),
        P("grp", None),
        P("section", None, None),
        P("section", None, None),
        P("section", None, TOK),
        P("section", None, TOK),
        P("section", None, None),
        P("section", None, TOK),
        P("section", None, TOK),
        P("section", None, TOK),
        P("section", TOK, None),
        P("section", "grp", TOK, None),
        P(),
        P(None, "section"),
        P("grp", TOK, "section"),
    )
    return jax.shard_map(
        shards,
        mesh=split,
        in_specs=placed,
        out_specs=(
            P("section", "grp", TOK, None),
            P("section", "grp", TOK, None),
            P("section", "grp", TOK, None),
            P("grp", TOK, "section"),
        ),
        check_vma=False,
    )
```

```python
import jax
import jax.numpy as jnp
from jax import lax
from jax.sharding import PartitionSpec as P

HDIM = 128
TSTEPS = 4


TOK = ("ta", "tb")
QUAD = 4

eps = 1e-06
masked_score = -1e30


def from_behind(block, axis, distance):
    devices = range(lax.axis_size(axis))
    route = [((i - distance) % len(devices), i) for i in devices]
    return lax.ppermute(block, axis, route)


def layer_norm(field):
    mean = jnp.mean(field, axis=-1, keepdims=True)
    centred = field - mean
    spread = jnp.mean(centred * centred, axis=-1, keepdims=True)
    return centred * lax.rsqrt(spread + eps)


def modulate(field, shift, scale):
    return layer_norm(field) * (1.0 + scale) + shift


def head_norm(field, gain):
    height, width = field.shape
    shaped = field.reshape(height, width // HDIM, HDIM)
    power = jnp.mean(shaped * shaped, axis=-1, keepdims=True)
    return (shaped * lax.rsqrt(power + eps) * gain).reshape(height, width)


def attend(queries, keys, values, valid):
    height, width = queries.shape
    heads = width // HDIM
    scores = jnp.einsum(
        "qhd,khd->qhk",
        queries.reshape(height, heads, HDIM),
        keys.reshape(-1, heads, HDIM),
        preferred_element_type=jnp.float32,
    ) * HDIM ** (-0.5)
    scores = jnp.where(valid[None, None, :], scores, masked_score)
    highest = jnp.max(scores, axis=-1, keepdims=True)
    expo = jnp.where(valid[None, None, :], jnp.exp(scores - highest), 0.0)
    total = jnp.sum(expo, axis=-1)
    mixed = jnp.einsum(
        "qhk,khd->qhd",
        expo.astype(jnp.bfloat16),
        values.reshape(-1, heads, HDIM),
        preferred_element_type=jnp.float32,
    )
    return (mixed / total[..., None]).reshape(height, width).astype(jnp.bfloat16)


def cols_to_rows(cols):
    got = lax.all_to_all(cols, TOK, split_axis=0, concat_axis=0, tiled=True)
    count, rows, width = got.shape
    return jnp.transpose(got, (1, 0, 2)).reshape(rows, count * width)


def broadcast_rows(block, devices):
    copies = jnp.broadcast_to(block[None], (devices,) + block.shape)
    got = lax.all_to_all(copies, TOK, split_axis=0, concat_axis=0, tiled=True)
    return got.reshape(-1, block.shape[-1])


def shards(
    image_in,
    text_in,
    text_length,
    entry_order,
    step_index,
    image_modulation,
    text_modulation,
    image_to_heads,
    text_to_heads,
    head_gain,
    image_from_heads,
    text_from_heads,
    image_up,
    image_down,
    stale_cache,
    final_modulation,
    final_weight,
    latents,
):
    section = lax.axis_index("section")
    last_section = lax.axis_size("section") - 1
    position = lax.axis_index("ta") * lax.axis_size("tb") + lax.axis_index("tb")
    devices = lax.axis_size("ta") * lax.axis_size("tb")
    image_x = image_in[0, 0].astype(jnp.float32)
    text_x = text_in[0, 0].astype(jnp.float32)
    image_rows = image_x.shape[0]
    text_rows = text_x.shape[0]
    width = image_x.shape[1]
    patch = lax.dynamic_index_in_dim(entry_order[0], section, 0, False)
    step_now = lax.dynamic_index_in_dim(step_index[0], patch, 0, False)
    modul = (
        lax.dynamic_index_in_dim(image_modulation[0], step_now, 0, False)
        .astype(jnp.float32)
        .reshape(6, width)
    )
    text_mod = (
        lax.dynamic_index_in_dim(text_modulation[0], step_now, 0, False)
        .astype(jnp.float32)
        .reshape(3, width)
    )
    image_normed = modulate(image_x, modul[0], modul[1]).astype(jnp.bfloat16)
    text_normed = modulate(text_x, text_mod[0], text_mod[1]).astype(jnp.bfloat16)
    stale = stale_cache[0, 0]
    cache_rows = stale.shape[0]
    heads = width // HDIM

    def by_head(pieces):
        pack = jnp.concatenate(
            [piece.reshape(piece.shape[0], heads, HDIM) for piece in pieces], axis=0
        )
        pack = jnp.transpose(pack, (1, 0, 2))
        pack = jnp.pad(pack, ((0, devices - heads), (0, 0), (0, 0)))
        return lax.all_to_all(pack, TOK, split_axis=0, concat_axis=0, tiled=True)

    every_text = lax.all_gather(text_normed, TOK, axis=0, tiled=True)
    every_image = broadcast_rows(image_normed, devices)
    stale_late, every_image = lax.optimization_barrier((stale, every_image))
    got_cache = by_head([stale_late[:, :width], stale_late[:, width:]])
    image_cols = jnp.dot(every_image, image_to_heads[0], preferred_element_type=jnp.float32)
    got_cache, every_text = lax.optimization_barrier((got_cache, every_text))
    text_cols = jnp.dot(every_text, text_to_heads[0], preferred_element_type=jnp.float32)
    image_proj = cols_to_rows(image_cols.astype(jnp.bfloat16).reshape(devices, image_rows, -1))
    text_proj = cols_to_rows(text_cols.astype(jnp.bfloat16).reshape(devices, text_rows, -1))
    gains = head_gain[0]
    image_query = head_norm(image_proj[:, :width].astype(jnp.float32), gains[0]).astype(
        jnp.bfloat16
    )
    image_key = head_norm(image_proj[:, width : 2 * width].astype(jnp.float32), gains[1]).astype(
        jnp.bfloat16
    )
    text_query = head_norm(text_proj[:, :width].astype(jnp.float32), gains[2]).astype(jnp.bfloat16)
    text_key = head_norm(text_proj[:, width : 2 * width].astype(jnp.float32), gains[3]).astype(
        jnp.bfloat16
    )
    image_value = image_proj[:, 2 * width :]
    text_value = text_proj[:, 2 * width :]
    fresh_image = jnp.concatenate([image_key, image_value], axis=1)
    group = lax.axis_size("tb")
    blocks = devices // group
    mine = lax.axis_index("tb")
    quad = [fresh_image]
    for shift in range(1, group):
        turn = [(j * group + b, j * group + (b + shift) % group) for j in range(blocks) for b in range(group)]
        quad.append(lax.ppermute(fresh_image, TOK, turn))
    quad = jnp.stack(quad)
    quad = jnp.take(quad, (mine - jnp.arange(group)) % group, axis=0).reshape(-1, fresh_image.shape[1])
    route = [(j * group + b, j + blocks * b) for j in range(blocks) for b in range(group)]
    moved = lax.ppermute(quad, TOK, route)
    patch_len = image_rows * devices
    per_patch = patch_len // cache_rows
    current = jnp.where(position // per_patch == patch, moved, stale)
    row_q = jnp.concatenate([image_query, text_query], axis=0)
    row_k = jnp.concatenate([image_key, text_key], axis=0)
    row_v = jnp.concatenate([image_value, text_value], axis=0)
    got = by_head([row_q, row_k, row_v])
    got, current = lax.optimization_barrier((got, current))
    rows = image_rows + text_rows

    def part(first, count, source=got):
        return source[:, first : first + count].reshape(-1, HDIM)

    queries = jnp.concatenate([part(0, image_rows), part(image_rows, text_rows)], axis=0)
    fresh_k = part(rows, image_rows)
    text_k = part(rows + image_rows, text_rows)
    fresh_v = part(2 * rows, image_rows)
    text_v = part(2 * rows + image_rows, text_rows)
    cache_k = part(0, cache_rows, got_cache)
    cache_v = part(cache_rows, cache_rows, got_cache)
    begin = patch * patch_len
    cache_k = lax.dynamic_update_slice_in_dim(cache_k, fresh_k, begin, 0)
    cache_v = lax.dynamic_update_slice_in_dim(cache_v, fresh_v, begin, 0)
    keys = jnp.concatenate([cache_k, text_k], axis=0)
    values = jnp.concatenate([cache_v, text_v], axis=0)
    text_count = text_length[0]
    valid = jnp.concatenate(
        [
            jnp.ones((cache_k.shape[0],), bool),
            jnp.arange(text_k.shape[0], dtype=jnp.int32) < text_count,
        ]
    )
    head_out = attend(queries, keys, values, valid)
    image_heads = broadcast_rows(head_out[:patch_len], devices).reshape(devices, patch_len, HDIM)
    text_heads = lax.all_gather(head_out[patch_len:], TOK, axis=0, tiled=False)
    def from_heads(blocks, weight):
        return jnp.einsum(
            "hrd,hdc->rc",
            blocks[:heads],
            weight.reshape(heads, HDIM, -1),
            preferred_element_type=jnp.float32,
        ).astype(jnp.bfloat16)

    image_back = cols_to_rows(
        from_heads(image_heads, image_from_heads[0]).reshape(devices, image_rows, -1)
    )
    text_back = cols_to_rows(
        from_heads(text_heads, text_from_heads[0]).reshape(devices, text_rows, -1)
    )
    image_mid = image_x + modul[2] * image_back.astype(jnp.float32)
    text_out = (text_x + text_mod[2] * text_back.astype(jnp.float32)).astype(jnp.bfloat16)
    mlp_normed = modulate(image_mid, modul[3], modul[4]).astype(jnp.bfloat16)
    up_weight = image_up[0]
    down_weight = image_down[0]
    hidden = jax.nn.gelu(
        jnp.dot(
            broadcast_rows(mlp_normed, devices),
            up_weight,
            preferred_element_type=jnp.float32,
        ),
        approximate=True,
    ).astype(jnp.bfloat16)
    partial = jnp.dot(hidden, down_weight, preferred_element_type=jnp.float32)
    partial, text_back = lax.optimization_barrier((partial, text_back))
    reduced = jnp.sum(
        lax.all_to_all(
            partial.astype(jnp.bfloat16).reshape(devices, image_rows, width),
            TOK,
            split_axis=0,
            concat_axis=0,
            tiled=True,
        ).astype(jnp.float32),
        axis=0,
    )
    image_out = (image_mid + modul[5] * reduced).astype(jnp.bfloat16)
    text_next = from_behind(text_out, "section", 1)
    image_next = from_behind(image_out, "section", 1)
    final_source = jnp.where(section == last_section, image_out, image_next)
    patch_last = entry_order[0, last_section]
    step_last = lax.dynamic_index_in_dim(step_index[0], patch_last, 0, False)
    final_mod = (
        lax.dynamic_index_in_dim(final_modulation, step_last, 0, False)
        .astype(jnp.float32)
        .reshape(2, width)
    )
    normed = modulate(final_source.astype(jnp.float32), final_mod[0], final_mod[1]).astype(
        jnp.bfloat16
    )
    velocity = jnp.dot(normed, final_weight, preferred_element_type=jnp.float32)
    latents_next = latents[0] + -1.0 / TSTEPS * velocity
    return (image_next[None, None], text_next[None, None], current[None, None], latents_next[None])


def solution(mesh):
    shape = mesh.devices.shape
    split = jax.sharding.Mesh(
        mesh.devices.reshape(shape[:2] + (shape[2] // QUAD, QUAD)),
        ("section", "grp", "ta", "tb"),
    )
    placed = (
        P("section", "grp", TOK, None),
        P("section", "grp", TOK, None),
        P("grp"),
        P("grp", None),
        P("grp", None),
        P("section", None, None),
        P("section", None, None),
        P("section", None, TOK),
        P("section", None, TOK),
        P("section", None, None),
        P("section", None, TOK),
        P("section", None, TOK),
        P("section", None, TOK),
        P("section", TOK, None),
        P("section", "grp", TOK, None),
        P(),
        P(None, "section"),
        P("grp", TOK, "section"),
    )
    return jax.shard_map(
        shards,
        mesh=split,
        in_specs=placed,
        out_specs=(
            P("section", "grp", TOK, None),
            P("section", "grp", TOK, None),
            P("section", "grp", TOK, None),
            P("grp", TOK, "section"),
        ),
        check_vma=False,
    )
```

```python
import jax
import jax.numpy as jnp
from jax import lax
from jax.sharding import PartitionSpec as P

HDIM = 128
TSTEPS = 4


TOK = ("ta", "tb")
QUAD = 4

eps = 1e-06
masked_score = -1e30


def from_behind(block, axis, distance):
    devices = range(lax.axis_size(axis))
    route = [((i - distance) % len(devices), i) for i in devices]
    return lax.ppermute(block, axis, route)


def layer_norm(field):
    mean = jnp.mean(field, axis=-1, keepdims=True)
    centred = field - mean
    spread = jnp.mean(centred * centred, axis=-1, keepdims=True)
    return centred * lax.rsqrt(spread + eps)


def modulate(field, shift, scale):
    return layer_norm(field) * (1.0 + scale) + shift


def head_norm(field, gain):
    height, width = field.shape
    shaped = field.reshape(height, width // HDIM, HDIM)
    power = jnp.mean(shaped * shaped, axis=-1, keepdims=True)
    return (shaped * lax.rsqrt(power + eps) * gain).reshape(height, width)


def attend(queries, keys, values, valid):
    height, width = queries.shape
    heads = width // HDIM
    scores = jnp.einsum(
        "qhd,khd->qhk",
        queries.reshape(height, heads, HDIM),
        keys.reshape(-1, heads, HDIM),
        preferred_element_type=jnp.float32,
    ) * HDIM ** (-0.5)
    scores = jnp.where(valid[None, None, :], scores, masked_score)
    highest = jnp.max(scores, axis=-1, keepdims=True)
    expo = jnp.where(valid[None, None, :], jnp.exp(scores - highest), 0.0)
    total = jnp.sum(expo, axis=-1)
    mixed = jnp.einsum(
        "qhk,khd->qhd",
        expo.astype(jnp.bfloat16),
        values.reshape(-1, heads, HDIM),
        preferred_element_type=jnp.float32,
    )
    return (mixed / total[..., None]).reshape(height, width).astype(jnp.bfloat16)


def cols_to_rows(cols):
    got = lax.all_to_all(cols, TOK, split_axis=0, concat_axis=0, tiled=True)
    count, rows, width = got.shape
    return jnp.transpose(got, (1, 0, 2)).reshape(rows, count * width)


def broadcast_rows(block, devices):
    copies = jnp.broadcast_to(block[None], (devices,) + block.shape)
    got = lax.all_to_all(copies, TOK, split_axis=0, concat_axis=0, tiled=True)
    return got.reshape(-1, block.shape[-1])


def shards(
    image_in,
    text_in,
    text_length,
    entry_order,
    step_index,
    image_modulation,
    text_modulation,
    image_to_heads,
    text_to_heads,
    head_gain,
    image_from_heads,
    text_from_heads,
    image_up,
    image_down,
    stale_cache,
    final_modulation,
    final_weight,
    latents,
):
    section = lax.axis_index("section")
    last_section = lax.axis_size("section") - 1
    position = lax.axis_index("ta") * lax.axis_size("tb") + lax.axis_index("tb")
    devices = lax.axis_size("ta") * lax.axis_size("tb")
    image_x = image_in[0, 0].astype(jnp.float32)
    text_x = text_in[0, 0].astype(jnp.float32)
    image_rows = image_x.shape[0]
    text_rows = text_x.shape[0]
    width = image_x.shape[1]
    patch = lax.dynamic_index_in_dim(entry_order[0], section, 0, False)
    step_now = lax.dynamic_index_in_dim(step_index[0], patch, 0, False)
    modul = (
        lax.dynamic_index_in_dim(image_modulation[0], step_now, 0, False)
        .astype(jnp.float32)
        .reshape(6, width)
    )
    text_mod = (
        lax.dynamic_index_in_dim(text_modulation[0], step_now, 0, False)
        .astype(jnp.float32)
        .reshape(3, width)
    )
    image_normed = modulate(image_x, modul[0], modul[1]).astype(jnp.bfloat16)
    text_normed = modulate(text_x, text_mod[0], text_mod[1]).astype(jnp.bfloat16)
    stale = stale_cache[0, 0]
    cache_rows = stale.shape[0]
    heads = width // HDIM

    def by_head(pieces):
        pack = jnp.concatenate(
            [piece.reshape(piece.shape[0], heads, HDIM) for piece in pieces], axis=0
        )
        pack = jnp.transpose(pack, (1, 0, 2))
        pack = jnp.pad(pack, ((0, devices - heads), (0, 0), (0, 0)))
        return lax.all_to_all(pack, TOK, split_axis=0, concat_axis=0, tiled=True)

    every_text = lax.all_gather(text_normed, TOK, axis=0, tiled=True)
    every_image = broadcast_rows(image_normed, devices)
    stale_late, every_image = lax.optimization_barrier((stale, every_image))
    got_cache = by_head([stale_late[:, :width], stale_late[:, width:]])
    image_cols = jnp.dot(every_image, image_to_heads[0], preferred_element_type=jnp.float32)
    got_cache, every_text = lax.optimization_barrier((got_cache, every_text))
    image_proj = cols_to_rows(image_cols.astype(jnp.bfloat16).reshape(devices, image_rows, -1))
    gains = head_gain[0]
    image_query = head_norm(image_proj[:, :width].astype(jnp.float32), gains[0]).astype(
        jnp.bfloat16
    )
    image_key = head_norm(image_proj[:, width : 2 * width].astype(jnp.float32), gains[1]).astype(
        jnp.bfloat16
    )
    image_value = image_proj[:, 2 * width :]
    got_image = by_head([image_query, image_key, image_value])
    got_image, every_text = lax.optimization_barrier((got_image, every_text))
    text_cols = jnp.dot(every_text, text_to_heads[0], preferred_element_type=jnp.float32)
    text_proj = cols_to_rows(text_cols.astype(jnp.bfloat16).reshape(devices, text_rows, -1))
    text_query = head_norm(text_proj[:, :width].astype(jnp.float32), gains[2]).astype(jnp.bfloat16)
    text_key = head_norm(text_proj[:, width : 2 * width].astype(jnp.float32), gains[3]).astype(
        jnp.bfloat16
    )
    text_value = text_proj[:, 2 * width :]
    fresh_image = jnp.concatenate([image_key, image_value], axis=1)
    group = lax.axis_size("tb")
    blocks = devices // group
    mine = lax.axis_index("tb")
    quad = [fresh_image]
    for shift in range(1, group):
        turn = [(j * group + b, j * group + (b + shift) % group) for j in range(blocks) for b in range(group)]
        quad.append(lax.ppermute(fresh_image, TOK, turn))
    quad = jnp.stack(quad)
    quad = jnp.take(quad, (mine - jnp.arange(group)) % group, axis=0).reshape(-1, fresh_image.shape[1])
    route = [(j * group + b, j + blocks * b) for j in range(blocks) for b in range(group)]
    moved = lax.ppermute(quad, TOK, route)
    patch_len = image_rows * devices
    per_patch = patch_len // cache_rows
    current = jnp.where(position // per_patch == patch, moved, stale)
    got = by_head([text_query, text_key, text_value])
    got, current = lax.optimization_barrier((got, current))

    def part(first, count, source=got):
        return source[:, first : first + count].reshape(-1, HDIM)

    queries = jnp.concatenate([part(0, image_rows, got_image), part(0, text_rows)], axis=0)
    fresh_k = part(image_rows, image_rows, got_image)
    text_k = part(text_rows, text_rows)
    fresh_v = part(2 * image_rows, image_rows, got_image)
    text_v = part(2 * text_rows, text_rows)
    cache_k = part(0, cache_rows, got_cache)
    cache_v = part(cache_rows, cache_rows, got_cache)
    begin = patch * patch_len
    cache_k = lax.dynamic_update_slice_in_dim(cache_k, fresh_k, begin, 0)
    cache_v = lax.dynamic_update_slice_in_dim(cache_v, fresh_v, begin, 0)
    keys = jnp.concatenate([cache_k, text_k], axis=0)
    values = jnp.concatenate([cache_v, text_v], axis=0)
    text_count = text_length[0]
    valid = jnp.concatenate(
        [
            jnp.ones((cache_k.shape[0],), bool),
            jnp.arange(text_k.shape[0], dtype=jnp.int32) < text_count,
        ]
    )
    head_out = attend(queries, keys, values, valid)
    image_heads = broadcast_rows(head_out[:patch_len], devices).reshape(devices, patch_len, HDIM)
    text_heads = lax.all_gather(head_out[patch_len:], TOK, axis=0, tiled=False)
    def from_heads(blocks, weight):
        return jnp.einsum(
            "hrd,hdc->rc",
            blocks[:heads],
            weight.reshape(heads, HDIM, -1),
            preferred_element_type=jnp.float32,
        ).astype(jnp.bfloat16)

    image_back = cols_to_rows(
        from_heads(image_heads, image_from_heads[0]).reshape(devices, image_rows, -1)
    )
    text_back = cols_to_rows(
        from_heads(text_heads, text_from_heads[0]).reshape(devices, text_rows, -1)
    )
    image_mid = image_x + modul[2] * image_back.astype(jnp.float32)
    text_out = (text_x + text_mod[2] * text_back.astype(jnp.float32)).astype(jnp.bfloat16)
    mlp_normed = modulate(image_mid, modul[3], modul[4]).astype(jnp.bfloat16)
    up_weight = image_up[0]
    down_weight = image_down[0]
    hidden = jax.nn.gelu(
        jnp.dot(
            broadcast_rows(mlp_normed, devices),
            up_weight,
            preferred_element_type=jnp.float32,
        ),
        approximate=True,
    ).astype(jnp.bfloat16)
    partial = jnp.dot(hidden, down_weight, preferred_element_type=jnp.float32)
    partial, text_back = lax.optimization_barrier((partial, text_back))
    reduced = jnp.sum(
        lax.all_to_all(
            partial.astype(jnp.bfloat16).reshape(devices, image_rows, width),
            TOK,
            split_axis=0,
            concat_axis=0,
            tiled=True,
        ).astype(jnp.float32),
        axis=0,
    )
    image_out = (image_mid + modul[5] * reduced).astype(jnp.bfloat16)
    text_next = from_behind(text_out, "section", 1)
    image_next = from_behind(image_out, "section", 1)
    final_source = jnp.where(section == last_section, image_out, image_next)
    patch_last = entry_order[0, last_section]
    step_last = lax.dynamic_index_in_dim(step_index[0], patch_last, 0, False)
    final_mod = (
        lax.dynamic_index_in_dim(final_modulation, step_last, 0, False)
        .astype(jnp.float32)
        .reshape(2, width)
    )
    normed = modulate(final_source.astype(jnp.float32), final_mod[0], final_mod[1]).astype(
        jnp.bfloat16
    )
    velocity = jnp.dot(normed, final_weight, preferred_element_type=jnp.float32)
    latents_next = latents[0] + -1.0 / TSTEPS * velocity
    return (image_next[None, None], text_next[None, None], current[None, None], latents_next[None])


def solution(mesh):
    shape = mesh.devices.shape
    split = jax.sharding.Mesh(
        mesh.devices.reshape(shape[:2] + (shape[2] // QUAD, QUAD)),
        ("section", "grp", "ta", "tb"),
    )
    placed = (
        P("section", "grp", TOK, None),
        P("section", "grp", TOK, None),
        P("grp"),
        P("grp", None),
        P("grp", None),
        P("section", None, None),
        P("section", None, None),
        P("section", None, TOK),
        P("section", None, TOK),
        P("section", None, None),
        P("section", None, TOK),
        P("section", None, TOK),
        P("section", None, TOK),
        P("section", TOK, None),
        P("section", "grp", TOK, None),
        P(),
        P(None, "section"),
        P("grp", TOK, "section"),
    )
    return jax.shard_map(
        shards,
        mesh=split,
        in_specs=placed,
        out_specs=(
            P("section", "grp", TOK, None),
            P("section", "grp", TOK, None),
            P("section", "grp", TOK, None),
            P("grp", TOK, "section"),
        ),
        check_vma=False,
    )
```
